128 devices in a mesh: gx: 8 (over x, z_hi), gy: 16 (over y, z_lo, core).
Axes of the slice: x: 4, y: 4, z: 4 (z_hi: 2, z_lo: 2; z = z_hi * 2 + z_lo), core: 2. Of those that a mesh axis runs over, the one named last changes fastest.
Arguments:
- right_side: float32 [16, 1024, 1024], P(None, 'gy', 'gx'), may hold values from -8 to 8
- conduct: float32 [16, 1024, 1024], P(None, 'gy', 'gx'), may hold values from 0.3 to 3
- excavated: int32 [16, 1024, 1024], P(None, 'gy', 'gx'), may hold values 0 or 1
- vectors_x: float32 [1024, 1024], replicated, may hold values from -0.1875 to 0.1875
- mass_x: float32 [1024], P('gy'), may hold values from 0.5 to 2
- values_x: float32 [1024], replicated, may hold values from 0.05 to 5
- vectors_y: float32 [1024, 1024], replicated, may hold values from -0.1875 to 0.1875
- mass_y: float32 [1024], P('gx'), may hold values from 0.5 to 2
- values_y: float32 [1024], replicated, may hold values from 0.05 to 5
- vertical_diag: float32 [16], replicated, may hold values from 3.2 to 4.5
- vertical_coupling: float32 [15], replicated, may hold values from 0.5 to 1.5
Outputs:
- adjoint: float32 [16, 1024, 1024], P(None, 'gy', 'gx')
- residual: float32 [16, 1024, 1024], P(None, 'gy', 'gx')
The draws below stay inside these ranges and needn't reach their ends.
All inputs are finite; a program needn't handle non-finite values. No bound on the sum of `excavated` on one device may be relied on, other than what follows from the above.
Results may differ from the reference program's by a relative error of at most 0.0001.
Values sent between devices are 32-bit elements; how exact they have to be, the bound alone decides.
No kernel may reach another device: no remote copies, remote signals or barrier semaphores. Data moves between devices by JAX's collectives and lax.ppermute only.
A program may use at most 64 MiB of HBM per device.

```python
import math
import jax
import jax.numpy as jnp
from jax import lax

NX = 1024
NY = 1024
NZ = 16
ITERS = 2


def place_ends(drawn, stream_key, least, top_value):
    shape = drawn.shape
    spot = [jax.random.randint(jax.random.fold_in(stream_key, axis), (), 0, shape[axis]) for axis in range(len(shape))]
    drawn = drawn.at[tuple(spot)].set(least)
    longest = shape.index(max(shape))
    spot[longest] = (spot[longest] + 1) % shape[longest]
    return drawn.at[tuple(spot)].set(top_value)


def steps_of(stream_key, shape, cuts, least, high):
    factor_of = 1.0
    for dim, shards_of in cuts:
        steps = jax.random.uniform(jax.random.fold_in(jax.random.fold_in(stream_key, 6), dim), (shards_of,), jnp.float32, least / len(cuts), high / len(cuts))
        factor_of = factor_of * jnp.repeat(jnp.exp(steps), shape[dim] // shards_of).reshape((-1,) + (1,) * (len(shape) - 1 - dim))
    return factor_of


def centred(key, shape, deviation, most, cuts=(), kind=jnp.bfloat16):
    values = deviation * jax.random.normal(key, shape, jnp.float32)
    if cuts:
        values = values * steps_of(key, shape, cuts, -0.22, 0.18)
    return jnp.clip(values, -most, most).astype(kind)


def setup_inputs(seed: int = 0) -> dict:
    streams_of = jax.random.split(jax.random.key(seed), 12)
    return {
        "right_side": centred(streams_of[0], (NZ, NX, NY), 1.0, 8.0, ((1, 16), (2, 8)), jnp.float32),
        "conduct": jnp.clip(jnp.exp(math.log(3.0) - 2.3025851 * jax.random.uniform(streams_of[1], (NZ, NX, NY), jnp.float32) ** steps_of(streams_of[1], (NZ, NX, NY), ((1, 16), (2, 8)), -0.2, 0.2)), 0.3, 3.0),
        "excavated": place_ends((jax.random.randint(streams_of[2], (NZ, NX, NY), 0, 2) < 1).astype(jnp.int32), jax.random.fold_in(streams_of[2], 1), 0, 1),
        "vectors_x": centred(streams_of[3], (NX, NX), NX ** -0.5, 0.1875, (), jnp.float32),
        "mass_x": jnp.clip(jnp.exp(math.log(2.0) - 1.3862944 * jax.random.uniform(streams_of[4], (NX,), jnp.float32) ** steps_of(streams_of[4], (NX,), ((0, 16),), -0.2, 0.2)), 0.5, 2.0),
        "values_x": jnp.clip(jnp.exp(jax.random.uniform(streams_of[5], (NX,), jnp.float32, math.log(0.05), math.log(5.0))), 0.05, 5.0),
        "vectors_y": centred(streams_of[6], (NY, NY), NY ** -0.5, 0.1875, (), jnp.float32),
        "mass_y": jnp.clip(jnp.exp(math.log(2.0) - 1.3862944 * jax.random.uniform(streams_of[7], (NY,), jnp.float32) ** steps_of(streams_of[7], (NY,), ((0, 8),), -0.2, 0.2)), 0.5, 2.0),
        "values_y": jnp.clip(jnp.exp(jax.random.uniform(streams_of[8], (NY,), jnp.float32, math.log(0.05), math.log(5.0))), 0.05, 5.0),
        "vertical_diag": jnp.clip(jax.random.uniform(streams_of[9], (NZ,), jnp.float32, 3.2, 4.5), 3.2, 4.5),
        "vertical_coupling": jnp.clip(jax.random.uniform(streams_of[10], (NZ - 1,), jnp.float32, 0.5, 1.5), 0.5, 1.5),
    }


storage_term = 0.2


def harmonic(first, second):
    return 2.0 * first * second / (first + second)


def neighbours(padded):
    return [padded[2:, 1:-1, 1:-1], padded[:-2, 1:-1, 1:-1],
            padded[1:-1, 2:, 1:-1], padded[1:-1, :-2, 1:-1],
            padded[1:-1, 1:-1, 2:], padded[1:-1, 1:-1, :-2]]


def faces_from(padded):
    center = padded[1:-1, 1:-1, 1:-1]
    return [harmonic(center, other) for other in neighbours(padded)]


def stencil(padded, faces):
    center = padded[1:-1, 1:-1, 1:-1]
    result = storage_term * center
    for face, other in zip(faces, neighbours(padded)):
        result = result + face * (center - other)
    return result


def vertical_solve(rhs, diagonal, coupling, shifts):
    count = rhs.shape[0]
    ratios = []
    partial_value = []
    denom = diagonal[0] + shifts
    ratios.append(-coupling[0] / denom)
    partial_value.append(rhs[0] / denom)
    for position in range(1, count):
        denom = diagonal[position] + shifts + coupling[position - 1] * ratios[-1]
        if position < count - 1:
            ratios.append(-coupling[position] / denom)
        partial_value.append((rhs[position] + coupling[position - 1] * partial_value[-1]) / denom)
    solved = [partial_value[count - 1]]
    for position in range(count - 2, -1, -1):
        solved.append(partial_value[position] - ratios[position] * solved[-1])
    return jnp.stack(solved[::-1], axis=0)


def precondition(values, vectors_x, mass_x, values_x, vectors_y, mass_y, values_y, vertical_diag, vertical_coupling):
    highest = lax.Precision.HIGHEST
    scaled = values * mass_x[None, :, None] * mass_y[None, None, :]
    modes = jnp.einsum('zxy,xi->ziy', scaled, vectors_x, precision=highest)
    modes = jnp.einsum('ziy,yj->zij', modes, vectors_y, precision=highest)
    shifts = values_x[:, None] + values_y[None, :]
    solved = vertical_solve(modes, vertical_diag, vertical_coupling, shifts)
    solved = jnp.einsum('zij,yj->ziy', solved, vectors_y, precision=highest)
    return jnp.einsum('ziy,xi->zxy', solved, vectors_x, precision=highest)


def reference(right_side, conduct, excavated, vectors_x, mass_x, values_x, vectors_y, mass_y, values_y, vertical_diag, vertical_coupling):
    active = excavated.astype(jnp.float32)
    faces = faces_from(jnp.pad(conduct, 1))
    adjoint = jnp.zeros_like(right_side)
    residual = right_side
    for iteration in range(ITERS):
        update = precondition(residual, vectors_x, mass_x, values_x, vectors_y, mass_y, values_y, vertical_diag, vertical_coupling)
        adjoint = adjoint + update
        masked = active * update
        image = stencil(jnp.pad(masked, 1), faces) + (1.0 - active) * update
        residual = residual - image
    return adjoint, residual
```

```python
import jax
import jax.numpy as jnp
from jax import lax
from jax.experimental import pallas as pl
from jax.experimental.pallas import tpu as pltpu
from jax.sharding import PartitionSpec as P

ITERS = 2


storage_term = 0.2


def padded_2(block, sides, width):
    for axis, dim in sides:
        count = lax.axis_size(axis)
        forward = [(i, i + 1) for i in range(count - 1)]
        backward = [(target, source) for source, target in forward]
        low = lax.ppermute(
            lax.slice_in_dim(block, block.shape[dim] - width, None, axis=dim), axis, forward
        )
        high = lax.ppermute(lax.slice_in_dim(block, 0, width, axis=dim), axis, backward)
        block = jnp.concatenate([low, block, high], axis=dim)
    return block


def harmonic(first, second):
    return 2.0 * first * second / (first + second)


def neighbours(padded):
    return [
        padded[2:, 1:-1, 1:-1],
        padded[:-2, 1:-1, 1:-1],
        padded[1:-1, 2:, 1:-1],
        padded[1:-1, :-2, 1:-1],
        padded[1:-1, 1:-1, 2:],
        padded[1:-1, 1:-1, :-2],
    ]


def faces_from(padded):
    center = padded[1:-1, 1:-1, 1:-1]
    return [harmonic(center, other) for other in neighbours(padded)]


def stencil(padded, faces):
    center = padded[1:-1, 1:-1, 1:-1]
    result = storage_term * center
    for face, other in zip(faces, neighbours(padded)):
        result = result + face * (center - other)
    return result


def pad_vertical(values):
    return jnp.pad(values, ((1, 1), (0, 0), (0, 0)))


def solve_kernel(diag_ref, coup_ref, shifts_ref, rhs_ref, out_ref, ratio_ref):
    count = rhs_ref.shape[0]
    shifts = shifts_ref[...]
    denom = diag_ref[0] + shifts
    ratio = -coup_ref[0] / denom
    ratio_ref[0] = ratio
    part = rhs_ref[0] / denom
    out_ref[0] = part
    for position in range(1, count):
        denom = diag_ref[position] + shifts + coup_ref[position - 1] * ratio
        if position < count - 1:
            ratio = -coup_ref[position] / denom
            ratio_ref[position] = ratio
        part = (rhs_ref[position] + coup_ref[position - 1] * part) / denom
        out_ref[position] = part
    solved = part
    for position in range(count - 2, -1, -1):
        solved = out_ref[position] - ratio_ref[position] * solved
        out_ref[position] = solved


def vertical_solve(rhs, diagonal, coupling, shifts):
    smem = pl.BlockSpec(memory_space=pltpu.SMEM)
    vmem = pl.BlockSpec(memory_space=pltpu.VMEM)
    return pl.pallas_call(
        solve_kernel,
        out_shape=jax.ShapeDtypeStruct(rhs.shape, rhs.dtype),
        in_specs=[smem, smem, vmem, vmem],
        out_specs=vmem,
        scratch_shapes=[pltpu.VMEM(rhs.shape, rhs.dtype)],
    )(diagonal, coupling, shifts, rhs)


def shards(
    right_side,
    conduct,
    excavated,
    vectors_x,
    mass_x,
    values_x,
    vectors_y,
    mass_y,
    values_y,
    vertical_diag,
    vertical_coupling,
):
    highest = lax.Precision.HIGHEST
    active = excavated.astype(jnp.float32)
    rim_conduct = padded_2(conduct, (("gy", 1), ("gx", 2)), 1)
    faces = faces_from(pad_vertical(rim_conduct))
    local_modes = right_side.shape[1] // lax.axis_size("gx")
    mode_start = (lax.axis_index("gx") * lax.axis_size("gy") + lax.axis_index("gy")) * local_modes
    local_values = lax.dynamic_slice_in_dim(values_x, mode_start, local_modes, 0)
    shifts = local_values[:, None] + values_y[None, :]
    adjoint = jnp.zeros_like(right_side)
    residual = right_side
    for iteration in range(ITERS):
        scaled = residual * mass_x[None, :, None] * mass_y[None, None, :]
        modes = jnp.einsum(
            "zxy,xi->ziy",
            lax.all_to_all(scaled, "gy", split_axis=0, concat_axis=1, tiled=True),
            vectors_x,
            precision=highest,
        )
        modes = lax.all_to_all(modes, "gx", split_axis=1, concat_axis=2, tiled=True)
        modes = jnp.einsum("zxy,yj->zxj", modes, vectors_y, precision=highest)
        modes = lax.all_to_all(modes, "gy", split_axis=1, concat_axis=0, tiled=True)
        solved = vertical_solve(modes, vertical_diag, vertical_coupling, shifts)
        solved = lax.all_to_all(solved, "gy", split_axis=0, concat_axis=1, tiled=True)
        solved = jnp.einsum("zxj,yj->zxy", solved, vectors_y, precision=highest)
        solved = lax.all_to_all(solved, "gx", split_axis=2, concat_axis=1, tiled=True)
        solved = jnp.einsum("ziy,xi->zxy", solved, vectors_x, precision=highest)
        update = lax.all_to_all(solved, "gy", split_axis=1, concat_axis=0, tiled=True)
        adjoint = adjoint + update
        masked = active * update
        rim_masked = padded_2(masked, (("gy", 1), ("gx", 2)), 1)
        image = stencil(pad_vertical(rim_masked), faces) + (1.0 - active) * update
        residual = residual - image
    return (adjoint, residual)


def solution(mesh):
    in_specs = (
        P(None, "gy", "gx"),
        P(None, "gy", "gx"),
        P(None, "gy", "gx"),
        P(),
        P("gy"),
        P(),
        P(),
        P("gx"),
        P(),
        P(),
        P(),
    )
    out_specs = (P(None, "gy", "gx"), P(None, "gy", "gx"))
    return jax.shard_map(shards, mesh=mesh, in_specs=in_specs, out_specs=out_specs, check_vma=False)
```

```python
import jax
import jax.numpy as jnp
from jax import lax
from jax.experimental import pallas as pl
from jax.experimental.pallas import tpu as pltpu
from jax.sharding import PartitionSpec as P

ITERS = 2


storage_term = 0.2


def padded_2(block, sides, width):
    for axis, dim in sides:
        count = lax.axis_size(axis)
        forward = [(i, i + 1) for i in range(count - 1)]
        backward = [(target, source) for source, target in forward]
        low = lax.ppermute(
            lax.slice_in_dim(block, block.shape[dim] - width, None, axis=dim), axis, forward
        )
        high = lax.ppermute(lax.slice_in_dim(block, 0, width, axis=dim), axis, backward)
        block = jnp.concatenate([low, block, high], axis=dim)
    return block


def harmonic(first, second):
    return 2.0 * first * second / (first + second)


def neighbours(padded):
    return [
        padded[2:, 1:-1, 1:-1],
        padded[:-2, 1:-1, 1:-1],
        padded[1:-1, 2:, 1:-1],
        padded[1:-1, :-2, 1:-1],
        padded[1:-1, 1:-1, 2:],
        padded[1:-1, 1:-1, :-2],
    ]


def faces_from(padded):
    center = padded[1:-1, 1:-1, 1:-1]
    return [harmonic(center, other) for other in neighbours(padded)]


def stencil(padded, faces):
    center = padded[1:-1, 1:-1, 1:-1]
    result = storage_term * center
    for face, other in zip(faces, neighbours(padded)):
        result = result + face * (center - other)
    return result


def pad_vertical(values):
    return jnp.pad(values, ((1, 1), (0, 0), (0, 0)))


def solve_kernel(diag_ref, coup_ref, shifts_ref, rhs_ref, out_ref, ratio_ref):
    count = rhs_ref.shape[0]
    shifts = shifts_ref[...]
    denom = diag_ref[0] + shifts
    ratio = -coup_ref[0] / denom
    ratio_ref[0] = ratio
    part = rhs_ref[0] / denom
    out_ref[0] = part
    for position in range(1, count):
        denom = diag_ref[position] + shifts + coup_ref[position - 1] * ratio
        if position < count - 1:
            ratio = -coup_ref[position] / denom
            ratio_ref[position] = ratio
        part = (rhs_ref[position] + coup_ref[position - 1] * part) / denom
        out_ref[position] = part
    solved = part
    for position in range(count - 2, -1, -1):
        solved = out_ref[position] - ratio_ref[position] * solved
        out_ref[position] = solved


def vertical_solve(rhs, diagonal, coupling, shifts):
    smem = pl.BlockSpec(memory_space=pltpu.SMEM)
    vmem = pl.BlockSpec(memory_space=pltpu.VMEM)
    return pl.pallas_call(
        solve_kernel,
        out_shape=jax.ShapeDtypeStruct(rhs.shape, rhs.dtype),
        in_specs=[smem, smem, vmem, vmem],
        out_specs=vmem,
        scratch_shapes=[pltpu.VMEM(rhs.shape, rhs.dtype)],
    )(diagonal, coupling, shifts, rhs)


def shards(
    right_side,
    conduct,
    excavated,
    vectors_x,
    mass_x,
    values_x,
    vectors_y,
    mass_y,
    values_y,
    vertical_diag,
    vertical_coupling,
):
    highest = lax.Precision.HIGHEST
    active = excavated.astype(jnp.float32)
    rim_conduct = padded_2(conduct, (("gy", 1), ("gx", 2)), 1)
    faces = faces_from(pad_vertical(rim_conduct))
    local_modes = vectors_x.shape[1] // (lax.axis_size("gx") * lax.axis_size("gy"))
    mode_start = (lax.axis_index("gx") * lax.axis_size("gy") + lax.axis_index("gy")) * local_modes
    local_values = lax.dynamic_slice_in_dim(values_x, mode_start, local_modes, 0)
    shifts = local_values[:, None] + values_y[None, :]
    adjoint = jnp.zeros_like(right_side)
    residual = right_side
    everyone = ("gx", "gy")
    blocks_y = lax.axis_size("gx")
    for iteration in range(ITERS):
        scaled = residual * mass_x[None, :, None] * mass_y[None, None, :]
        modes = jnp.einsum(
            "zxy,xi->ziy",
            lax.all_to_all(scaled, "gy", split_axis=0, concat_axis=1, tiled=True),
            vectors_x,
            precision=highest,
        )
        chunks = modes.reshape(-1, local_modes, modes.shape[2])
        chunks = lax.all_to_all(chunks, everyone, split_axis=0, concat_axis=0, tiled=True)
        chunks = chunks.reshape(blocks_y, -1, local_modes, chunks.shape[2])
        modes = jnp.einsum(
            "azil,alj->zij",
            chunks,
            vectors_y.reshape(blocks_y, -1, vectors_y.shape[1]),
            precision=highest,
        )
        solved = vertical_solve(modes, vertical_diag, vertical_coupling, shifts)
        chunks = jnp.einsum(
            "zij,alj->azil",
            solved,
            vectors_y.reshape(blocks_y, -1, vectors_y.shape[1]),
            precision=highest,
        )
        chunks = chunks.reshape(-1, local_modes, chunks.shape[3])
        chunks = lax.all_to_all(chunks, everyone, split_axis=0, concat_axis=0, tiled=True)
        solved = chunks.reshape(1, -1, chunks.shape[2])
        solved = jnp.einsum("ziy,xi->zxy", solved, vectors_x, precision=highest)
        update = lax.all_to_all(solved, "gy", split_axis=1, concat_axis=0, tiled=True)
        adjoint = adjoint + update
        masked = active * update
        rim_masked = padded_2(masked, (("gy", 1), ("gx", 2)), 1)
        image = stencil(pad_vertical(rim_masked), faces) + (1.0 - active) * update
        residual = residual - image
    return (adjoint, residual)


def solution(mesh):
    in_specs = (
        P(None, "gy", "gx"),
        P(None, "gy", "gx"),
        P(None, "gy", "gx"),
        P(),
        P("gy"),
        P(),
        P(),
        P("gx"),
        P(),
        P(),
        P(),
    )
    out_specs = (P(None, "gy", "gx"), P(None, "gy", "gx"))
    return jax.shard_map(shards, mesh=mesh, in_specs=in_specs, out_specs=out_specs, check_vma=False)
```

```python
import jax
import jax.numpy as jnp
from jax import lax
from jax.experimental import pallas as pl
from jax.experimental.pallas import tpu as pltpu
from jax.sharding import PartitionSpec as P

ITERS = 2


storage_term = 0.2


def edges(block):
    strips = []
    for axis, dim in (("gy", 1), ("gx", 2)):
        count = lax.axis_size(axis)
        forward = [(i, i + 1) for i in range(count - 1)]
        backward = [(target, source) for source, target in forward]
        last = lax.index_in_dim(block, block.shape[dim] - 1, axis=dim, keepdims=False)
        first = lax.index_in_dim(block, 0, axis=dim, keepdims=False)
        strips.append((lax.ppermute(last, axis, forward), lax.ppermute(first, axis, backward)))
    return strips


def harmonic(first, second):
    return 2.0 * first * second / (first + second)


def neighbours(center, strips):
    (x_low, x_high), (y_low, y_high) = strips
    zeros = jnp.zeros_like(center[:1])
    return [
        jnp.concatenate([center[1:], zeros], axis=0),
        jnp.concatenate([zeros, center[:-1]], axis=0),
        jnp.concatenate([center[:, 1:], x_high[:, None, :]], axis=1),
        jnp.concatenate([x_low[:, None, :], center[:, :-1]], axis=1),
        jnp.concatenate([center[:, :, 1:], y_high[:, :, None]], axis=2),
        jnp.concatenate([y_low[:, :, None], center[:, :, :-1]], axis=2),
    ]


def faces_from(center):
    return [harmonic(center, other) for other in neighbours(center, edges(center))]


def stencil(center, faces):
    result = storage_term * center
    for face, other in zip(faces, neighbours(center, edges(center))):
        result = result + face * (center - other)
    return result


def solve_kernel(diag_ref, coup_ref, shifts_ref, rhs_ref, out_ref, ratio_ref):
    count = rhs_ref.shape[0]
    shifts = shifts_ref[...]
    denom = diag_ref[0] + shifts
    ratio = -coup_ref[0] / denom
    ratio_ref[0] = ratio
    part = rhs_ref[0] / denom
    out_ref[0] = part
    for position in range(1, count):
        denom = diag_ref[position] + shifts + coup_ref[position - 1] * ratio
        if position < count - 1:
            ratio = -coup_ref[position] / denom
            ratio_ref[position] = ratio
        part = (rhs_ref[position] + coup_ref[position - 1] * part) / denom
        out_ref[position] = part
    solved = part
    for position in range(count - 2, -1, -1):
        solved = out_ref[position] - ratio_ref[position] * solved
        out_ref[position] = solved


def vertical_solve(rhs, diagonal, coupling, shifts):
    smem = pl.BlockSpec(memory_space=pltpu.SMEM)
    vmem = pl.BlockSpec(memory_space=pltpu.VMEM)
    return pl.pallas_call(
        solve_kernel,
        out_shape=jax.ShapeDtypeStruct(rhs.shape, rhs.dtype),
        in_specs=[smem, smem, vmem, vmem],
        out_specs=vmem,
        scratch_shapes=[pltpu.VMEM(rhs.shape, rhs.dtype)],
    )(diagonal, coupling, shifts, rhs)


def shards(
    right_side,
    conduct,
    excavated,
    vectors_x,
    mass_x,
    values_x,
    vectors_y,
    mass_y,
    values_y,
    vertical_diag,
    vertical_coupling,
):
    highest = lax.Precision.HIGHEST
    active = excavated.astype(jnp.float32)
    faces = faces_from(conduct)
    local_modes = vectors_x.shape[1] // (lax.axis_size("gx") * lax.axis_size("gy"))
    mode_start = (lax.axis_index("gx") * lax.axis_size("gy") + lax.axis_index("gy")) * local_modes
    local_values = lax.dynamic_slice_in_dim(values_x, mode_start, local_modes, 0)
    shifts = local_values[:, None] + values_y[None, :]
    adjoint = jnp.zeros_like(right_side)
    residual = right_side
    everyone = ("gx", "gy")
    blocks_y = lax.axis_size("gx")
    for iteration in range(ITERS):
        scaled = residual * mass_x[None, :, None] * mass_y[None, None, :]
        modes = jnp.einsum(
            "zxy,xi->ziy",
            lax.all_to_all(scaled, "gy", split_axis=0, concat_axis=1, tiled=True),
            vectors_x,
            precision=highest,
        )
        chunks = modes.reshape(-1, local_modes, modes.shape[2])
        chunks = lax.all_to_all(chunks, everyone, split_axis=0, concat_axis=0, tiled=True)
        chunks = chunks.reshape(blocks_y, -1, local_modes, chunks.shape[2])
        modes = jnp.einsum(
            "azil,alj->zij",
            chunks,
            vectors_y.reshape(blocks_y, -1, vectors_y.shape[1]),
            precision=highest,
        )
        solved = vertical_solve(modes, vertical_diag, vertical_coupling, shifts)
        chunks = jnp.einsum(
            "zij,alj->azil",
            solved,
            vectors_y.reshape(blocks_y, -1, vectors_y.shape[1]),
            precision=highest,
        )
        chunks = chunks.reshape(-1, local_modes, chunks.shape[3])
        chunks = lax.all_to_all(chunks, everyone, split_axis=0, concat_axis=0, tiled=True)
        solved = chunks.reshape(1, -1, chunks.shape[2])
        solved = jnp.einsum("ziy,xi->zxy", solved, vectors_x, precision=highest)
        update = lax.all_to_all(solved, "gy", split_axis=1, concat_axis=0, tiled=True)
        adjoint = adjoint + update
        masked = active * update
        image = stencil(masked, faces) + (1.0 - active) * update
        residual = residual - image
    return (adjoint, residual)


def solution(mesh):
    in_specs = (
        P(None, "gy", "gx"),
        P(None, "gy", "gx"),
        P(None, "gy", "gx"),
        P(),
        P("gy"),
        P(),
        P(),
        P("gx"),
        P(),
        P(),
        P(),
    )
    out_specs = (P(None, "gy", "gx"), P(None, "gy", "gx"))
    return jax.shard_map(shards, mesh=mesh, in_specs=in_specs, out_specs=out_specs, check_vma=False)
```

```python
import jax
import jax.numpy as jnp
from jax import lax
from jax.experimental import pallas as pl
from jax.experimental.pallas import tpu as pltpu
from jax.sharding import PartitionSpec as P

ITERS = 2


storage_term = 0.2


def edges(block):
    strips = []
    for axis, dim in (("gy", 1), ("gx", 2)):
        count = lax.axis_size(axis)
        forward = [(i, i + 1) for i in range(count - 1)]
        backward = [(target, source) for source, target in forward]
        last = lax.index_in_dim(block, block.shape[dim] - 1, axis=dim, keepdims=False)
        first = lax.index_in_dim(block, 0, axis=dim, keepdims=False)
        strips.append((lax.ppermute(last, axis, forward), lax.ppermute(first, axis, backward)))
    return strips


def harmonic(first, second):
    return 2.0 * first * second / (first + second)


def neighbours(center, strips):
    (x_low, x_high), (y_low, y_high) = strips
    zeros = jnp.zeros_like(center[:1])
    return [
        jnp.concatenate([center[1:], zeros], axis=0),
        jnp.concatenate([zeros, center[:-1]], axis=0),
        jnp.concatenate([center[:, 1:], x_high[:, None, :]], axis=1),
        jnp.concatenate([x_low[:, None, :], center[:, :-1]], axis=1),
        jnp.concatenate([center[:, :, 1:], y_high[:, :, None]], axis=2),
        jnp.concatenate([y_low[:, :, None], center[:, :, :-1]], axis=2),
    ]


def faces_from(center):
    return [harmonic(center, other) for other in neighbours(center, edges(center))]


def stencil(center, faces):
    result = storage_term * center
    for face, other in zip(faces, neighbours(center, edges(center))):
        result = result + face * (center - other)
    return result


def solve_kernel(diag_ref, coup_ref, shifts_ref, rhs_ref, out_ref, ratio_ref):
    count = rhs_ref.shape[0]
    shifts = shifts_ref[...]
    denom = diag_ref[0] + shifts
    ratio = -coup_ref[0] / denom
    ratio_ref[0] = ratio
    part = rhs_ref[0] / denom
    out_ref[0] = part
    for position in range(1, count):
        denom = diag_ref[position] + shifts + coup_ref[position - 1] * ratio
        if position < count - 1:
            ratio = -coup_ref[position] / denom
            ratio_ref[position] = ratio
        part = (rhs_ref[position] + coup_ref[position - 1] * part) / denom
        out_ref[position] = part
    solved = part
    for position in range(count - 2, -1, -1):
        solved = out_ref[position] - ratio_ref[position] * solved
        out_ref[position] = solved


def vertical_solve(rhs, diagonal, coupling, shifts):
    smem = pl.BlockSpec(memory_space=pltpu.SMEM)
    vmem = pl.BlockSpec(memory_space=pltpu.VMEM)
    return pl.pallas_call(
        solve_kernel,
        out_shape=jax.ShapeDtypeStruct(rhs.shape, rhs.dtype),
        in_specs=[smem, smem, vmem, vmem],
        out_specs=vmem,
        scratch_shapes=[pltpu.VMEM(rhs.shape, rhs.dtype)],
    )(diagonal, coupling, shifts, rhs)


def shards(
    right_side,
    conduct,
    excavated,
    vectors_x,
    mass_x,
    values_x,
    vectors_y,
    mass_y,
    values_y,
    vertical_diag,
    vertical_coupling,
):
    highest = lax.Precision.HIGHEST
    active = excavated.astype(jnp.float32)
    faces = faces_from(conduct)
    local_modes = vectors_x.shape[1] // (lax.axis_size("gx") * lax.axis_size("gy"))
    mode_start = (lax.axis_index("gx") * lax.axis_size("gy") + lax.axis_index("gy")) * local_modes
    local_values = lax.dynamic_slice_in_dim(values_x, mode_start, local_modes, 0)
    shifts = local_values[:, None] + values_y[None, :]
    adjoint = jnp.zeros_like(right_side)
    residual = right_side
    everyone = ("gx", "gy")
    blocks_y = lax.axis_size("gx")
    halves = 2
    half_modes = local_modes // halves
    basis_y = vectors_y.reshape(blocks_y, -1, vectors_y.shape[1])
    basis_x = vectors_x.reshape(vectors_x.shape[0], -1, local_modes)
    for iteration in range(ITERS):
        scaled = residual * mass_x[None, :, None] * mass_y[None, None, :]
        width = scaled.shape[2] // halves
        modes = []
        for half in range(halves):
            part = lax.slice_in_dim(scaled, half * width, (half + 1) * width, axis=2)
            part = lax.all_to_all(part, "gy", split_axis=0, concat_axis=1, tiled=True)
            modes.append(jnp.einsum("zxy,xi->ziy", part, vectors_x, precision=highest))
        modes = jnp.concatenate(modes, axis=2)
        modes = modes.reshape(-1, local_modes, modes.shape[2])
        pieces = []
        for half in range(halves):
            lo = half * half_modes
            chunks = lax.slice_in_dim(modes, lo, lo + half_modes, axis=1)
            chunks = lax.all_to_all(chunks, everyone, split_axis=0, concat_axis=0, tiled=True)
            chunks = chunks.reshape(blocks_y, -1, half_modes, chunks.shape[2])
            spectral = jnp.einsum("azil,alj->zij", chunks, basis_y, precision=highest)
            solved = vertical_solve(
                spectral, vertical_diag, vertical_coupling, lax.slice_in_dim(shifts, lo, lo + half_modes, axis=0)
            )
            chunks = jnp.einsum("zij,alj->azil", solved, basis_y, precision=highest)
            chunks = chunks.reshape(-1, half_modes, chunks.shape[3])
            chunks = lax.all_to_all(chunks, everyone, split_axis=0, concat_axis=0, tiled=True)
            pieces.append(
                jnp.einsum(
                    "cky,xck->xy",
                    chunks,
                    lax.slice_in_dim(basis_x, lo, lo + half_modes, axis=2),
                    precision=highest,
                )
            )
        solved = (pieces[0] + pieces[1])[None]
        update = lax.all_to_all(solved, "gy", split_axis=1, concat_axis=0, tiled=True)
        adjoint = adjoint + update
        masked = active * update
        image = stencil(masked, faces) + (1.0 - active) * update
        residual = residual - image
    return (adjoint, residual)


def solution(mesh):
    in_specs = (
        P(None, "gy", "gx"),
        P(None, "gy", "gx"),
        P(None, "gy", "gx"),
        P(),
        P("gy"),
        P(),
        P(),
        P("gx"),
        P(),
        P(),
        P(),
    )
    out_specs = (P(None, "gy", "gx"), P(None, "gy", "gx"))
    return jax.shard_map(shards, mesh=mesh, in_specs=in_specs, out_specs=out_specs, check_vma=False)
```

```python
import jax
import jax.numpy as jnp
from jax import lax
from jax.experimental import pallas as pl
from jax.experimental.pallas import tpu as pltpu
from jax.sharding import PartitionSpec as P

ITERS = 2


storage_term = 0.2


def edges(block):
    strips = []
    for axis, dim in (("gy", 1), ("gx", 2)):
        count = lax.axis_size(axis)
        forward = [(i, i + 1) for i in range(count - 1)]
        backward = [(target, source) for source, target in forward]
        last = lax.index_in_dim(block, block.shape[dim] - 1, axis=dim, keepdims=False)
        first = lax.index_in_dim(block, 0, axis=dim, keepdims=False)
        strips.append((lax.ppermute(last, axis, forward), lax.ppermute(first, axis, backward)))
    return strips


def harmonic(first, second):
    return 2.0 * first * second / (first + second)


def neighbours(center, strips):
    (x_low, x_high), (y_low, y_high) = strips
    zeros = jnp.zeros_like(center[:1])
    return [
        jnp.concatenate([center[1:], zeros], axis=0),
        jnp.concatenate([zeros, center[:-1]], axis=0),
        jnp.concatenate([center[:, 1:], x_high[:, None, :]], axis=1),
        jnp.concatenate([x_low[:, None, :], center[:, :-1]], axis=1),
        jnp.concatenate([center[:, :, 1:], y_high[:, :, None]], axis=2),
        jnp.concatenate([y_low[:, :, None], center[:, :, :-1]], axis=2),
    ]


def faces_from(center):
    return [harmonic(center, other) for other in neighbours(center, edges(center))]


def stencil(center, faces):
    result = storage_term * center
    for face, other in zip(faces, neighbours(center, edges(center))):
        result = result + face * (center - other)
    return result


def solve_kernel(diag_ref, coup_ref, shifts_ref, rhs_ref, out_ref, ratio_ref):
    count = rhs_ref.shape[0]
    shifts = shifts_ref[...]
    denom = diag_ref[0] + shifts
    ratio = -coup_ref[0] / denom
    ratio_ref[0] = ratio
    part = rhs_ref[0] / denom
    out_ref[0] = part
    for position in range(1, count):
        denom = diag_ref[position] + shifts + coup_ref[position - 1] * ratio
        if position < count - 1:
            ratio = -coup_ref[position] / denom
            ratio_ref[position] = ratio
        part = (rhs_ref[position] + coup_ref[position - 1] * part) / denom
        out_ref[position] = part
    solved = part
    for position in range(count - 2, -1, -1):
        solved = out_ref[position] - ratio_ref[position] * solved
        out_ref[position] = solved


def vertical_solve(rhs, diagonal, coupling, shifts):
    smem = pl.BlockSpec(memory_space=pltpu.SMEM)
    vmem = pl.BlockSpec(memory_space=pltpu.VMEM)
    return pl.pallas_call(
        solve_kernel,
        out_shape=jax.ShapeDtypeStruct(rhs.shape, rhs.dtype),
        in_specs=[smem, smem, vmem, vmem],
        out_specs=vmem,
        scratch_shapes=[pltpu.VMEM(rhs.shape, rhs.dtype)],
    )(diagonal, coupling, shifts, rhs)


def shards(
    right_side,
    conduct,
    excavated,
    vectors_x,
    mass_x,
    values_x,
    vectors_y,
    mass_y,
    values_y,
    vertical_diag,
    vertical_coupling,
):
    precision = lax.Precision.HIGH
    active = excavated.astype(jnp.float32)
    faces = faces_from(conduct)
    local_modes = vectors_x.shape[1] // (lax.axis_size("gx") * lax.axis_size("gy"))
    mode_start = (lax.axis_index("gx") * lax.axis_size("gy") + lax.axis_index("gy")) * local_modes
    local_values = lax.dynamic_slice_in_dim(values_x, mode_start, local_modes, 0)
    shifts = local_values[:, None] + values_y[None, :]
    adjoint = jnp.zeros_like(right_side)
    residual = right_side
    everyone = ("gx", "gy")
    blocks_y = lax.axis_size("gx")
    for iteration in range(ITERS):
        scaled = residual * mass_x[None, :, None] * mass_y[None, None, :]
        modes = jnp.einsum(
            "zxy,xi->ziy",
            lax.all_to_all(scaled, "gy", split_axis=0, concat_axis=1, tiled=True),
            vectors_x,
            precision=precision,
        )
        chunks = modes.reshape(-1, local_modes, modes.shape[2])
        chunks = lax.all_to_all(chunks, everyone, split_axis=0, concat_axis=0, tiled=True)
        chunks = chunks.reshape(blocks_y, -1, local_modes, chunks.shape[2])
        modes = jnp.einsum(
            "azil,alj->zij",
            chunks,
            vectors_y.reshape(blocks_y, -1, vectors_y.shape[1]),
            precision=precision,
        )
        solved = vertical_solve(modes, vertical_diag, vertical_coupling, shifts)
        chunks = jnp.einsum(
            "zij,alj->azil",
            solved,
            vectors_y.reshape(blocks_y, -1, vectors_y.shape[1]),
            precision=precision,
        )
        chunks = chunks.reshape(-1, local_modes, chunks.shape[3])
        chunks = lax.all_to_all(chunks, everyone, split_axis=0, concat_axis=0, tiled=True)
        solved = chunks.reshape(1, -1, chunks.shape[2])
        solved = jnp.einsum("ziy,xi->zxy", solved, vectors_x, precision=precision)
        update = lax.all_to_all(solved, "gy", split_axis=1, concat_axis=0, tiled=True)
        adjoint = adjoint + update
        masked = active * update
        image = stencil(masked, faces) + (1.0 - active) * update
        residual = residual - image
    return (adjoint, residual)


def solution(mesh):
    in_specs = (
        P(None, "gy", "gx"),
        P(None, "gy", "gx"),
        P(None, "gy", "gx"),
        P(),
        P("gy"),
        P(),
        P(),
        P("gx"),
        P(),
        P(),
        P(),
    )
    out_specs = (P(None, "gy", "gx"), P(None, "gy", "gx"))
    return jax.shard_map(shards, mesh=mesh, in_specs=in_specs, out_specs=out_specs, check_vma=False)
```

```python
import jax
import jax.numpy as jnp
from jax import lax
from jax.experimental import pallas as pl
from jax.experimental.pallas import tpu as pltpu
from jax.sharding import PartitionSpec as P

ITERS = 2


storage_term = 0.2


def edges(block):
    strips = []
    for axis, dim in (("gy", 1), ("gx", 2)):
        count = lax.axis_size(axis)
        forward = [(i, i + 1) for i in range(count - 1)]
        backward = [(target, source) for source, target in forward]
        last = lax.index_in_dim(block, block.shape[dim] - 1, axis=dim, keepdims=False)
        first = lax.index_in_dim(block, 0, axis=dim, keepdims=False)
        strips.append((lax.ppermute(last, axis, forward), lax.ppermute(first, axis, backward)))
    return strips


def harmonic(first, second):
    return 2.0 * first * second / (first + second)


def neighbours(center, strips):
    (x_low, x_high), (y_low, y_high) = strips
    zeros = jnp.zeros_like(center[:1])
    return [
        jnp.concatenate([center[1:], zeros], axis=0),
        jnp.concatenate([zeros, center[:-1]], axis=0),
        jnp.concatenate([center[:, 1:], x_high[:, None, :]], axis=1),
        jnp.concatenate([x_low[:, None, :], center[:, :-1]], axis=1),
        jnp.concatenate([center[:, :, 1:], y_high[:, :, None]], axis=2),
        jnp.concatenate([y_low[:, :, None], center[:, :, :-1]], axis=2),
    ]


def faces_from(center):
    return [harmonic(center, other) for other in neighbours(center, edges(center))]


def stencil(center, faces):
    result = storage_term * center
    for face, other in zip(faces, neighbours(center, edges(center))):
        result = result + face * (center - other)
    return result


def solve_kernel(diag_ref, coup_ref, shifts_ref, rhs_ref, out_ref, ratio_ref):
    count = rhs_ref.shape[0]
    shifts = shifts_ref[...]
    denom = diag_ref[0] + shifts
    ratio = -coup_ref[0] / denom
    ratio_ref[0] = ratio
    part = rhs_ref[0] / denom
    out_ref[0] = part
    for position in range(1, count):
        denom = diag_ref[position] + shifts + coup_ref[position - 1] * ratio
        if position < count - 1:
            ratio = -coup_ref[position] / denom
            ratio_ref[position] = ratio
        part = (rhs_ref[position] + coup_ref[position - 1] * part) / denom
        out_ref[position] = part
    solved = part
    for position in range(count - 2, -1, -1):
        solved = out_ref[position] - ratio_ref[position] * solved
        out_ref[position] = solved


def vertical_solve(rhs, diagonal, coupling, shifts):
    smem = pl.BlockSpec(memory_space=pltpu.SMEM)
    vmem = pl.BlockSpec(memory_space=pltpu.VMEM)
    return pl.pallas_call(
        solve_kernel,
        out_shape=jax.ShapeDtypeStruct(rhs.shape, rhs.dtype),
        in_specs=[smem, smem, vmem, vmem],
        out_specs=vmem,
        scratch_shapes=[pltpu.VMEM(rhs.shape, rhs.dtype)],
    )(diagonal, coupling, shifts, rhs)


def split_bf16(values):
    rounded = lax.reduce_precision(values, exponent_bits=8, mantissa_bits=7)
    return rounded.astype(jnp.bfloat16), (values - rounded).astype(jnp.bfloat16)


def transform(spec, data, basis):
    high, low = split_bf16(data)
    basis_high, basis_low = basis

    def product(first, second):
        return jnp.einsum(spec, first, second, preferred_element_type=jnp.float32)

    return product(high, basis_high) + (product(low, basis_high) + product(high, basis_low))


def shards(
    right_side,
    conduct,
    excavated,
    vectors_x,
    mass_x,
    values_x,
    vectors_y,
    mass_y,
    values_y,
    vertical_diag,
    vertical_coupling,
):
    active = excavated.astype(jnp.float32)
    faces = faces_from(conduct)
    local_modes = vectors_x.shape[1] // (lax.axis_size("gx") * lax.axis_size("gy"))
    mode_start = (lax.axis_index("gx") * lax.axis_size("gy") + lax.axis_index("gy")) * local_modes
    local_values = lax.dynamic_slice_in_dim(values_x, mode_start, local_modes, 0)
    shifts = local_values[:, None] + values_y[None, :]
    adjoint = jnp.zeros_like(right_side)
    residual = right_side
    everyone = ("gx", "gy")
    blocks_y = lax.axis_size("gx")
    basis_x = split_bf16(vectors_x)
    basis_y = tuple(piece.reshape(blocks_y, -1, vectors_y.shape[1]) for piece in split_bf16(vectors_y))
    for iteration in range(ITERS):
        scaled = residual * mass_x[None, :, None] * mass_y[None, None, :]
        modes = transform(
            "zxy,xi->ziy",
            lax.all_to_all(scaled, "gy", split_axis=0, concat_axis=1, tiled=True),
            basis_x,
        )
        chunks = modes.reshape(-1, local_modes, modes.shape[2])
        chunks = lax.all_to_all(chunks, everyone, split_axis=0, concat_axis=0, tiled=True)
        chunks = chunks.reshape(blocks_y, -1, local_modes, chunks.shape[2])
        modes = transform("azil,alj->zij", chunks, basis_y)
        solved = vertical_solve(modes, vertical_diag, vertical_coupling, shifts)
        chunks = transform("zij,alj->azil", solved, basis_y)
        chunks = chunks.reshape(-1, local_modes, chunks.shape[3])
        chunks = lax.all_to_all(chunks, everyone, split_axis=0, concat_axis=0, tiled=True)
        solved = chunks.reshape(1, -1, chunks.shape[2])
        solved = transform("ziy,xi->zxy", solved, basis_x)
        update = lax.all_to_all(solved, "gy", split_axis=1, concat_axis=0, tiled=True)
        adjoint = adjoint + update
        masked = active * update
        image = stencil(masked, faces) + (1.0 - active) * update
        residual = residual - image
    return (adjoint, residual)


def solution(mesh):
    in_specs = (
        P(None, "gy", "gx"),
        P(None, "gy", "gx"),
        P(None, "gy", "gx"),
        P(),
        P("gy"),
        P(),
        P(),
        P("gx"),
        P(),
        P(),
        P(),
    )
    out_specs = (P(None, "gy", "gx"), P(None, "gy", "gx"))
    return jax.shard_map(shards, mesh=mesh, in_specs=in_specs, out_specs=out_specs, check_vma=False)
```

```python
import jax
import jax.numpy as jnp
from jax import lax
from jax.experimental import pallas as pl
from jax.experimental.pallas import tpu as pltpu
from jax.sharding import PartitionSpec as P

ITERS = 2


storage_term = 0.2


def edge_pair(block, axis, dim):
    count = lax.axis_size(axis)
    forward = [(i, i + 1) for i in range(count - 1)]
    backward = [(target, source) for source, target in forward]
    last = lax.index_in_dim(block, block.shape[dim] - 1, axis=dim, keepdims=False)
    first = lax.index_in_dim(block, 0, axis=dim, keepdims=False)
    return lax.ppermute(last, axis, forward), lax.ppermute(first, axis, backward)


def edges(block):
    return [edge_pair(block, "gy", 1), edge_pair(block, "gx", 2)]


def harmonic(first, second):
    return 2.0 * first * second / (first + second)


def neighbours(center, strips):
    (x_low, x_high), (y_low, y_high) = strips
    zeros = jnp.zeros_like(center[:1])
    return [
        jnp.concatenate([center[1:], zeros], axis=0),
        jnp.concatenate([zeros, center[:-1]], axis=0),
        jnp.concatenate([center[:, 1:], x_high[:, None, :]], axis=1),
        jnp.concatenate([x_low[:, None, :], center[:, :-1]], axis=1),
        jnp.concatenate([center[:, :, 1:], y_high[:, :, None]], axis=2),
        jnp.concatenate([y_low[:, :, None], center[:, :, :-1]], axis=2),
    ]


def faces_from(center):
    return [harmonic(center, other) for other in neighbours(center, edges(center))]


def stencil(center, faces, strips):
    result = storage_term * center
    for face, other in zip(faces, neighbours(center, strips)):
        result = result + face * (center - other)
    return result


def solve_kernel(diag_ref, coup_ref, shifts_ref, rhs_ref, out_ref, ratio_ref):
    count = rhs_ref.shape[0]
    shifts = shifts_ref[...]
    denom = diag_ref[0] + shifts
    ratio = -coup_ref[0] / denom
    ratio_ref[0] = ratio
    part = rhs_ref[0] / denom
    out_ref[0] = part
    for position in range(1, count):
        denom = diag_ref[position] + shifts + coup_ref[position - 1] * ratio
        if position < count - 1:
            ratio = -coup_ref[position] / denom
            ratio_ref[position] = ratio
        part = (rhs_ref[position] + coup_ref[position - 1] * part) / denom
        out_ref[position] = part
    solved = part
    for position in range(count - 2, -1, -1):
        solved = out_ref[position] - ratio_ref[position] * solved
        out_ref[position] = solved


def vertical_solve(rhs, diagonal, coupling, shifts):
    smem = pl.BlockSpec(memory_space=pltpu.SMEM)
    vmem = pl.BlockSpec(memory_space=pltpu.VMEM)
    return pl.pallas_call(
        solve_kernel,
        out_shape=jax.ShapeDtypeStruct(rhs.shape, rhs.dtype),
        in_specs=[smem, smem, vmem, vmem],
        out_specs=vmem,
        scratch_shapes=[pltpu.VMEM(rhs.shape, rhs.dtype)],
    )(diagonal, coupling, shifts, rhs)


def split_bf16(values):
    rounded = lax.reduce_precision(values, exponent_bits=8, mantissa_bits=7)
    return rounded.astype(jnp.bfloat16), (values - rounded).astype(jnp.bfloat16)


def transform(spec, data, basis):
    high, low = split_bf16(data)
    basis_high, basis_low = basis

    def product(first, second):
        return jnp.einsum(spec, first, second, preferred_element_type=jnp.float32)

    return product(high, basis_high) + (product(low, basis_high) + product(high, basis_low))


def shards(
    right_side,
    conduct,
    excavated,
    vectors_x,
    mass_x,
    values_x,
    vectors_y,
    mass_y,
    values_y,
    vertical_diag,
    vertical_coupling,
):
    active = excavated.astype(jnp.float32)
    faces = faces_from(conduct)
    local_modes = vectors_x.shape[1] // (lax.axis_size("gx") * lax.axis_size("gy"))
    mode_start = (lax.axis_index("gx") * lax.axis_size("gy") + lax.axis_index("gy")) * local_modes
    local_values = lax.dynamic_slice_in_dim(values_x, mode_start, local_modes, 0)
    shifts = local_values[:, None] + values_y[None, :]
    adjoint = jnp.zeros_like(right_side)
    residual = right_side
    everyone = ("gx", "gy")
    blocks_y = lax.axis_size("gx")
    basis_x = split_bf16(vectors_x)
    rows = right_side.shape[1]
    framed_basis = []
    for piece in basis_x:
        blocks = piece.reshape(-1, rows, piece.shape[1])
        zero = jnp.zeros_like(blocks[:1, :1])
        below = jnp.concatenate([zero, blocks[:-1, -1:]], axis=0)
        above = jnp.concatenate([blocks[1:, :1], zero], axis=0)
        framed_basis.append(jnp.concatenate([below, blocks, above], axis=1))
    active_x = edge_pair(active, "gy", 1)
    basis_y = tuple(piece.reshape(blocks_y, -1, vectors_y.shape[1]) for piece in split_bf16(vectors_y))
    for iteration in range(ITERS):
        scaled = residual * mass_x[None, :, None] * mass_y[None, None, :]
        modes = transform(
            "zxy,xi->ziy",
            lax.all_to_all(scaled, "gy", split_axis=0, concat_axis=1, tiled=True),
            basis_x,
        )
        chunks = modes.reshape(-1, local_modes, modes.shape[2])
        chunks = lax.all_to_all(chunks, everyone, split_axis=0, concat_axis=0, tiled=True)
        chunks = chunks.reshape(blocks_y, -1, local_modes, chunks.shape[2])
        modes = transform("azil,alj->zij", chunks, basis_y)
        solved = vertical_solve(modes, vertical_diag, vertical_coupling, shifts)
        chunks = transform("zij,alj->azil", solved, basis_y)
        chunks = chunks.reshape(-1, local_modes, chunks.shape[3])
        chunks = lax.all_to_all(chunks, everyone, split_axis=0, concat_axis=0, tiled=True)
        solved = chunks.reshape(-1, chunks.shape[2])
        framed = transform("iy,bri->bry", solved, framed_basis)
        framed = lax.all_to_all(framed, "gy", split_axis=0, concat_axis=0, tiled=True)
        update = framed[:, 1:-1]
        adjoint = adjoint + update
        masked = active * update
        x_strips = (active_x[0] * framed[:, 0], active_x[1] * framed[:, -1])
        strips = (x_strips, edge_pair(masked, "gx", 2))
        image = stencil(masked, faces, strips) + (1.0 - active) * update
        residual = residual - image
    return (adjoint, residual)


def solution(mesh):
    in_specs = (
        P(None, "gy", "gx"),
        P(None, "gy", "gx"),
        P(None, "gy", "gx"),
        P(),
        P("gy"),
        P(),
        P(),
        P("gx"),
        P(),
        P(),
        P(),
    )
    out_specs = (P(None, "gy", "gx"), P(None, "gy", "gx"))
    return jax.shard_map(shards, mesh=mesh, in_specs=in_specs, out_specs=out_specs, check_vma=False)
```

```python
import jax
import jax.numpy as jnp
from jax import lax
from jax.experimental import pallas as pl
from jax.experimental.pallas import tpu as pltpu
from jax.sharding import PartitionSpec as P

ITERS = 2


storage_term = 0.2


def edges(block):
    strips = []
    for axis, dim in (("gy", 1), ("gx", 2)):
        count = lax.axis_size(axis)
        forward = [(i, i + 1) for i in range(count - 1)]
        backward = [(target, source) for source, target in forward]
        last = lax.index_in_dim(block, block.shape[dim] - 1, axis=dim, keepdims=False)
        first = lax.index_in_dim(block, 0, axis=dim, keepdims=False)
        strips.append((lax.ppermute(last, axis, forward), lax.ppermute(first, axis, backward)))
    return strips


def harmonic(first, second):
    return 2.0 * first * second / (first + second)


def framed(center, strips):
    (x_low, x_high), (y_low, y_high) = strips
    rows = jnp.concatenate([x_low[:, None, :], center, x_high[:, None, :]], axis=1)
    corner = jnp.zeros_like(center[:, :1, :1])
    low = jnp.concatenate([corner, y_low[:, :, None], corner], axis=1)
    high = jnp.concatenate([corner, y_high[:, :, None], corner], axis=1)
    block = jnp.concatenate([low, rows, high], axis=2)
    return jnp.pad(block, ((1, 1), (0, 0), (0, 0)))


def neighbours(padded):
    return [
        padded[2:, 1:-1, 1:-1],
        padded[:-2, 1:-1, 1:-1],
        padded[1:-1, 2:, 1:-1],
        padded[1:-1, :-2, 1:-1],
        padded[1:-1, 1:-1, 2:],
        padded[1:-1, 1:-1, :-2],
    ]


def faces_from(center):
    padded = framed(center, edges(center))
    return [harmonic(center, other) for other in neighbours(padded)]


def stencil(center, faces):
    padded = framed(center, edges(center))
    result = storage_term * center
    for face, other in zip(faces, neighbours(padded)):
        result = result + face * (center - other)
    return result


def solve_kernel(diag_ref, coup_ref, shifts_ref, rhs_ref, out_ref, ratio_ref):
    count = rhs_ref.shape[0]
    shifts = shifts_ref[...]
    denom = diag_ref[0] + shifts
    ratio = -coup_ref[0] / denom
    ratio_ref[0] = ratio
    part = rhs_ref[0] / denom
    out_ref[0] = part
    for position in range(1, count):
        denom = diag_ref[position] + shifts + coup_ref[position - 1] * ratio
        if position < count - 1:
            ratio = -coup_ref[position] / denom
            ratio_ref[position] = ratio
        part = (rhs_ref[position] + coup_ref[position - 1] * part) / denom
        out_ref[position] = part
    solved = part
    for position in range(count - 2, -1, -1):
        solved = out_ref[position] - ratio_ref[position] * solved
        out_ref[position] = solved


def vertical_solve(rhs, diagonal, coupling, shifts):
    smem = pl.BlockSpec(memory_space=pltpu.SMEM)
    vmem = pl.BlockSpec(memory_space=pltpu.VMEM)
    return pl.pallas_call(
        solve_kernel,
        out_shape=jax.ShapeDtypeStruct(rhs.shape, rhs.dtype),
        in_specs=[smem, smem, vmem, vmem],
        out_specs=vmem,
        scratch_shapes=[pltpu.VMEM(rhs.shape, rhs.dtype)],
    )(diagonal, coupling, shifts, rhs)


def split_bf16(values):
    rounded = lax.reduce_precision(values, exponent_bits=8, mantissa_bits=7)
    return rounded.astype(jnp.bfloat16), (values - rounded).astype(jnp.bfloat16)


def transform(spec, data, basis):
    high, low = split_bf16(data)
    basis_high, basis_low = basis

    def product(first, second):
        return jnp.einsum(spec, first, second, preferred_element_type=jnp.float32)

    return product(high, basis_high) + (product(low, basis_high) + product(high, basis_low))


def shards(
    right_side,
    conduct,
    excavated,
    vectors_x,
    mass_x,
    values_x,
    vectors_y,
    mass_y,
    values_y,
    vertical_diag,
    vertical_coupling,
):
    active = excavated.astype(jnp.float32)
    faces = faces_from(conduct)
    local_modes = vectors_x.shape[1] // (lax.axis_size("gx") * lax.axis_size("gy"))
    mode_start = (lax.axis_index("gx") * lax.axis_size("gy") + lax.axis_index("gy")) * local_modes
    local_values = lax.dynamic_slice_in_dim(values_x, mode_start, local_modes, 0)
    shifts = local_values[:, None] + values_y[None, :]
    adjoint = jnp.zeros_like(right_side)
    residual = right_side
    everyone = ("gx", "gy")
    blocks_y = lax.axis_size("gx")
    basis_x = split_bf16(vectors_x)
    basis_y = tuple(piece.reshape(blocks_y, -1, vectors_y.shape[1]) for piece in split_bf16(vectors_y))
    for iteration in range(ITERS):
        scaled = residual * mass_x[None, :, None] * mass_y[None, None, :]
        modes = transform(
            "zxy,xi->ziy",
            lax.all_to_all(scaled, "gy", split_axis=0, concat_axis=1, tiled=True),
            basis_x,
        )
        chunks = modes.reshape(-1, local_modes, modes.shape[2])
        chunks = lax.all_to_all(chunks, everyone, split_axis=0, concat_axis=0, tiled=True)
        chunks = chunks.reshape(blocks_y, -1, local_modes, chunks.shape[2])
        modes = transform("azil,alj->zij", chunks, basis_y)
        solved = vertical_solve(modes, vertical_diag, vertical_coupling, shifts)
        chunks = transform("zij,alj->azil", solved, basis_y)
        chunks = chunks.reshape(-1, local_modes, chunks.shape[3])
        chunks = lax.all_to_all(chunks, everyone, split_axis=0, concat_axis=0, tiled=True)
        solved = chunks.reshape(1, -1, chunks.shape[2])
        solved = transform("ziy,xi->zxy", solved, basis_x)
        update = lax.all_to_all(solved, "gy", split_axis=1, concat_axis=0, tiled=True)
        adjoint = adjoint + update
        masked = active * update
        image = stencil(masked, faces) + (1.0 - active) * update
        residual = residual - image
    return (adjoint, residual)


def solution(mesh):
    in_specs = (
        P(None, "gy", "gx"),
        P(None, "gy", "gx"),
        P(None, "gy", "gx"),
        P(),
        P("gy"),
        P(),
        P(),
        P("gx"),
        P(),
        P(),
        P(),
    )
    out_specs = (P(None, "gy", "gx"), P(None, "gy", "gx"))
    return jax.shard_map(shards, mesh=mesh, in_specs=in_specs, out_specs=out_specs, check_vma=False)
```

```python
import jax
import jax.numpy as jnp
from jax import lax
from jax.experimental import pallas as pl
from jax.experimental.pallas import tpu as pltpu
from jax.sharding import PartitionSpec as P

ITERS = 2


storage_term = 0.2


def edges(block):
    strips = []
    for axis, dim in (("gy", 1), ("gx", 2)):
        count = lax.axis_size(axis)
        forward = [(i, i + 1) for i in range(count - 1)]
        backward = [(target, source) for source, target in forward]
        last = lax.index_in_dim(block, block.shape[dim] - 1, axis=dim, keepdims=False)
        first = lax.index_in_dim(block, 0, axis=dim, keepdims=False)
        strips.append((lax.ppermute(last, axis, forward), lax.ppermute(first, axis, backward)))
    return strips


def harmonic(first, second):
    return 2.0 * first * second / (first + second)


def neighbours(center, strips):
    (x_low, x_high), (y_low, y_high) = strips
    zeros = jnp.zeros_like(center[:1])
    return [
        jnp.concatenate([center[1:], zeros], axis=0),
        jnp.concatenate([zeros, center[:-1]], axis=0),
        jnp.concatenate([center[:, 1:], x_high[:, None, :]], axis=1),
        jnp.concatenate([x_low[:, None, :], center[:, :-1]], axis=1),
        jnp.concatenate([center[:, :, 1:], y_high[:, :, None]], axis=2),
        jnp.concatenate([y_low[:, :, None], center[:, :, :-1]], axis=2),
    ]


def faces_from(center):
    return [harmonic(center, other) for other in neighbours(center, edges(center))]


def stencil_kernel(
    update_ref, active_ref, residual_ref, faces_ref, x_low_ref, x_high_ref,
    y_low_ref, y_high_ref, mass_x_ref, mass_y_ref, out_ref, scaled_ref,
):
    planes, rows, cols = update_ref.shape
    row = lax.broadcasted_iota(jnp.int32, (rows, cols), 0)
    col = lax.broadcasted_iota(jnp.int32, (rows, cols), 1)
    row_forward = pltpu.roll(row, 1, 0) == jnp.where(row == 0, rows - 1, row - 1)
    col_forward = pltpu.roll(col, 1, 1) == jnp.where(col == 0, cols - 1, col - 1)

    def before(plane, axis, count, forward):
        return jnp.where(forward, pltpu.roll(plane, 1, axis), pltpu.roll(plane, count - 1, axis))

    def after(plane, axis, count, forward):
        return jnp.where(forward, pltpu.roll(plane, count - 1, axis), pltpu.roll(plane, 1, axis))

    zeros = jnp.zeros((rows, cols), jnp.float32)
    masked = [active_ref[z] * update_ref[z] for z in range(planes)]
    for z in range(planes):
        center = masked[z]
        x_low = jnp.broadcast_to(x_low_ref[pl.ds(z, 1), :], (rows, cols))
        x_high = jnp.broadcast_to(x_high_ref[pl.ds(z, 1), :], (rows, cols))
        others = [
            masked[z + 1] if z + 1 < planes else zeros,
            masked[z - 1] if z > 0 else zeros,
            jnp.where(row == rows - 1, x_high, after(center, 0, rows, row_forward)),
            jnp.where(row == 0, x_low, before(center, 0, rows, row_forward)),
            jnp.where(col == cols - 1, y_high_ref[z], after(center, 1, cols, col_forward)),
            jnp.where(col == 0, y_low_ref[z], before(center, 1, cols, col_forward)),
        ]
        result = storage_term * center
        for face, other in enumerate(others):
            result = result + faces_ref[face, z] * (center - other)
        update = update_ref[z]
        image = result + (1.0 - active_ref[z]) * update
        residual = residual_ref[z] - image
        out_ref[z] = residual
        scaled_ref[z] = residual * mass_x_ref[...] * mass_y_ref[...]


def fused_stencil(update, active, residual, faces, x_strips, y_strips, mass_x, mass_y):
    planes, rows, cols = update.shape
    y_low, y_high = (jnp.broadcast_to(s[:, :, None], update.shape) for s in y_strips)
    mass_x = jnp.broadcast_to(mass_x[:, None], (rows, cols))
    mass_y = jnp.broadcast_to(mass_y[None, :], (rows, cols))
    vmem = pl.BlockSpec(memory_space=pltpu.VMEM)
    shape = jax.ShapeDtypeStruct(update.shape, update.dtype)
    return pl.pallas_call(
        stencil_kernel,
        out_shape=(shape, shape),
        in_specs=[vmem] * 10,
        out_specs=(vmem, vmem),
    )(update, active, residual, faces, x_strips[0], x_strips[1], y_low, y_high, mass_x, mass_y)


def solve_kernel(diag_ref, coup_ref, shifts_ref, rhs_ref, out_ref, ratio_ref):
    count = rhs_ref.shape[0]
    shifts = shifts_ref[...]
    denom = diag_ref[0] + shifts
    ratio = -coup_ref[0] / denom
    ratio_ref[0] = ratio
    part = rhs_ref[0] / denom
    out_ref[0] = part
    for position in range(1, count):
        denom = diag_ref[position] + shifts + coup_ref[position - 1] * ratio
        if position < count - 1:
            ratio = -coup_ref[position] / denom
            ratio_ref[position] = ratio
        part = (rhs_ref[position] + coup_ref[position - 1] * part) / denom
        out_ref[position] = part
    solved = part
    for position in range(count - 2, -1, -1):
        solved = out_ref[position] - ratio_ref[position] * solved
        out_ref[position] = solved


def vertical_solve(rhs, diagonal, coupling, shifts):
    smem = pl.BlockSpec(memory_space=pltpu.SMEM)
    vmem = pl.BlockSpec(memory_space=pltpu.VMEM)
    return pl.pallas_call(
        solve_kernel,
        out_shape=jax.ShapeDtypeStruct(rhs.shape, rhs.dtype),
        in_specs=[smem, smem, vmem, vmem],
        out_specs=vmem,
        scratch_shapes=[pltpu.VMEM(rhs.shape, rhs.dtype)],
    )(diagonal, coupling, shifts, rhs)


def split_bf16(values):
    rounded = lax.reduce_precision(values, exponent_bits=8, mantissa_bits=7)
    return rounded.astype(jnp.bfloat16), (values - rounded).astype(jnp.bfloat16)


def transform(spec, data, basis):
    high, low = split_bf16(data)
    basis_high, basis_low = basis

    def product(first, second):
        return jnp.einsum(spec, first, second, preferred_element_type=jnp.float32)

    return product(high, basis_high) + (product(low, basis_high) + product(high, basis_low))


def shards(
    right_side,
    conduct,
    excavated,
    vectors_x,
    mass_x,
    values_x,
    vectors_y,
    mass_y,
    values_y,
    vertical_diag,
    vertical_coupling,
):
    active = excavated.astype(jnp.float32)
    faces = faces_from(conduct)
    local_modes = vectors_x.shape[1] // (lax.axis_size("gx") * lax.axis_size("gy"))
    mode_start = (lax.axis_index("gx") * lax.axis_size("gy") + lax.axis_index("gy")) * local_modes
    local_values = lax.dynamic_slice_in_dim(values_x, mode_start, local_modes, 0)
    shifts = local_values[:, None] + values_y[None, :]
    adjoint = jnp.zeros_like(right_side)
    residual = right_side
    everyone = ("gx", "gy")
    blocks_y = lax.axis_size("gx")
    basis_x = split_bf16(vectors_x)
    basis_y = tuple(piece.reshape(blocks_y, -1, vectors_y.shape[1]) for piece in split_bf16(vectors_y))
    faces = jnp.stack(faces)
    scaled = residual * mass_x[None, :, None] * mass_y[None, None, :]
    for iteration in range(ITERS):
        modes = transform(
            "zxy,xi->ziy",
            lax.all_to_all(scaled, "gy", split_axis=0, concat_axis=1, tiled=True),
            basis_x,
        )
        chunks = modes.reshape(-1, local_modes, modes.shape[2])
        chunks = lax.all_to_all(chunks, everyone, split_axis=0, concat_axis=0, tiled=True)
        chunks = chunks.reshape(blocks_y, -1, local_modes, chunks.shape[2])
        modes = transform("azil,alj->zij", chunks, basis_y)
        solved = vertical_solve(modes, vertical_diag, vertical_coupling, shifts)
        chunks = transform("zij,alj->azil", solved, basis_y)
        chunks = chunks.reshape(-1, local_modes, chunks.shape[3])
        chunks = lax.all_to_all(chunks, everyone, split_axis=0, concat_axis=0, tiled=True)
        solved = chunks.reshape(1, -1, chunks.shape[2])
        solved = transform("ziy,xi->zxy", solved, basis_x)
        update = lax.all_to_all(solved, "gy", split_axis=1, concat_axis=0, tiled=True)
        adjoint = adjoint + update
        x_strips, y_strips = edges(active * update)
        residual, scaled = fused_stencil(update, active, residual, faces, x_strips, y_strips, mass_x, mass_y)
    return (adjoint, residual)


def solution(mesh):
    in_specs = (
        P(None, "gy", "gx"),
        P(None, "gy", "gx"),
        P(None, "gy", "gx"),
        P(),
        P("gy"),
        P(),
        P(),
        P("gx"),
        P(),
        P(),
        P(),
    )
    out_specs = (P(None, "gy", "gx"), P(None, "gy", "gx"))
    return jax.shard_map(shards, mesh=mesh, in_specs=in_specs, out_specs=out_specs, check_vma=False)
```

```python
import jax
import jax.numpy as jnp
from jax import lax
from jax.experimental import pallas as pl
from jax.experimental.pallas import tpu as pltpu
from jax.sharding import PartitionSpec as P

ITERS = 2


storage_term = 0.2


def edges(block):
    strips = []
    for axis, dim in (("gy", 1), ("gx", 2)):
        count = lax.axis_size(axis)
        forward = [(i, i + 1) for i in range(count - 1)]
        backward = [(target, source) for source, target in forward]
        last = lax.index_in_dim(block, block.shape[dim] - 1, axis=dim, keepdims=False)
        first = lax.index_in_dim(block, 0, axis=dim, keepdims=False)
        strips.append((lax.ppermute(last, axis, forward), lax.ppermute(first, axis, backward)))
    return strips


def harmonic(first, second):
    return 2.0 * first * second / (first + second)


def neighbours(center, strips):
    (x_low, x_high), (y_low, y_high) = strips
    zeros = jnp.zeros_like(center[:1])
    return [
        jnp.concatenate([center[1:], zeros], axis=0),
        jnp.concatenate([zeros, center[:-1]], axis=0),
        jnp.concatenate([center[:, 1:], x_high[:, None, :]], axis=1),
        jnp.concatenate([x_low[:, None, :], center[:, :-1]], axis=1),
        jnp.concatenate([center[:, :, 1:], y_high[:, :, None]], axis=2),
        jnp.concatenate([y_low[:, :, None], center[:, :, :-1]], axis=2),
    ]


def faces_from(center):
    return [harmonic(center, other) for other in neighbours(center, edges(center))]


def stencil_kernel(update_ref, active_ref, residual_ref, *refs):
    face_refs, out_ref = refs[:-1], refs[-1]
    planes, rows, cols = update_ref.shape
    row = lax.broadcasted_iota(jnp.int32, (rows, cols), 0)
    col = lax.broadcasted_iota(jnp.int32, (rows, cols), 1)
    row_forward = pltpu.roll(row, 1, 0) == jnp.where(row == 0, rows - 1, row - 1)
    col_forward = pltpu.roll(col, 1, 1) == jnp.where(col == 0, cols - 1, col - 1)

    def before(plane, axis, count, forward):
        return jnp.where(forward, pltpu.roll(plane, 1, axis), pltpu.roll(plane, count - 1, axis))

    def after(plane, axis, count, forward):
        return jnp.where(forward, pltpu.roll(plane, count - 1, axis), pltpu.roll(plane, 1, axis))

    zeros = jnp.zeros((rows, cols), jnp.float32)
    masked = [active_ref[z] * update_ref[z] for z in range(planes)]
    for z in range(planes):
        center = masked[z]
        others = [
            masked[z + 1] if z + 1 < planes else zeros,
            masked[z - 1] if z > 0 else zeros,
            jnp.where(row == rows - 1, zeros, after(center, 0, rows, row_forward)),
            jnp.where(row == 0, zeros, before(center, 0, rows, row_forward)),
            jnp.where(col == cols - 1, zeros, after(center, 1, cols, col_forward)),
            jnp.where(col == 0, zeros, before(center, 1, cols, col_forward)),
        ]
        result = storage_term * center
        for face_ref, other in zip(face_refs, others):
            result = result + face_ref[z] * (center - other)
        update = update_ref[z]
        out_ref[z] = residual_ref[z] - (result + (1.0 - active_ref[z]) * update)


def fused_stencil(update, active, residual, faces):
    vmem = pl.BlockSpec(memory_space=pltpu.VMEM)
    return pl.pallas_call(
        stencil_kernel,
        out_shape=jax.ShapeDtypeStruct(update.shape, update.dtype),
        in_specs=[vmem] * (3 + len(faces)),
        out_specs=vmem,
    )(update, active, residual, *faces)


def add_halo_terms(residual, faces, strips):
    (x_low, x_high), (y_low, y_high) = strips
    residual = residual.at[:, 0, :].add(faces[3][:, 0, :] * x_low)
    residual = residual.at[:, -1, :].add(faces[2][:, -1, :] * x_high)
    residual = residual.at[:, :, 0].add(faces[5][:, :, 0] * y_low)
    return residual.at[:, :, -1].add(faces[4][:, :, -1] * y_high)


def solve_kernel(diag_ref, coup_ref, shifts_ref, rhs_ref, out_ref, ratio_ref):
    count = rhs_ref.shape[0]
    shifts = shifts_ref[...]
    denom = diag_ref[0] + shifts
    ratio = -coup_ref[0] / denom
    ratio_ref[0] = ratio
    part = rhs_ref[0] / denom
    out_ref[0] = part
    for position in range(1, count):
        denom = diag_ref[position] + shifts + coup_ref[position - 1] * ratio
        if position < count - 1:
            ratio = -coup_ref[position] / denom
            ratio_ref[position] = ratio
        part = (rhs_ref[position] + coup_ref[position - 1] * part) / denom
        out_ref[position] = part
    solved = part
    for position in range(count - 2, -1, -1):
        solved = out_ref[position] - ratio_ref[position] * solved
        out_ref[position] = solved


def vertical_solve(rhs, diagonal, coupling, shifts):
    smem = pl.BlockSpec(memory_space=pltpu.SMEM)
    vmem = pl.BlockSpec(memory_space=pltpu.VMEM)
    return pl.pallas_call(
        solve_kernel,
        out_shape=jax.ShapeDtypeStruct(rhs.shape, rhs.dtype),
        in_specs=[smem, smem, vmem, vmem],
        out_specs=vmem,
        scratch_shapes=[pltpu.VMEM(rhs.shape, rhs.dtype)],
    )(diagonal, coupling, shifts, rhs)


def split_bf16(values):
    rounded = lax.reduce_precision(values, exponent_bits=8, mantissa_bits=7)
    return rounded.astype(jnp.bfloat16), (values - rounded).astype(jnp.bfloat16)


def transform(spec, data, basis):
    high, low = split_bf16(data)
    basis_high, basis_low = basis

    def product(first, second):
        return jnp.einsum(spec, first, second, preferred_element_type=jnp.float32)

    return product(high, basis_high) + (product(low, basis_high) + product(high, basis_low))


def shards(
    right_side,
    conduct,
    excavated,
    vectors_x,
    mass_x,
    values_x,
    vectors_y,
    mass_y,
    values_y,
    vertical_diag,
    vertical_coupling,
):
    active = excavated.astype(jnp.float32)
    faces = faces_from(conduct)
    local_modes = vectors_x.shape[1] // (lax.axis_size("gx") * lax.axis_size("gy"))
    mode_start = (lax.axis_index("gx") * lax.axis_size("gy") + lax.axis_index("gy")) * local_modes
    local_values = lax.dynamic_slice_in_dim(values_x, mode_start, local_modes, 0)
    shifts = local_values[:, None] + values_y[None, :]
    adjoint = jnp.zeros_like(right_side)
    residual = right_side
    everyone = ("gx", "gy")
    blocks_y = lax.axis_size("gx")
    basis_x = split_bf16(vectors_x)
    basis_y = tuple(piece.reshape(blocks_y, -1, vectors_y.shape[1]) for piece in split_bf16(vectors_y))
    for iteration in range(ITERS):
        scaled = residual * mass_x[None, :, None] * mass_y[None, None, :]
        modes = transform(
            "zxy,xi->ziy",
            lax.all_to_all(scaled, "gy", split_axis=0, concat_axis=1, tiled=True),
            basis_x,
        )
        chunks = modes.reshape(-1, local_modes, modes.shape[2])
        chunks = lax.all_to_all(chunks, everyone, split_axis=0, concat_axis=0, tiled=True)
        chunks = chunks.reshape(blocks_y, -1, local_modes, chunks.shape[2])
        modes = transform("azil,alj->zij", chunks, basis_y)
        solved = vertical_solve(modes, vertical_diag, vertical_coupling, shifts)
        chunks = transform("zij,alj->azil", solved, basis_y)
        chunks = chunks.reshape(-1, local_modes, chunks.shape[3])
        chunks = lax.all_to_all(chunks, everyone, split_axis=0, concat_axis=0, tiled=True)
        solved = chunks.reshape(1, -1, chunks.shape[2])
        solved = transform("ziy,xi->zxy", solved, basis_x)
        update = lax.all_to_all(solved, "gy", split_axis=1, concat_axis=0, tiled=True)
        adjoint = adjoint + update
        strips = edges(active * update)
        residual = add_halo_terms(fused_stencil(update, active, residual, faces), faces, strips)
    return (adjoint, residual)


def solution(mesh):
    in_specs = (
        P(None, "gy", "gx"),
        P(None, "gy", "gx"),
        P(None, "gy", "gx"),
        P(),
        P("gy"),
        P(),
        P(),
        P("gx"),
        P(),
        P(),
        P(),
    )
    out_specs = (P(None, "gy", "gx"), P(None, "gy", "gx"))
    return jax.shard_map(shards, mesh=mesh, in_specs=in_specs, out_specs=out_specs, check_vma=False)
```

```python
import jax
import jax.numpy as jnp
from jax import lax
from jax.experimental import pallas as pl
from jax.experimental.pallas import tpu as pltpu
from jax.sharding import PartitionSpec as P

ITERS = 2


storage_term = 0.2


def edge_pair(block, axis, dim):
    count = lax.axis_size(axis)
    forward = [(i, i + 1) for i in range(count - 1)]
    backward = [(target, source) for source, target in forward]
    last = lax.index_in_dim(block, block.shape[dim] - 1, axis=dim, keepdims=False)
    first = lax.index_in_dim(block, 0, axis=dim, keepdims=False)
    return lax.ppermute(last, axis, forward), lax.ppermute(first, axis, backward)


def edges(block):
    return [edge_pair(block, "gy", 1), edge_pair(block, "gx", 2)]


def harmonic(first, second):
    return 2.0 * first * second / (first + second)


def neighbours(center, strips):
    (x_low, x_high), (y_low, y_high) = strips
    zeros = jnp.zeros_like(center[:1])
    return [
        jnp.concatenate([center[1:], zeros], axis=0),
        jnp.concatenate([zeros, center[:-1]], axis=0),
        jnp.concatenate([center[:, 1:], x_high[:, None, :]], axis=1),
        jnp.concatenate([x_low[:, None, :], center[:, :-1]], axis=1),
        jnp.concatenate([center[:, :, 1:], y_high[:, :, None]], axis=2),
        jnp.concatenate([y_low[:, :, None], center[:, :, :-1]], axis=2),
    ]


def faces_from(center):
    return [harmonic(center, other) for other in neighbours(center, edges(center))]


def framed_kernel(
    framed_ref, active_ref, residual_ref, adjoint_ref, x_low_ref, x_high_ref, y_low_ref, y_high_ref, *refs
):
    face_refs, residual_out, adjoint_out = refs[:-2], refs[-2], refs[-1]
    planes, rows, cols = active_ref.shape
    row = lax.broadcasted_iota(jnp.int32, (rows, cols), 0)
    col = lax.broadcasted_iota(jnp.int32, (rows, cols), 1)
    row_forward = pltpu.roll(row, 1, 0) == jnp.where(row == 0, rows - 1, row - 1)
    col_forward = pltpu.roll(col, 1, 1) == jnp.where(col == 0, cols - 1, col - 1)

    def before(plane, axis, count, forward):
        return jnp.where(forward, pltpu.roll(plane, 1, axis), pltpu.roll(plane, count - 1, axis))

    def after(plane, axis, count, forward):
        return jnp.where(forward, pltpu.roll(plane, count - 1, axis), pltpu.roll(plane, 1, axis))

    zeros = jnp.zeros((rows, cols), jnp.float32)
    updates = [framed_ref[z, pl.ds(1, rows), :] for z in range(planes)]
    masked = [active_ref[z] * updates[z] for z in range(planes)]
    for z in range(planes):
        center = masked[z]
        x_low = x_low_ref[pl.ds(z, 1), :] * framed_ref[z, pl.ds(0, 1), :]
        x_high = x_high_ref[pl.ds(z, 1), :] * framed_ref[z, pl.ds(rows + 1, 1), :]
        others = [
            masked[z + 1] if z + 1 < planes else zeros,
            masked[z - 1] if z > 0 else zeros,
            jnp.where(row == rows - 1, jnp.broadcast_to(x_high, (rows, cols)), after(center, 0, rows, row_forward)),
            jnp.where(row == 0, jnp.broadcast_to(x_low, (rows, cols)), before(center, 0, rows, row_forward)),
            jnp.where(col == cols - 1, y_high_ref[z], after(center, 1, cols, col_forward)),
            jnp.where(col == 0, y_low_ref[z], before(center, 1, cols, col_forward)),
        ]
        result = storage_term * center
        for face_ref, other in zip(face_refs, others):
            result = result + face_ref[z] * (center - other)
        update = updates[z]
        residual_out[z] = residual_ref[z] - (result + (1.0 - active_ref[z]) * update)
        adjoint_out[z] = adjoint_ref[z] + update


def framed_stencil(framed, active, residual, adjoint, x_strips, y_strips, faces):
    vmem = pl.BlockSpec(memory_space=pltpu.VMEM)
    shape = jax.ShapeDtypeStruct(active.shape, active.dtype)
    y_low, y_high = (jnp.broadcast_to(strip[:, :, None], active.shape) for strip in y_strips)
    return pl.pallas_call(
        framed_kernel,
        out_shape=(shape, shape),
        in_specs=[vmem] * (8 + len(faces)),
        out_specs=(vmem, vmem),
    )(framed, active, residual, adjoint, x_strips[0], x_strips[1], y_low, y_high, *faces)


def solve_kernel(diag_ref, coup_ref, shifts_ref, rhs_ref, out_ref, ratio_ref):
    count = rhs_ref.shape[0]
    shifts = shifts_ref[...]
    denom = diag_ref[0] + shifts
    ratio = -coup_ref[0] / denom
    ratio_ref[0] = ratio
    part = rhs_ref[0] / denom
    out_ref[0] = part
    for position in range(1, count):
        denom = diag_ref[position] + shifts + coup_ref[position - 1] * ratio
        if position < count - 1:
            ratio = -coup_ref[position] / denom
            ratio_ref[position] = ratio
        part = (rhs_ref[position] + coup_ref[position - 1] * part) / denom
        out_ref[position] = part
    solved = part
    for position in range(count - 2, -1, -1):
        solved = out_ref[position] - ratio_ref[position] * solved
        out_ref[position] = solved


def vertical_solve(rhs, diagonal, coupling, shifts):
    smem = pl.BlockSpec(memory_space=pltpu.SMEM)
    vmem = pl.BlockSpec(memory_space=pltpu.VMEM)
    return pl.pallas_call(
        solve_kernel,
        out_shape=jax.ShapeDtypeStruct(rhs.shape, rhs.dtype),
        in_specs=[smem, smem, vmem, vmem],
        out_specs=vmem,
        scratch_shapes=[pltpu.VMEM(rhs.shape, rhs.dtype)],
    )(diagonal, coupling, shifts, rhs)


def split_bf16(values):
    rounded = lax.reduce_precision(values, exponent_bits=8, mantissa_bits=7)
    return rounded.astype(jnp.bfloat16), (values - rounded).astype(jnp.bfloat16)


def transform(spec, data, basis):
    high, low = split_bf16(data)
    basis_high, basis_low = basis

    def product(first, second):
        return jnp.einsum(spec, first, second, preferred_element_type=jnp.float32)

    return product(high, basis_high) + (product(low, basis_high) + product(high, basis_low))


def shards(
    right_side,
    conduct,
    excavated,
    vectors_x,
    mass_x,
    values_x,
    vectors_y,
    mass_y,
    values_y,
    vertical_diag,
    vertical_coupling,
):
    active = excavated.astype(jnp.float32)
    faces = faces_from(conduct)
    local_modes = vectors_x.shape[1] // (lax.axis_size("gx") * lax.axis_size("gy"))
    mode_start = (lax.axis_index("gx") * lax.axis_size("gy") + lax.axis_index("gy")) * local_modes
    local_values = lax.dynamic_slice_in_dim(values_x, mode_start, local_modes, 0)
    shifts = local_values[:, None] + values_y[None, :]
    adjoint = jnp.zeros_like(right_side)
    residual = right_side
    everyone = ("gx", "gy")
    blocks_y = lax.axis_size("gx")
    basis_x = split_bf16(vectors_x)
    rows = right_side.shape[1]
    framed_basis = []
    for piece in basis_x:
        blocks = piece.reshape(-1, rows, piece.shape[1])
        zero = jnp.zeros_like(blocks[:1, :1])
        below = jnp.concatenate([zero, blocks[:-1, -1:]], axis=0)
        above = jnp.concatenate([blocks[1:, :1], zero], axis=0)
        framed_basis.append(jnp.concatenate([below, blocks, above], axis=1))
    active_x, active_y = edges(active)
    count_y = lax.axis_size("gx")
    forward_y = [(i, i + 1) for i in range(count_y - 1)]
    backward_y = [(target, source) for source, target in forward_y]
    basis_y = tuple(piece.reshape(blocks_y, -1, vectors_y.shape[1]) for piece in split_bf16(vectors_y))
    for iteration in range(ITERS):
        scaled = residual * mass_x[None, :, None] * mass_y[None, None, :]
        modes = transform(
            "zxy,xi->ziy",
            lax.all_to_all(scaled, "gy", split_axis=0, concat_axis=1, tiled=True),
            basis_x,
        )
        chunks = modes.reshape(-1, local_modes, modes.shape[2])
        chunks = lax.all_to_all(chunks, everyone, split_axis=0, concat_axis=0, tiled=True)
        chunks = chunks.reshape(blocks_y, -1, local_modes, chunks.shape[2])
        modes = transform("azil,alj->zij", chunks, basis_y)
        solved = vertical_solve(modes, vertical_diag, vertical_coupling, shifts)
        chunks = transform("zij,alj->azil", solved, basis_y)
        chunks = chunks.reshape(-1, local_modes, chunks.shape[3])
        chunks = lax.all_to_all(chunks, everyone, split_axis=0, concat_axis=0, tiled=True)
        solved = chunks.reshape(-1, chunks.shape[2])
        framed = transform("iy,bri->bry", solved, framed_basis)
        from_left = lax.ppermute(framed[:, 1:-1, -1], "gx", forward_y)
        from_right = lax.ppermute(framed[:, 1:-1, 0], "gx", backward_y)
        halo_row = jnp.concatenate([from_left, from_right], axis=1)[:, None, :]
        framed = jnp.concatenate([framed, halo_row], axis=1)
        framed = lax.all_to_all(framed, "gy", split_axis=0, concat_axis=0, tiled=True)
        y_strips = (active_y[0] * framed[:, -1, :rows], active_y[1] * framed[:, -1, rows:])
        residual, adjoint = framed_stencil(framed, active, residual, adjoint, active_x, y_strips, faces)
    return (adjoint, residual)


def solution(mesh):
    in_specs = (
        P(None, "gy", "gx"),
        P(None, "gy", "gx"),
        P(None, "gy", "gx"),
        P(),
        P("gy"),
        P(),
        P(),
        P("gx"),
        P(),
        P(),
        P(),
    )
    out_specs = (P(None, "gy", "gx"), P(None, "gy", "gx"))
    return jax.shard_map(shards, mesh=mesh, in_specs=in_specs, out_specs=out_specs, check_vma=False)
```

```python
import jax
import jax.numpy as jnp
from jax import lax
from jax.experimental import pallas as pl
from jax.experimental.pallas import tpu as pltpu
from jax.sharding import PartitionSpec as P

ITERS = 2


storage_term = 0.2


def edge_pair(block, axis, dim):
    count = lax.axis_size(axis)
    forward = [(i, i + 1) for i in range(count - 1)]
    backward = [(target, source) for source, target in forward]
    last = lax.index_in_dim(block, block.shape[dim] - 1, axis=dim, keepdims=False)
    first = lax.index_in_dim(block, 0, axis=dim, keepdims=False)
    return lax.ppermute(last, axis, forward), lax.ppermute(first, axis, backward)


def edges(block):
    return [edge_pair(block, "gy", block.ndim - 2), edge_pair(block, "gx", block.ndim - 1)]


def harmonic(first, second):
    return 2.0 * first * second / (first + second)


def neighbours(center, strips):
    (x_low, x_high), (y_low, y_high) = strips
    zeros = jnp.zeros_like(center[:1])
    return [
        jnp.concatenate([center[1:], zeros], axis=0),
        jnp.concatenate([zeros, center[:-1]], axis=0),
        jnp.concatenate([center[:, 1:], x_high[:, None, :]], axis=1),
        jnp.concatenate([x_low[:, None, :], center[:, :-1]], axis=1),
        jnp.concatenate([center[:, :, 1:], y_high[:, :, None]], axis=2),
        jnp.concatenate([y_low[:, :, None], center[:, :, :-1]], axis=2),
    ]


def faces_from(center, strips):
    return [harmonic(center, other) for other in neighbours(center, strips)]


def framed_kernel(
    framed_ref, active_ref, residual_ref, adjoint_ref, x_low_ref, x_high_ref, y_low_ref, y_high_ref, *refs
):
    face_refs, residual_out, adjoint_out = refs[:-2], refs[-2], refs[-1]
    planes, rows, cols = active_ref.shape
    row = lax.broadcasted_iota(jnp.int32, (rows, cols), 0)
    col = lax.broadcasted_iota(jnp.int32, (rows, cols), 1)
    row_forward = pltpu.roll(row, 1, 0) == jnp.where(row == 0, rows - 1, row - 1)
    col_forward = pltpu.roll(col, 1, 1) == jnp.where(col == 0, cols - 1, col - 1)

    def before(plane, axis, count, forward):
        return jnp.where(forward, pltpu.roll(plane, 1, axis), pltpu.roll(plane, count - 1, axis))

    def after(plane, axis, count, forward):
        return jnp.where(forward, pltpu.roll(plane, count - 1, axis), pltpu.roll(plane, 1, axis))

    zeros = jnp.zeros((rows, cols), jnp.float32)
    updates = [framed_ref[z, pl.ds(1, rows), :] for z in range(planes)]
    masked = [active_ref[z] * updates[z] for z in range(planes)]
    for z in range(planes):
        center = masked[z]
        x_low = x_low_ref[pl.ds(z, 1), :] * framed_ref[z, pl.ds(0, 1), :]
        x_high = x_high_ref[pl.ds(z, 1), :] * framed_ref[z, pl.ds(rows + 1, 1), :]
        others = [
            masked[z + 1] if z + 1 < planes else zeros,
            masked[z - 1] if z > 0 else zeros,
            jnp.where(row == rows - 1, jnp.broadcast_to(x_high, (rows, cols)), after(center, 0, rows, row_forward)),
            jnp.where(row == 0, jnp.broadcast_to(x_low, (rows, cols)), before(center, 0, rows, row_forward)),
            jnp.where(col == cols - 1, y_high_ref[z], after(center, 1, cols, col_forward)),
            jnp.where(col == 0, y_low_ref[z], before(center, 1, cols, col_forward)),
        ]
        result = storage_term * center
        for face_ref, other in zip(face_refs, others):
            result = result + face_ref[z] * (center - other)
        update = updates[z]
        residual_out[z] = residual_ref[z] - (result + (1.0 - active_ref[z]) * update)
        adjoint_out[z] = adjoint_ref[z] + update


def framed_stencil(framed, active, residual, adjoint, x_strips, y_strips, faces):
    vmem = pl.BlockSpec(memory_space=pltpu.VMEM)
    shape = jax.ShapeDtypeStruct(active.shape, active.dtype)
    y_low, y_high = (jnp.broadcast_to(strip[:, :, None], active.shape) for strip in y_strips)
    return pl.pallas_call(
        framed_kernel,
        out_shape=(shape, shape),
        in_specs=[vmem] * (8 + len(faces)),
        out_specs=(vmem, vmem),
    )(framed, active, residual, adjoint, x_strips[0], x_strips[1], y_low, y_high, *faces)


def solve_kernel(diag_ref, coup_ref, shifts_ref, rhs_ref, out_ref, ratio_ref):
    count = rhs_ref.shape[0]
    shifts = shifts_ref[...]
    denom = diag_ref[0] + shifts
    ratio = -coup_ref[0] / denom
    ratio_ref[0] = ratio
    part = rhs_ref[0] / denom
    out_ref[0] = part
    for position in range(1, count):
        denom = diag_ref[position] + shifts + coup_ref[position - 1] * ratio
        if position < count - 1:
            ratio = -coup_ref[position] / denom
            ratio_ref[position] = ratio
        part = (rhs_ref[position] + coup_ref[position - 1] * part) / denom
        out_ref[position] = part
    solved = part
    for position in range(count - 2, -1, -1):
        solved = out_ref[position] - ratio_ref[position] * solved
        out_ref[position] = solved


def vertical_solve(rhs, diagonal, coupling, shifts):
    smem = pl.BlockSpec(memory_space=pltpu.SMEM)
    vmem = pl.BlockSpec(memory_space=pltpu.VMEM)
    return pl.pallas_call(
        solve_kernel,
        out_shape=jax.ShapeDtypeStruct(rhs.shape, rhs.dtype),
        in_specs=[smem, smem, vmem, vmem],
        out_specs=vmem,
        scratch_shapes=[pltpu.VMEM(rhs.shape, rhs.dtype)],
    )(diagonal, coupling, shifts, rhs)


def split_bf16(values):
    rounded = lax.reduce_precision(values, exponent_bits=8, mantissa_bits=7)
    return rounded.astype(jnp.bfloat16), (values - rounded).astype(jnp.bfloat16)


def transform(spec, data, basis):
    high, low = split_bf16(data)
    basis_high, basis_low = basis

    def product(first, second):
        return jnp.einsum(spec, first, second, preferred_element_type=jnp.float32)

    return product(high, basis_high) + (product(low, basis_high) + product(high, basis_low))


def shards(
    right_side,
    conduct,
    excavated,
    vectors_x,
    mass_x,
    values_x,
    vectors_y,
    mass_y,
    values_y,
    vertical_diag,
    vertical_coupling,
):
    active = excavated.astype(jnp.float32)
    both = edges(jnp.stack([conduct, active]))
    faces = faces_from(conduct, [(low[0], high[0]) for low, high in both])
    active_x, active_y = [(low[1], high[1]) for low, high in both]
    local_modes = vectors_x.shape[1] // (lax.axis_size("gx") * lax.axis_size("gy"))
    mode_start = (lax.axis_index("gx") * lax.axis_size("gy") + lax.axis_index("gy")) * local_modes
    local_values = lax.dynamic_slice_in_dim(values_x, mode_start, local_modes, 0)
    shifts = local_values[:, None] + values_y[None, :]
    adjoint = jnp.zeros_like(right_side)
    residual = right_side
    everyone = ("gx", "gy")
    blocks_y = lax.axis_size("gx")
    basis_x = split_bf16(vectors_x)
    rows = right_side.shape[1]
    framed_basis = []
    for piece in basis_x:
        blocks = piece.reshape(-1, rows, piece.shape[1])
        zero = jnp.zeros_like(blocks[:1, :1])
        below = jnp.concatenate([zero, blocks[:-1, -1:]], axis=0)
        above = jnp.concatenate([blocks[1:, :1], zero], axis=0)
        framed_basis.append(jnp.concatenate([below, blocks, above], axis=1))
    count_y = lax.axis_size("gx")
    forward_y = [(i, i + 1) for i in range(count_y - 1)]
    backward_y = [(target, source) for source, target in forward_y]
    basis_y = tuple(piece.reshape(blocks_y, -1, vectors_y.shape[1]) for piece in split_bf16(vectors_y))
    for iteration in range(ITERS):
        scaled = residual * mass_x[None, :, None] * mass_y[None, None, :]
        modes = transform(
            "zxy,xi->ziy",
            lax.all_to_all(scaled, "gy", split_axis=0, concat_axis=1, tiled=True),
            basis_x,
        )
        chunks = modes.reshape(-1, local_modes, modes.shape[2])
        chunks = lax.all_to_all(chunks, everyone, split_axis=0, concat_axis=0, tiled=True)
        chunks = chunks.reshape(blocks_y, -1, local_modes, chunks.shape[2])
        modes = transform("azil,alj->zij", chunks, basis_y)
        solved = vertical_solve(modes, vertical_diag, vertical_coupling, shifts)
        chunks = transform("zij,alj->azil", solved, basis_y)
        chunks = chunks.reshape(-1, local_modes, chunks.shape[3])
        chunks = lax.all_to_all(chunks, everyone, split_axis=0, concat_axis=0, tiled=True)
        solved = chunks.reshape(-1, chunks.shape[2])
        framed = transform("iy,bri->bry", solved, framed_basis)
        from_left = lax.ppermute(framed[:, 1:-1, -1], "gx", forward_y)
        from_right = lax.ppermute(framed[:, 1:-1, 0], "gx", backward_y)
        halo_row = jnp.concatenate([from_left, from_right], axis=1)[:, None, :]
        framed = jnp.concatenate([framed, halo_row], axis=1)
        framed = lax.all_to_all(framed, "gy", split_axis=0, concat_axis=0, tiled=True)
        y_strips = (active_y[0] * framed[:, -1, :rows], active_y[1] * framed[:, -1, rows:])
        residual, adjoint = framed_stencil(framed, active, residual, adjoint, active_x, y_strips, faces)
    return (adjoint, residual)


def solution(mesh):
    in_specs = (
        P(None, "gy", "gx"),
        P(None, "gy", "gx"),
        P(None, "gy", "gx"),
        P(),
        P("gy"),
        P(),
        P(),
        P("gx"),
        P(),
        P(),
        P(),
    )
    out_specs = (P(None, "gy", "gx"), P(None, "gy", "gx"))
    return jax.shard_map(shards, mesh=mesh, in_specs=in_specs, out_specs=out_specs, check_vma=False)
```

```python
import jax
import jax.numpy as jnp
from jax import lax
from jax.experimental import pallas as pl
from jax.experimental.pallas import tpu as pltpu
from jax.sharding import PartitionSpec as P

ITERS = 2


storage_term = 0.2


def edge_pair(block, axis, dim):
    count = lax.axis_size(axis)
    forward = [(i, i + 1) for i in range(count - 1)]
    backward = [(target, source) for source, target in forward]
    last = lax.index_in_dim(block, block.shape[dim] - 1, axis=dim, keepdims=False)
    first = lax.index_in_dim(block, 0, axis=dim, keepdims=False)
    return lax.ppermute(last, axis, forward), lax.ppermute(first, axis, backward)


def edges(block):
    return [edge_pair(block, "gy", block.ndim - 2), edge_pair(block, "gx", block.ndim - 1)]


def harmonic(first, second):
    return 2.0 * first * second / (first + second)


def neighbours(center, strips):
    (x_low, x_high), (y_low, y_high) = strips
    zeros = jnp.zeros_like(center[:1])
    return [
        jnp.concatenate([center[1:], zeros], axis=0),
        jnp.concatenate([zeros, center[:-1]], axis=0),
        jnp.concatenate([center[:, 1:], x_high[:, None, :]], axis=1),
        jnp.concatenate([x_low[:, None, :], center[:, :-1]], axis=1),
        jnp.concatenate([center[:, :, 1:], y_high[:, :, None]], axis=2),
        jnp.concatenate([y_low[:, :, None], center[:, :, :-1]], axis=2),
    ]


def faces_from(center, strips):
    return [harmonic(center, other) for other in neighbours(center, strips)]


def framed_kernel(
    framed_ref, active_ref, residual_ref, adjoint_ref, x_low_ref, x_high_ref, y_low_ref, y_high_ref, *refs
):
    face_refs, residual_out, adjoint_out = refs[:-2], refs[-2], refs[-1]
    planes, rows, cols = active_ref.shape
    row = lax.broadcasted_iota(jnp.int32, (rows, cols), 0)
    col = lax.broadcasted_iota(jnp.int32, (rows, cols), 1)
    row_forward = pltpu.roll(row, 1, 0) == jnp.where(row == 0, rows - 1, row - 1)
    col_forward = pltpu.roll(col, 1, 1) == jnp.where(col == 0, cols - 1, col - 1)

    def before(plane, axis, count, forward):
        return jnp.where(forward, pltpu.roll(plane, 1, axis), pltpu.roll(plane, count - 1, axis))

    def after(plane, axis, count, forward):
        return jnp.where(forward, pltpu.roll(plane, count - 1, axis), pltpu.roll(plane, 1, axis))

    zeros = jnp.zeros((rows, cols), jnp.float32)
    updates = [framed_ref[z, pl.ds(1, rows), :] for z in range(planes)]
    masked = [active_ref[z] * updates[z] for z in range(planes)]
    for z in range(planes):
        center = masked[z]
        x_low = x_low_ref[pl.ds(z, 1), :] * framed_ref[z, pl.ds(0, 1), :]
        x_high = x_high_ref[pl.ds(z, 1), :] * framed_ref[z, pl.ds(rows + 1, 1), :]
        others = [
            masked[z + 1] if z + 1 < planes else zeros,
            masked[z - 1] if z > 0 else zeros,
            jnp.where(row == rows - 1, jnp.broadcast_to(x_high, (rows, cols)), after(center, 0, rows, row_forward)),
            jnp.where(row == 0, jnp.broadcast_to(x_low, (rows, cols)), before(center, 0, rows, row_forward)),
            jnp.where(col == cols - 1, y_high_ref[z], after(center, 1, cols, col_forward)),
            jnp.where(col == 0, y_low_ref[z], before(center, 1, cols, col_forward)),
        ]
        result = storage_term * center
        for face_ref, other in zip(face_refs, others):
            result = result + face_ref[z] * (center - other)
        update = updates[z]
        residual_out[z] = residual_ref[z] - (result + (1.0 - active_ref[z]) * update)
        adjoint_out[z] = adjoint_ref[z] + update


def framed_stencil(framed, active, residual, adjoint, x_strips, y_strips, faces):
    vmem = pl.BlockSpec(memory_space=pltpu.VMEM)
    shape = jax.ShapeDtypeStruct(active.shape, active.dtype)
    y_low, y_high = (jnp.broadcast_to(strip[:, :, None], active.shape) for strip in y_strips)
    return pl.pallas_call(
        framed_kernel,
        out_shape=(shape, shape),
        in_specs=[vmem] * (8 + len(faces)),
        out_specs=(vmem, vmem),
    )(framed, active, residual, adjoint, x_strips[0], x_strips[1], y_low, y_high, *faces)


def solve_kernel(diag_ref, coup_ref, shifts_ref, rhs_ref, out_ref, ratio_ref):
    count = rhs_ref.shape[0]
    shifts = shifts_ref[...]
    denom = diag_ref[0] + shifts
    ratio = -coup_ref[0] / denom
    ratio_ref[0] = ratio
    part = rhs_ref[0] / denom
    out_ref[0] = part
    for position in range(1, count):
        denom = diag_ref[position] + shifts + coup_ref[position - 1] * ratio
        if position < count - 1:
            ratio = -coup_ref[position] / denom
            ratio_ref[position] = ratio
        part = (rhs_ref[position] + coup_ref[position - 1] * part) / denom
        out_ref[position] = part
    solved = part
    for position in range(count - 2, -1, -1):
        solved = out_ref[position] - ratio_ref[position] * solved
        out_ref[position] = solved


def vertical_solve(rhs, diagonal, coupling, shifts):
    smem = pl.BlockSpec(memory_space=pltpu.SMEM)
    vmem = pl.BlockSpec(memory_space=pltpu.VMEM)
    return pl.pallas_call(
        solve_kernel,
        out_shape=jax.ShapeDtypeStruct(rhs.shape, rhs.dtype),
        in_specs=[smem, smem, vmem, vmem],
        out_specs=vmem,
        scratch_shapes=[pltpu.VMEM(rhs.shape, rhs.dtype)],
    )(diagonal, coupling, shifts, rhs)


def split_bf16(values):
    rounded = lax.reduce_precision(values, exponent_bits=8, mantissa_bits=7)
    return rounded.astype(jnp.bfloat16), (values - rounded).astype(jnp.bfloat16)


def transform(spec, data, basis):
    high, low = split_bf16(data)
    basis_high, basis_low = basis

    def product(first, second):
        return jnp.einsum(spec, first, second, preferred_element_type=jnp.float32)

    return product(high, basis_high) + (product(low, basis_high) + product(high, basis_low))


def shards(
    right_side,
    conduct,
    excavated,
    vectors_x,
    mass_x,
    values_x,
    vectors_y,
    mass_y,
    values_y,
    vertical_diag,
    vertical_coupling,
):
    active = excavated.astype(jnp.float32)
    both = edges(jnp.stack([conduct, active]))
    faces = faces_from(conduct, [(low[0], high[0]) for low, high in both])
    active_x, active_y = [(low[1], high[1]) for low, high in both]
    local_modes = vectors_x.shape[1] // (lax.axis_size("gx") * lax.axis_size("gy"))
    mode_start = (lax.axis_index("gx") * lax.axis_size("gy") + lax.axis_index("gy")) * local_modes
    local_values = lax.dynamic_slice_in_dim(values_x, mode_start, local_modes, 0)
    shifts = local_values[:, None] + values_y[None, :]
    adjoint = jnp.zeros_like(right_side)
    residual = right_side
    everyone = ("gx", "gy")
    blocks_y = lax.axis_size("gx")
    basis_x = split_bf16(vectors_x)
    rows = right_side.shape[1]
    framed_basis = []
    for piece in basis_x:
        blocks = piece.reshape(-1, rows, piece.shape[1])
        zero = jnp.zeros_like(blocks[:1, :1])
        below = jnp.concatenate([zero, blocks[:-1, -1:]], axis=0)
        above = jnp.concatenate([blocks[1:, :1], zero], axis=0)
        framed_basis.append(jnp.concatenate([below, blocks, above], axis=1))
    count_y = lax.axis_size("gx")
    forward_y = [(i, i + 1) for i in range(count_y - 1)]
    backward_y = [(target, source) for source, target in forward_y]
    basis_y = tuple(piece.reshape(blocks_y, -1, vectors_y.shape[1]) for piece in split_bf16(vectors_y))
    for iteration in range(ITERS):
        scaled = residual * mass_x[None, :, None] * mass_y[None, None, :]
        modes = transform(
            "zxy,xi->ziy",
            lax.all_to_all(scaled, "gy", split_axis=0, concat_axis=1, tiled=True),
            basis_x,
        )
        chunks = modes.reshape(-1, local_modes, modes.shape[2])
        chunks = lax.all_to_all(chunks, everyone, split_axis=0, concat_axis=0, tiled=True)
        chunks = chunks.reshape(blocks_y, -1, local_modes, chunks.shape[2])
        modes = transform("azil,alj->zij", chunks, basis_y)
        solved = vertical_solve(modes, vertical_diag, vertical_coupling, shifts)
        chunks = transform("zij,alj->azil", solved, basis_y)
        chunks = chunks.reshape(-1, local_modes, chunks.shape[3])
        chunks = lax.all_to_all(chunks, everyone, split_axis=0, concat_axis=0, tiled=True)
        solved = chunks.reshape(-1, chunks.shape[2])
        sides = jnp.concatenate([solved[:, :1], solved[:, -1:]], axis=1)
        sides = transform("iy,bri->bry", sides, framed_basis)
        from_left = lax.ppermute(sides[:, 1:-1, 1], "gx", forward_y)
        from_right = lax.ppermute(sides[:, 1:-1, 0], "gx", backward_y)
        framed = transform("iy,bri->bry", solved, framed_basis)
        halo_row = jnp.concatenate([from_left, from_right], axis=1)[:, None, :]
        framed = jnp.concatenate([framed, halo_row], axis=1)
        framed = lax.all_to_all(framed, "gy", split_axis=0, concat_axis=0, tiled=True)
        y_strips = (active_y[0] * framed[:, -1, :rows], active_y[1] * framed[:, -1, rows:])
        residual, adjoint = framed_stencil(framed, active, residual, adjoint, active_x, y_strips, faces)
    return (adjoint, residual)


def solution(mesh):
    in_specs = (
        P(None, "gy", "gx"),
        P(None, "gy", "gx"),
        P(None, "gy", "gx"),
        P(),
        P("gy"),
        P(),
        P(),
        P("gx"),
        P(),
        P(),
        P(),
    )
    out_specs = (P(None, "gy", "gx"), P(None, "gy", "gx"))
    return jax.shard_map(shards, mesh=mesh, in_specs=in_specs, out_specs=out_specs, check_vma=False)
```

```python
import jax
import jax.numpy as jnp
from jax import lax
from jax.experimental import pallas as pl
from jax.experimental.pallas import tpu as pltpu
from jax.sharding import PartitionSpec as P

ITERS = 2


storage_term = 0.2


def edge_pair(block, axis, dim):
    count = lax.axis_size(axis)
    forward = [(i, i + 1) for i in range(count - 1)]
    backward = [(target, source) for source, target in forward]
    last = lax.index_in_dim(block, block.shape[dim] - 1, axis=dim, keepdims=False)
    first = lax.index_in_dim(block, 0, axis=dim, keepdims=False)
    return lax.ppermute(last, axis, forward), lax.ppermute(first, axis, backward)


def edges(block):
    return [edge_pair(block, "gy", block.ndim - 2), edge_pair(block, "gx", block.ndim - 1)]


def harmonic(first, second):
    return 2.0 * first * second / (first + second)


def neighbours(center, strips):
    (x_low, x_high), (y_low, y_high) = strips
    zeros = jnp.zeros_like(center[:1])
    return [
        jnp.concatenate([center[1:], zeros], axis=0),
        jnp.concatenate([zeros, center[:-1]], axis=0),
        jnp.concatenate([center[:, 1:], x_high[:, None, :]], axis=1),
        jnp.concatenate([x_low[:, None, :], center[:, :-1]], axis=1),
        jnp.concatenate([center[:, :, 1:], y_high[:, :, None]], axis=2),
        jnp.concatenate([y_low[:, :, None], center[:, :, :-1]], axis=2),
    ]


def faces_from(center, strips):
    return [harmonic(center, other) for other in neighbours(center, strips)]


def framed_kernel(
    framed_ref, active_ref, residual_ref, adjoint_ref, x_low_ref, x_high_ref, y_low_ref, y_high_ref, *refs
):
    face_refs, residual_out, adjoint_out = refs[:-2], refs[-2], refs[-1]
    planes, rows, cols = active_ref.shape
    row = lax.broadcasted_iota(jnp.int32, (rows, cols), 0)
    col = lax.broadcasted_iota(jnp.int32, (rows, cols), 1)
    row_forward = pltpu.roll(row, 1, 0) == jnp.where(row == 0, rows - 1, row - 1)
    col_forward = pltpu.roll(col, 1, 1) == jnp.where(col == 0, cols - 1, col - 1)

    def before(plane, axis, count, forward):
        return jnp.where(forward, pltpu.roll(plane, 1, axis), pltpu.roll(plane, count - 1, axis))

    def after(plane, axis, count, forward):
        return jnp.where(forward, pltpu.roll(plane, count - 1, axis), pltpu.roll(plane, 1, axis))

    zeros = jnp.zeros((rows, cols), jnp.float32)
    updates = [framed_ref[z, pl.ds(1, rows), :] for z in range(planes)]
    masked = [active_ref[z] * updates[z] for z in range(planes)]
    for z in range(planes):
        center = masked[z]
        x_low = x_low_ref[pl.ds(z, 1), :] * framed_ref[z, pl.ds(0, 1), :]
        x_high = x_high_ref[pl.ds(z, 1), :] * framed_ref[z, pl.ds(rows + 1, 1), :]
        others = [
            masked[z + 1] if z + 1 < planes else zeros,
            masked[z - 1] if z > 0 else zeros,
            jnp.where(row == rows - 1, jnp.broadcast_to(x_high, (rows, cols)), after(center, 0, rows, row_forward)),
            jnp.where(row == 0, jnp.broadcast_to(x_low, (rows, cols)), before(center, 0, rows, row_forward)),
            jnp.where(col == cols - 1, y_high_ref[z], after(center, 1, cols, col_forward)),
            jnp.where(col == 0, y_low_ref[z], before(center, 1, cols, col_forward)),
        ]
        result = storage_term * center
        for face_ref, other in zip(face_refs, others):
            result = result + face_ref[z] * (center - other)
        update = updates[z]
        residual_out[z] = residual_ref[z] - (result + (1.0 - active_ref[z]) * update)
        adjoint_out[z] = adjoint_ref[z] + update


def framed_stencil(framed, active, residual, adjoint, x_strips, y_strips, faces):
    vmem = pl.BlockSpec(memory_space=pltpu.VMEM)
    shape = jax.ShapeDtypeStruct(active.shape, active.dtype)
    y_low, y_high = (jnp.broadcast_to(strip[:, :, None], active.shape) for strip in y_strips)
    return pl.pallas_call(
        framed_kernel,
        out_shape=(shape, shape),
        in_specs=[vmem] * (8 + len(faces)),
        out_specs=(vmem, vmem),
    )(framed, active, residual, adjoint, x_strips[0], x_strips[1], y_low, y_high, *faces)


def solve_kernel(diag_ref, coup_ref, shifts_ref, rhs_ref, out_ref, ratio_ref):
    count = rhs_ref.shape[0]
    shifts = shifts_ref[...]
    denom = diag_ref[0] + shifts
    ratio = -coup_ref[0] / denom
    ratio_ref[0] = ratio
    part = rhs_ref[0] / denom
    out_ref[0] = part
    for position in range(1, count):
        denom = diag_ref[position] + shifts + coup_ref[position - 1] * ratio
        if position < count - 1:
            ratio = -coup_ref[position] / denom
            ratio_ref[position] = ratio
        part = (rhs_ref[position] + coup_ref[position - 1] * part) / denom
        out_ref[position] = part
    solved = part
    for position in range(count - 2, -1, -1):
        solved = out_ref[position] - ratio_ref[position] * solved
        out_ref[position] = solved


def vertical_solve(rhs, diagonal, coupling, shifts):
    smem = pl.BlockSpec(memory_space=pltpu.SMEM)
    vmem = pl.BlockSpec(memory_space=pltpu.VMEM)
    return pl.pallas_call(
        solve_kernel,
        out_shape=jax.ShapeDtypeStruct(rhs.shape, rhs.dtype),
        in_specs=[smem, smem, vmem, vmem],
        out_specs=vmem,
        scratch_shapes=[pltpu.VMEM(rhs.shape, rhs.dtype)],
    )(diagonal, coupling, shifts, rhs)


def split_bf16(values):
    rounded = lax.reduce_precision(values, exponent_bits=8, mantissa_bits=7)
    return rounded.astype(jnp.bfloat16), (values - rounded).astype(jnp.bfloat16)


def transform(spec, data, basis):
    high, low = split_bf16(data)
    basis_high, basis_low = basis

    def product(first, second):
        return jnp.einsum(spec, first, second, preferred_element_type=jnp.float32)

    return product(high, basis_high) + (product(low, basis_high) + product(high, basis_low))


def shards(
    right_side,
    conduct,
    excavated,
    vectors_x,
    mass_x,
    values_x,
    vectors_y,
    mass_y,
    values_y,
    vertical_diag,
    vertical_coupling,
):
    active = excavated.astype(jnp.float32)
    both = edges(jnp.stack([conduct, active]))
    faces = faces_from(conduct, [(low[0], high[0]) for low, high in both])
    active_x, active_y = [(low[1], high[1]) for low, high in both]
    local_modes = vectors_x.shape[1] // (lax.axis_size("gx") * lax.axis_size("gy"))
    mode_start = (lax.axis_index("gx") * lax.axis_size("gy") + lax.axis_index("gy")) * local_modes
    local_values = lax.dynamic_slice_in_dim(values_x, mode_start, local_modes, 0)
    shifts = local_values[:, None] + values_y[None, :]
    adjoint = jnp.zeros_like(right_side)
    residual = right_side
    everyone = ("gx", "gy")
    blocks_y = lax.axis_size("gx")
    basis_x = split_bf16(vectors_x)
    rows = right_side.shape[1]
    count_y = lax.axis_size("gx")
    forward_y = [(i, i + 1) for i in range(count_y - 1)]
    backward_y = [(target, source) for source, target in forward_y]
    basis_y = tuple(piece.reshape(blocks_y, -1, vectors_y.shape[1]) for piece in split_bf16(vectors_y))
    for iteration in range(ITERS):
        scaled = residual * mass_x[None, :, None] * mass_y[None, None, :]
        modes = transform(
            "zxy,xi->ziy",
            lax.all_to_all(scaled, "gy", split_axis=0, concat_axis=1, tiled=True),
            basis_x,
        )
        chunks = modes.reshape(-1, local_modes, modes.shape[2])
        chunks = lax.all_to_all(chunks, everyone, split_axis=0, concat_axis=0, tiled=True)
        chunks = chunks.reshape(blocks_y, -1, local_modes, chunks.shape[2])
        modes = transform("azil,alj->zij", chunks, basis_y)
        solved = vertical_solve(modes, vertical_diag, vertical_coupling, shifts)
        chunks = transform("zij,alj->azil", solved, basis_y)
        chunks = chunks.reshape(-1, local_modes, chunks.shape[3])
        chunks = lax.all_to_all(chunks, everyone, split_axis=0, concat_axis=0, tiled=True)
        solved = chunks.reshape(-1, chunks.shape[2])
        plane = transform("iy,xi->xy", solved, basis_x)
        blocks = plane.reshape(-1, rows, plane.shape[1])
        from_left = lax.ppermute(blocks[:, :, -1], "gx", forward_y)
        from_right = lax.ppermute(blocks[:, :, 0], "gx", backward_y)
        zero = jnp.zeros_like(blocks[:1, :1])
        below = jnp.concatenate([zero, blocks[:-1, -1:]], axis=0)
        above = jnp.concatenate([blocks[1:, :1], zero], axis=0)
        halo_row = jnp.concatenate([from_left, from_right], axis=1)[:, None, :]
        framed = jnp.concatenate([below, blocks, above, halo_row], axis=1)
        framed = lax.all_to_all(framed, "gy", split_axis=0, concat_axis=0, tiled=True)
        y_strips = (active_y[0] * framed[:, -1, :rows], active_y[1] * framed[:, -1, rows:])
        residual, adjoint = framed_stencil(framed, active, residual, adjoint, active_x, y_strips, faces)
    return (adjoint, residual)


def solution(mesh):
    in_specs = (
        P(None, "gy", "gx"),
        P(None, "gy", "gx"),
        P(None, "gy", "gx"),
        P(),
        P("gy"),
        P(),
        P(),
        P("gx"),
        P(),
        P(),
        P(),
    )
    out_specs = (P(None, "gy", "gx"), P(None, "gy", "gx"))
    return jax.shard_map(shards, mesh=mesh, in_specs=in_specs, out_specs=out_specs, check_vma=False)
```

```python
import jax
import jax.numpy as jnp
from jax import lax
from jax.experimental import pallas as pl
from jax.experimental.pallas import tpu as pltpu
from jax.sharding import PartitionSpec as P

ITERS = 2


storage_term = 0.2


def edge_pair(block, axis, dim):
    count = lax.axis_size(axis)
    forward = [(i, i + 1) for i in range(count - 1)]
    backward = [(target, source) for source, target in forward]
    last = lax.index_in_dim(block, block.shape[dim] - 1, axis=dim, keepdims=False)
    first = lax.index_in_dim(block, 0, axis=dim, keepdims=False)
    return lax.ppermute(last, axis, forward), lax.ppermute(first, axis, backward)


def edges(block):
    return [edge_pair(block, "gy", block.ndim - 2), edge_pair(block, "gx", block.ndim - 1)]


def harmonic(first, second):
    return 2.0 * first * second / (first + second)


def neighbours(center, strips):
    (x_low, x_high), (y_low, y_high) = strips
    zeros = jnp.zeros_like(center[:1])
    return [
        jnp.concatenate([center[1:], zeros], axis=0),
        jnp.concatenate([zeros, center[:-1]], axis=0),
        jnp.concatenate([center[:, 1:], x_high[:, None, :]], axis=1),
        jnp.concatenate([x_low[:, None, :], center[:, :-1]], axis=1),
        jnp.concatenate([center[:, :, 1:], y_high[:, :, None]], axis=2),
        jnp.concatenate([y_low[:, :, None], center[:, :, :-1]], axis=2),
    ]


def faces_from(center, strips):
    return [harmonic(center, other) for other in neighbours(center, strips)]


def framed_kernel(framed_ref, active_ref, residual_ref, *refs):
    if len(refs) == 12:
        adjoint_ref = None
    else:
        adjoint_ref, refs = refs[0], refs[1:]
    x_low_ref, x_high_ref, y_low_ref, y_high_ref = refs[:4]
    face_refs, residual_out, adjoint_out = refs[4:-2], refs[-2], refs[-1]
    planes, rows, cols = active_ref.shape
    row = lax.broadcasted_iota(jnp.int32, (rows, cols), 0)
    col = lax.broadcasted_iota(jnp.int32, (rows, cols), 1)
    row_forward = pltpu.roll(row, 1, 0) == jnp.where(row == 0, rows - 1, row - 1)
    col_forward = pltpu.roll(col, 1, 1) == jnp.where(col == 0, cols - 1, col - 1)

    def before(plane, axis, count, forward):
        return jnp.where(forward, pltpu.roll(plane, 1, axis), pltpu.roll(plane, count - 1, axis))

    def after(plane, axis, count, forward):
        return jnp.where(forward, pltpu.roll(plane, count - 1, axis), pltpu.roll(plane, 1, axis))

    zeros = jnp.zeros((rows, cols), jnp.float32)
    updates = [framed_ref[z, pl.ds(1, rows), :] for z in range(planes)]
    masked = [active_ref[z] * updates[z] for z in range(planes)]
    for z in range(planes):
        center = masked[z]
        x_low = x_low_ref[pl.ds(z, 1), :] * framed_ref[z, pl.ds(0, 1), :]
        x_high = x_high_ref[pl.ds(z, 1), :] * framed_ref[z, pl.ds(rows + 1, 1), :]
        others = [
            masked[z + 1] if z + 1 < planes else zeros,
            masked[z - 1] if z > 0 else zeros,
            jnp.where(row == rows - 1, jnp.broadcast_to(x_high, (rows, cols)), after(center, 0, rows, row_forward)),
            jnp.where(row == 0, jnp.broadcast_to(x_low, (rows, cols)), before(center, 0, rows, row_forward)),
            jnp.where(col == cols - 1, y_high_ref[z], after(center, 1, cols, col_forward)),
            jnp.where(col == 0, y_low_ref[z], before(center, 1, cols, col_forward)),
        ]
        result = storage_term * center
        for face_ref, other in zip(face_refs, others):
            result = result + face_ref[z] * (center - other)
        update = updates[z]
        residual_out[z] = residual_ref[z] - (result + (1.0 - active_ref[z]) * update)
        adjoint_out[z] = update if adjoint_ref is None else adjoint_ref[z] + update


def framed_stencil(framed, active, residual, adjoint, x_strips, y_strips, faces):
    vmem = pl.BlockSpec(memory_space=pltpu.VMEM)
    shape = jax.ShapeDtypeStruct(active.shape, active.dtype)
    y_low, y_high = (jnp.broadcast_to(strip[:, :, None], active.shape) for strip in y_strips)
    carried = [] if adjoint is None else [adjoint]
    operands = [framed, active, residual, *carried, x_strips[0], x_strips[1], y_low, y_high, *faces]
    return pl.pallas_call(
        framed_kernel,
        out_shape=(shape, shape),
        in_specs=[vmem] * len(operands),
        out_specs=(vmem, vmem),
    )(*operands)


def solve_kernel(diag_ref, coup_ref, shifts_ref, rhs_ref, out_ref, ratio_ref):
    count = rhs_ref.shape[0]
    shifts = shifts_ref[...]
    denom = diag_ref[0] + shifts
    ratio = -coup_ref[0] / denom
    ratio_ref[0] = ratio
    part = rhs_ref[0] / denom
    out_ref[0] = part
    for position in range(1, count):
        denom = diag_ref[position] + shifts + coup_ref[position - 1] * ratio
        if position < count - 1:
            ratio = -coup_ref[position] / denom
            ratio_ref[position] = ratio
        part = (rhs_ref[position] + coup_ref[position - 1] * part) / denom
        out_ref[position] = part
    solved = part
    for position in range(count - 2, -1, -1):
        solved = out_ref[position] - ratio_ref[position] * solved
        out_ref[position] = solved


def vertical_solve(rhs, diagonal, coupling, shifts):
    smem = pl.BlockSpec(memory_space=pltpu.SMEM)
    vmem = pl.BlockSpec(memory_space=pltpu.VMEM)
    return pl.pallas_call(
        solve_kernel,
        out_shape=jax.ShapeDtypeStruct(rhs.shape, rhs.dtype),
        in_specs=[smem, smem, vmem, vmem],
        out_specs=vmem,
        scratch_shapes=[pltpu.VMEM(rhs.shape, rhs.dtype)],
    )(diagonal, coupling, shifts, rhs)


def split_bf16(values):
    rounded = lax.reduce_precision(values, exponent_bits=8, mantissa_bits=7)
    return rounded.astype(jnp.bfloat16), (values - rounded).astype(jnp.bfloat16)


def transform(spec, data, basis):
    high, low = split_bf16(data)
    basis_high, basis_low = basis

    def product(first, second):
        return jnp.einsum(spec, first, second, preferred_element_type=jnp.float32)

    return product(high, basis_high) + (product(low, basis_high) + product(high, basis_low))


def shards(
    right_side,
    conduct,
    excavated,
    vectors_x,
    mass_x,
    values_x,
    vectors_y,
    mass_y,
    values_y,
    vertical_diag,
    vertical_coupling,
):
    active = excavated.astype(jnp.float32)
    both = edges(jnp.stack([conduct, active]))
    faces = faces_from(conduct, [(low[0], high[0]) for low, high in both])
    active_x, active_y = [(low[1], high[1]) for low, high in both]
    local_modes = vectors_x.shape[1] // (lax.axis_size("gx") * lax.axis_size("gy"))
    mode_start = (lax.axis_index("gx") * lax.axis_size("gy") + lax.axis_index("gy")) * local_modes
    local_values = lax.dynamic_slice_in_dim(values_x, mode_start, local_modes, 0)
    shifts = local_values[:, None] + values_y[None, :]
    adjoint = None
    residual = right_side
    everyone = ("gx", "gy")
    blocks_y = lax.axis_size("gx")
    basis_x = split_bf16(vectors_x)
    rows = right_side.shape[1]
    count_y = lax.axis_size("gx")
    forward_y = [(i, i + 1) for i in range(count_y - 1)]
    backward_y = [(target, source) for source, target in forward_y]
    basis_y = tuple(piece.reshape(blocks_y, -1, vectors_y.shape[1]) for piece in split_bf16(vectors_y))
    for iteration in range(ITERS):
        scaled = residual * mass_x[None, :, None] * mass_y[None, None, :]
        modes = transform(
            "zxy,xi->ziy",
            lax.all_to_all(scaled, "gy", split_axis=0, concat_axis=1, tiled=True),
            basis_x,
        )
        chunks = modes.reshape(-1, local_modes, modes.shape[2])
        chunks = lax.all_to_all(chunks, everyone, split_axis=0, concat_axis=0, tiled=True)
        chunks = chunks.reshape(blocks_y, -1, local_modes, chunks.shape[2])
        modes = transform("azil,alj->zij", chunks, basis_y)
        solved = vertical_solve(modes, vertical_diag, vertical_coupling, shifts)
        chunks = transform("zij,alj->azil", solved, basis_y)
        chunks = chunks.reshape(-1, local_modes, chunks.shape[3])
        chunks = lax.all_to_all(chunks, everyone, split_axis=0, concat_axis=0, tiled=True)
        solved = chunks.reshape(-1, chunks.shape[2])
        plane = transform("iy,xi->xy", solved, basis_x)
        blocks = plane.reshape(-1, rows, plane.shape[1])
        from_left = lax.ppermute(blocks[:, :, -1], "gx", forward_y)
        from_right = lax.ppermute(blocks[:, :, 0], "gx", backward_y)
        zero = jnp.zeros_like(blocks[:1, :1])
        below = jnp.concatenate([zero, blocks[:-1, -1:]], axis=0)
        above = jnp.concatenate([blocks[1:, :1], zero], axis=0)
        halo_row = jnp.concatenate([from_left, from_right], axis=1)[:, None, :]
        framed = jnp.concatenate([below, blocks, above, halo_row], axis=1)
        framed = lax.all_to_all(framed, "gy", split_axis=0, concat_axis=0, tiled=True)
        y_strips = (active_y[0] * framed[:, -1, :rows], active_y[1] * framed[:, -1, rows:])
        residual, adjoint = framed_stencil(framed, active, residual, adjoint, active_x, y_strips, faces)
    return (adjoint, residual)


def solution(mesh):
    in_specs = (
        P(None, "gy", "gx"),
        P(None, "gy", "gx"),
        P(None, "gy", "gx"),
        P(),
        P("gy"),
        P(),
        P(),
        P("gx"),
        P(),
        P(),
        P(),
    )
    out_specs = (P(None, "gy", "gx"), P(None, "gy", "gx"))
    return jax.shard_map(shards, mesh=mesh, in_specs=in_specs, out_specs=out_specs, check_vma=False)
```

```python
import jax
import jax.numpy as jnp
from jax import lax
from jax.experimental import pallas as pl
from jax.experimental.pallas import tpu as pltpu
from jax.sharding import PartitionSpec as P

ITERS = 2


storage_term = 0.2


def edge_pair(block, axis, dim):
    count = lax.axis_size(axis)
    forward = [(i, i + 1) for i in range(count - 1)]
    backward = [(target, source) for source, target in forward]
    last = lax.index_in_dim(block, block.shape[dim] - 1, axis=dim, keepdims=False)
    first = lax.index_in_dim(block, 0, axis=dim, keepdims=False)
    return lax.ppermute(last, axis, forward), lax.ppermute(first, axis, backward)


def edges(block):
    return [edge_pair(block, "gy", block.ndim - 2), edge_pair(block, "gx", block.ndim - 1)]


def harmonic(first, second):
    return 2.0 * first * second / (first + second)


def neighbours(center, strips):
    (x_low, x_high), (y_low, y_high) = strips
    zeros = jnp.zeros_like(center[:1])
    return [
        jnp.concatenate([center[1:], zeros], axis=0),
        jnp.concatenate([zeros, center[:-1]], axis=0),
        jnp.concatenate([center[:, 1:], x_high[:, None, :]], axis=1),
        jnp.concatenate([x_low[:, None, :], center[:, :-1]], axis=1),
        jnp.concatenate([center[:, :, 1:], y_high[:, :, None]], axis=2),
        jnp.concatenate([y_low[:, :, None], center[:, :, :-1]], axis=2),
    ]


def faces_from(center, strips):
    return [harmonic(center, other) for other in neighbours(center, strips)]


def framed_kernel(framed_ref, active_ref, residual_ref, *refs):
    if len(refs) == 12:
        adjoint_ref = None
    else:
        adjoint_ref, refs = refs[0], refs[1:]
    x_low_ref, x_high_ref, y_low_ref, y_high_ref = refs[:4]
    face_refs, residual_out, adjoint_out = refs[4:-2], refs[-2], refs[-1]
    planes, rows, cols = active_ref.shape
    row = lax.broadcasted_iota(jnp.int32, (rows, cols), 0)
    col = lax.broadcasted_iota(jnp.int32, (rows, cols), 1)
    row_forward = pltpu.roll(row, 1, 0) == jnp.where(row == 0, rows - 1, row - 1)
    col_forward = pltpu.roll(col, 1, 1) == jnp.where(col == 0, cols - 1, col - 1)

    def before(plane, axis, count, forward):
        return jnp.where(forward, pltpu.roll(plane, 1, axis), pltpu.roll(plane, count - 1, axis))

    def after(plane, axis, count, forward):
        return jnp.where(forward, pltpu.roll(plane, count - 1, axis), pltpu.roll(plane, 1, axis))

    zeros = jnp.zeros((rows, cols), jnp.float32)
    updates = [framed_ref[z, pl.ds(1, rows), :] for z in range(planes)]
    masked = [active_ref[z] * updates[z] for z in range(planes)]
    for z in range(planes):
        center = masked[z]
        x_low = x_low_ref[pl.ds(z, 1), :] * framed_ref[z, pl.ds(0, 1), :]
        x_high = x_high_ref[pl.ds(z, 1), :] * framed_ref[z, pl.ds(rows + 1, 1), :]
        others = [
            masked[z + 1] if z + 1 < planes else zeros,
            masked[z - 1] if z > 0 else zeros,
            jnp.where(row == rows - 1, jnp.broadcast_to(x_high, (rows, cols)), after(center, 0, rows, row_forward)),
            jnp.where(row == 0, jnp.broadcast_to(x_low, (rows, cols)), before(center, 0, rows, row_forward)),
            jnp.where(col == cols - 1, y_high_ref[z], after(center, 1, cols, col_forward)),
            jnp.where(col == 0, y_low_ref[z], before(center, 1, cols, col_forward)),
        ]
        result = storage_term * center
        for face_ref, other in zip(face_refs, others):
            result = result + face_ref[z] * (center - other)
        update = updates[z]
        residual_out[z] = residual_ref[z] - (result + (1.0 - active_ref[z]) * update)
        adjoint_out[z] = update if adjoint_ref is None else adjoint_ref[z] + update


def framed_stencil(framed, active, residual, adjoint, x_strips, y_strips, faces):
    vmem = pl.BlockSpec(memory_space=pltpu.VMEM)
    shape = jax.ShapeDtypeStruct(active.shape, active.dtype)
    y_low, y_high = (jnp.broadcast_to(strip[:, :, None], active.shape) for strip in y_strips)
    carried = [] if adjoint is None else [adjoint]
    operands = [framed, active, residual, *carried, x_strips[0], x_strips[1], y_low, y_high, *faces]
    return pl.pallas_call(
        framed_kernel,
        out_shape=(shape, shape),
        in_specs=[vmem] * len(operands),
        out_specs=(vmem, vmem),
    )(*operands)


def solve_kernel(diag_ref, coup_ref, shifts_ref, rhs_ref, out_ref, ratio_ref):
    count = rhs_ref.shape[0]
    shifts = shifts_ref[...]
    denom = diag_ref[0] + shifts
    ratio = -coup_ref[0] / denom
    ratio_ref[0] = ratio
    part = rhs_ref[0] / denom
    out_ref[0] = part
    for position in range(1, count):
        denom = diag_ref[position] + shifts + coup_ref[position - 1] * ratio
        if position < count - 1:
            ratio = -coup_ref[position] / denom
            ratio_ref[position] = ratio
        part = (rhs_ref[position] + coup_ref[position - 1] * part) / denom
        out_ref[position] = part
    solved = part
    for position in range(count - 2, -1, -1):
        solved = out_ref[position] - ratio_ref[position] * solved
        out_ref[position] = solved


def vertical_solve(rhs, diagonal, coupling, shifts):
    smem = pl.BlockSpec(memory_space=pltpu.SMEM)
    vmem = pl.BlockSpec(memory_space=pltpu.VMEM)
    return pl.pallas_call(
        solve_kernel,
        out_shape=jax.ShapeDtypeStruct(rhs.shape, rhs.dtype),
        in_specs=[smem, smem, vmem, vmem],
        out_specs=vmem,
        scratch_shapes=[pltpu.VMEM(rhs.shape, rhs.dtype)],
    )(diagonal, coupling, shifts, rhs)


def split_bf16(values):
    rounded = lax.reduce_precision(values, exponent_bits=8, mantissa_bits=7)
    return rounded.astype(jnp.bfloat16), (values - rounded).astype(jnp.bfloat16)


def transform(spec, data, basis):
    high, low = split_bf16(data)
    basis_high, basis_low = basis

    def product(first, second):
        return jnp.einsum(spec, first, second, preferred_element_type=jnp.float32)

    return product(high, basis_high) + (product(low, basis_high) + product(high, basis_low))


def shards(
    right_side,
    conduct,
    excavated,
    vectors_x,
    mass_x,
    values_x,
    vectors_y,
    mass_y,
    values_y,
    vertical_diag,
    vertical_coupling,
):
    active = excavated.astype(jnp.float32)
    both = edges(jnp.stack([conduct, active]))
    faces = faces_from(conduct, [(low[0], high[0]) for low, high in both])
    active_x, active_y = [(low[1], high[1]) for low, high in both]
    local_modes = vectors_x.shape[1] // (lax.axis_size("gx") * lax.axis_size("gy"))
    mode_start = (lax.axis_index("gx") * lax.axis_size("gy") + lax.axis_index("gy")) * local_modes
    local_values = lax.dynamic_slice_in_dim(values_x, mode_start, local_modes, 0)
    shifts = local_values[:, None] + values_y[None, :]
    adjoint = None
    residual = right_side
    everyone = ("gx", "gy")
    blocks_y = lax.axis_size("gx")
    basis_x = split_bf16(vectors_x)
    rows = right_side.shape[1]
    count_y = lax.axis_size("gx")
    block_y = lax.axis_index("gx")
    forward_y = [(i, i + 1) for i in range(count_y - 1)]
    backward_y = [(target, source) for source, target in forward_y]
    basis_y = tuple(piece.reshape(blocks_y, -1, vectors_y.shape[1]) for piece in split_bf16(vectors_y))
    for iteration in range(ITERS):
        scaled = residual * mass_x[None, :, None] * mass_y[None, None, :]
        modes = transform(
            "zxy,xi->ziy",
            lax.all_to_all(scaled, "gy", split_axis=0, concat_axis=1, tiled=True),
            basis_x,
        )
        chunks = modes.reshape(-1, local_modes, modes.shape[2])
        chunks = lax.all_to_all(chunks, everyone, split_axis=0, concat_axis=0, tiled=True)
        chunks = chunks.reshape(blocks_y, -1, local_modes, chunks.shape[2])
        modes = transform("azil,alj->zij", chunks, basis_y)
        solved = vertical_solve(modes, vertical_diag, vertical_coupling, shifts)
        chunks = transform("zij,alj->azil", solved, basis_y)
        chunks = chunks.reshape(-1, local_modes, chunks.shape[3])
        chunks = lax.all_to_all(chunks, everyone, split_axis=0, concat_axis=0, tiled=True)
        solved = chunks.reshape(-1, chunks.shape[2])
        plane = transform("iy,xi->xy", solved, basis_x)
        blocks = plane.reshape(-1, rows, plane.shape[1])
        gathered = lax.all_gather(jnp.concatenate([blocks[:, :, 0], blocks[:, :, -1]], axis=1), "gx")
        from_left = lax.dynamic_index_in_dim(gathered, jnp.maximum(block_y - 1, 0), keepdims=False)[:, rows:]
        from_left = jnp.where(block_y > 0, from_left, 0.0)
        from_right = lax.dynamic_index_in_dim(gathered, jnp.minimum(block_y + 1, count_y - 1), keepdims=False)
        from_right = jnp.where(block_y < count_y - 1, from_right[:, :rows], 0.0)
        zero = jnp.zeros_like(blocks[:1, :1])
        below = jnp.concatenate([zero, blocks[:-1, -1:]], axis=0)
        above = jnp.concatenate([blocks[1:, :1], zero], axis=0)
        halo_row = jnp.concatenate([from_left, from_right], axis=1)[:, None, :]
        framed = jnp.concatenate([below, blocks, above, halo_row], axis=1)
        framed = lax.all_to_all(framed, "gy", split_axis=0, concat_axis=0, tiled=True)
        y_strips = (active_y[0] * framed[:, -1, :rows], active_y[1] * framed[:, -1, rows:])
        residual, adjoint = framed_stencil(framed, active, residual, adjoint, active_x, y_strips, faces)
    return (adjoint, residual)


def solution(mesh):
    in_specs = (
        P(None, "gy", "gx"),
        P(None, "gy", "gx"),
        P(None, "gy", "gx"),
        P(),
        P("gy"),
        P(),
        P(),
        P("gx"),
        P(),
        P(),
        P(),
    )
    out_specs = (P(None, "gy", "gx"), P(None, "gy", "gx"))
    return jax.shard_map(shards, mesh=mesh, in_specs=in_specs, out_specs=out_specs, check_vma=False)
```

```python
import jax
import jax.numpy as jnp
from jax import lax
from jax.experimental import pallas as pl
from jax.experimental.pallas import tpu as pltpu
from jax.sharding import PartitionSpec as P

ITERS = 2


storage_term = 0.2


def edge_pair(block, axis, dim):
    count = lax.axis_size(axis)
    forward = [(i, i + 1) for i in range(count - 1)]
    backward = [(target, source) for source, target in forward]
    last = lax.index_in_dim(block, block.shape[dim] - 1, axis=dim, keepdims=False)
    first = lax.index_in_dim(block, 0, axis=dim, keepdims=False)
    return lax.ppermute(last, axis, forward), lax.ppermute(first, axis, backward)


def edges(block):
    return [edge_pair(block, "gy", block.ndim - 2), edge_pair(block, "gx", block.ndim - 1)]


def harmonic(first, second):
    return 2.0 * first * second / (first + second)


def neighbours(center, strips):
    (x_low, x_high), (y_low, y_high) = strips
    zeros = jnp.zeros_like(center[:1])
    return [
        jnp.concatenate([center[1:], zeros], axis=0),
        jnp.concatenate([zeros, center[:-1]], axis=0),
        jnp.concatenate([center[:, 1:], x_high[:, None, :]], axis=1),
        jnp.concatenate([x_low[:, None, :], center[:, :-1]], axis=1),
        jnp.concatenate([center[:, :, 1:], y_high[:, :, None]], axis=2),
        jnp.concatenate([y_low[:, :, None], center[:, :, :-1]], axis=2),
    ]


def faces_from(center, strips):
    return [harmonic(center, other) for other in neighbours(center, strips)]


def framed_kernel(framed_ref, active_ref, residual_ref, *refs):
    if len(refs) == 11:
        adjoint_ref = None
    else:
        adjoint_ref, refs = refs[0], refs[1:]
    x_low_ref, x_high_ref, y_active_ref = refs[:3]
    face_refs, residual_out, adjoint_out = refs[3:-2], refs[-2], refs[-1]
    planes, rows, cols = active_ref.shape
    halo_rows = jnp.concatenate([framed_ref[z, pl.ds(rows + 2, 1), :] for z in range(planes)], axis=0)
    halo_columns = jnp.transpose(halo_rows * y_active_ref[...])
    row = lax.broadcasted_iota(jnp.int32, (rows, cols), 0)
    col = lax.broadcasted_iota(jnp.int32, (rows, cols), 1)
    row_forward = pltpu.roll(row, 1, 0) == jnp.where(row == 0, rows - 1, row - 1)
    col_forward = pltpu.roll(col, 1, 1) == jnp.where(col == 0, cols - 1, col - 1)

    def before(plane, axis, count, forward):
        return jnp.where(forward, pltpu.roll(plane, 1, axis), pltpu.roll(plane, count - 1, axis))

    def after(plane, axis, count, forward):
        return jnp.where(forward, pltpu.roll(plane, count - 1, axis), pltpu.roll(plane, 1, axis))

    zeros = jnp.zeros((rows, cols), jnp.float32)
    updates = [framed_ref[z, pl.ds(1, rows), :] for z in range(planes)]
    masked = [active_ref[z] * updates[z] for z in range(planes)]
    for z in range(planes):
        center = masked[z]
        x_low = x_low_ref[pl.ds(z, 1), :] * framed_ref[z, pl.ds(0, 1), :]
        x_high = x_high_ref[pl.ds(z, 1), :] * framed_ref[z, pl.ds(rows + 1, 1), :]
        others = [
            masked[z + 1] if z + 1 < planes else zeros,
            masked[z - 1] if z > 0 else zeros,
            jnp.where(row == rows - 1, jnp.broadcast_to(x_high, (rows, cols)), after(center, 0, rows, row_forward)),
            jnp.where(row == 0, jnp.broadcast_to(x_low, (rows, cols)), before(center, 0, rows, row_forward)),
            jnp.where(
                col == cols - 1,
                jnp.broadcast_to(halo_columns[rows:, z : z + 1], (rows, cols)),
                after(center, 1, cols, col_forward),
            ),
            jnp.where(
                col == 0, jnp.broadcast_to(halo_columns[:rows, z : z + 1], (rows, cols)), before(center, 1, cols, col_forward)
            ),
        ]
        result = storage_term * center
        for face_ref, other in zip(face_refs, others):
            result = result + face_ref[z] * (center - other)
        update = updates[z]
        residual_out[z] = residual_ref[z] - (result + (1.0 - active_ref[z]) * update)
        adjoint_out[z] = update if adjoint_ref is None else adjoint_ref[z] + update


def framed_stencil(framed, active, residual, adjoint, x_strips, y_active, faces):
    vmem = pl.BlockSpec(memory_space=pltpu.VMEM)
    shape = jax.ShapeDtypeStruct(active.shape, active.dtype)
    carried = [] if adjoint is None else [adjoint]
    operands = [framed, active, residual, *carried, x_strips[0], x_strips[1], y_active, *faces]
    return pl.pallas_call(
        framed_kernel,
        out_shape=(shape, shape),
        in_specs=[vmem] * len(operands),
        out_specs=(vmem, vmem),
    )(*operands)


def solve_kernel(diag_ref, coup_ref, shifts_ref, rhs_ref, out_ref, ratio_ref):
    count = rhs_ref.shape[0]
    shifts = shifts_ref[...]
    denom = diag_ref[0] + shifts
    ratio = -coup_ref[0] / denom
    ratio_ref[0] = ratio
    part = rhs_ref[0] / denom
    out_ref[0] = part
    for position in range(1, count):
        denom = diag_ref[position] + shifts + coup_ref[position - 1] * ratio
        if position < count - 1:
            ratio = -coup_ref[position] / denom
            ratio_ref[position] = ratio
        part = (rhs_ref[position] + coup_ref[position - 1] * part) / denom
        out_ref[position] = part
    solved = part
    for position in range(count - 2, -1, -1):
        solved = out_ref[position] - ratio_ref[position] * solved
        out_ref[position] = solved


def vertical_solve(rhs, diagonal, coupling, shifts):
    smem = pl.BlockSpec(memory_space=pltpu.SMEM)
    vmem = pl.BlockSpec(memory_space=pltpu.VMEM)
    return pl.pallas_call(
        solve_kernel,
        out_shape=jax.ShapeDtypeStruct(rhs.shape, rhs.dtype),
        in_specs=[smem, smem, vmem, vmem],
        out_specs=vmem,
        scratch_shapes=[pltpu.VMEM(rhs.shape, rhs.dtype)],
    )(diagonal, coupling, shifts, rhs)


def split_bf16(values):
    rounded = lax.reduce_precision(values, exponent_bits=8, mantissa_bits=7)
    return rounded.astype(jnp.bfloat16), (values - rounded).astype(jnp.bfloat16)


def transform(spec, data, basis):
    high, low = split_bf16(data)
    basis_high, basis_low = basis

    def product(first, second):
        return jnp.einsum(spec, first, second, preferred_element_type=jnp.float32)

    return product(high, basis_high) + (product(low, basis_high) + product(high, basis_low))


def shards(
    right_side,
    conduct,
    excavated,
    vectors_x,
    mass_x,
    values_x,
    vectors_y,
    mass_y,
    values_y,
    vertical_diag,
    vertical_coupling,
):
    active = excavated.astype(jnp.float32)
    both = edges(jnp.stack([conduct, active]))
    faces = faces_from(conduct, [(low[0], high[0]) for low, high in both])
    active_x, active_y = [(low[1], high[1]) for low, high in both]
    local_modes = vectors_x.shape[1] // (lax.axis_size("gx") * lax.axis_size("gy"))
    mode_start = (lax.axis_index("gx") * lax.axis_size("gy") + lax.axis_index("gy")) * local_modes
    local_values = lax.dynamic_slice_in_dim(values_x, mode_start, local_modes, 0)
    shifts = local_values[:, None] + values_y[None, :]
    adjoint = None
    residual = right_side
    everyone = ("gx", "gy")
    blocks_y = lax.axis_size("gx")
    basis_x = split_bf16(vectors_x)
    rows = right_side.shape[1]
    y_active = jnp.concatenate(active_y, axis=1)
    count_y = lax.axis_size("gx")
    forward_y = [(i, i + 1) for i in range(count_y - 1)]
    backward_y = [(target, source) for source, target in forward_y]
    basis_y = tuple(piece.reshape(blocks_y, -1, vectors_y.shape[1]) for piece in split_bf16(vectors_y))
    for iteration in range(ITERS):
        scaled = residual * mass_x[None, :, None] * mass_y[None, None, :]
        modes = transform(
            "zxy,xi->ziy",
            lax.all_to_all(scaled, "gy", split_axis=0, concat_axis=1, tiled=True),
            basis_x,
        )
        chunks = modes.reshape(-1, local_modes, modes.shape[2])
        chunks = lax.all_to_all(chunks, everyone, split_axis=0, concat_axis=0, tiled=True)
        chunks = chunks.reshape(blocks_y, -1, local_modes, chunks.shape[2])
        modes = transform("azil,alj->zij", chunks, basis_y)
        solved = vertical_solve(modes, vertical_diag, vertical_coupling, shifts)
        chunks = transform("zij,alj->azil", solved, basis_y)
        chunks = chunks.reshape(-1, local_modes, chunks.shape[3])
        chunks = lax.all_to_all(chunks, everyone, split_axis=0, concat_axis=0, tiled=True)
        solved = chunks.reshape(-1, chunks.shape[2])
        plane = transform("iy,xi->xy", solved, basis_x)
        blocks = plane.reshape(-1, rows, plane.shape[1])
        from_left = lax.ppermute(blocks[:, :, -1], "gx", forward_y)
        from_right = lax.ppermute(blocks[:, :, 0], "gx", backward_y)
        zero = jnp.zeros_like(blocks[:1, :1])
        below = jnp.concatenate([zero, blocks[:-1, -1:]], axis=0)
        above = jnp.concatenate([blocks[1:, :1], zero], axis=0)
        halo_row = jnp.concatenate([from_left, from_right], axis=1)[:, None, :]
        framed = jnp.concatenate([below, blocks, above, halo_row], axis=1)
        framed = lax.all_to_all(framed, "gy", split_axis=0, concat_axis=0, tiled=True)
        residual, adjoint = framed_stencil(framed, active, residual, adjoint, active_x, y_active, faces)
    return (adjoint, residual)


def solution(mesh):
    in_specs = (
        P(None, "gy", "gx"),
        P(None, "gy", "gx"),
        P(None, "gy", "gx"),
        P(),
        P("gy"),
        P(),
        P(),
        P("gx"),
        P(),
        P(),
        P(),
    )
    out_specs = (P(None, "gy", "gx"), P(None, "gy", "gx"))
    return jax.shard_map(shards, mesh=mesh, in_specs=in_specs, out_specs=out_specs, check_vma=False)
```

```python
import functools

import jax
import jax.numpy as jnp
from jax import lax
from jax.experimental import pallas as pl
from jax.experimental.pallas import tpu as pltpu
from jax.sharding import PartitionSpec as P

ITERS = 2


storage_term = 0.2


def edge_pair(block, axis, dim):
    count = lax.axis_size(axis)
    forward = [(i, i + 1) for i in range(count - 1)]
    backward = [(target, source) for source, target in forward]
    last = lax.index_in_dim(block, block.shape[dim] - 1, axis=dim, keepdims=False)
    first = lax.index_in_dim(block, 0, axis=dim, keepdims=False)
    return lax.ppermute(last, axis, forward), lax.ppermute(first, axis, backward)


def edges(block):
    return [edge_pair(block, "gy", block.ndim - 2), edge_pair(block, "gx", block.ndim - 1)]


def harmonic(first, second):
    return 2.0 * first * second / (first + second)


def neighbours(center, strips):
    (x_low, x_high), (y_low, y_high) = strips
    zeros = jnp.zeros_like(center[:1])
    return [
        jnp.concatenate([center[1:], zeros], axis=0),
        jnp.concatenate([zeros, center[:-1]], axis=0),
        jnp.concatenate([center[:, 1:], x_high[:, None, :]], axis=1),
        jnp.concatenate([x_low[:, None, :], center[:, :-1]], axis=1),
        jnp.concatenate([center[:, :, 1:], y_high[:, :, None]], axis=2),
        jnp.concatenate([y_low[:, :, None], center[:, :, :-1]], axis=2),
    ]


def faces_from(center, strips):
    return [harmonic(center, other) for other in neighbours(center, strips)]


def framed_kernel(has_adjoint, has_scale, framed_ref, active_ref, residual_ref, *refs):
    refs = list(refs)
    adjoint_ref = refs.pop(0) if has_adjoint else None
    x_low_ref, x_high_ref, y_low_ref, y_high_ref = refs[:4]
    refs = refs[4:]
    mass_x_ref, mass_y_ref = (refs.pop(0), refs.pop(0)) if has_scale else (None, None)
    scaled_out = refs.pop() if has_scale else None
    face_refs, residual_out, adjoint_out = refs[:-2], refs[-2], refs[-1]
    planes, rows, cols = active_ref.shape
    row = lax.broadcasted_iota(jnp.int32, (rows, cols), 0)
    col = lax.broadcasted_iota(jnp.int32, (rows, cols), 1)
    row_forward = pltpu.roll(row, 1, 0) == jnp.where(row == 0, rows - 1, row - 1)
    col_forward = pltpu.roll(col, 1, 1) == jnp.where(col == 0, cols - 1, col - 1)

    def before(plane, axis, count, forward):
        return jnp.where(forward, pltpu.roll(plane, 1, axis), pltpu.roll(plane, count - 1, axis))

    def after(plane, axis, count, forward):
        return jnp.where(forward, pltpu.roll(plane, count - 1, axis), pltpu.roll(plane, 1, axis))

    zeros = jnp.zeros((rows, cols), jnp.float32)
    updates = [framed_ref[z, pl.ds(1, rows), :] for z in range(planes)]
    masked = [active_ref[z] * updates[z] for z in range(planes)]
    for z in range(planes):
        center = masked[z]
        x_low = x_low_ref[pl.ds(z, 1), :] * framed_ref[z, pl.ds(0, 1), :]
        x_high = x_high_ref[pl.ds(z, 1), :] * framed_ref[z, pl.ds(rows + 1, 1), :]
        others = [
            masked[z + 1] if z + 1 < planes else zeros,
            masked[z - 1] if z > 0 else zeros,
            jnp.where(row == rows - 1, jnp.broadcast_to(x_high, (rows, cols)), after(center, 0, rows, row_forward)),
            jnp.where(row == 0, jnp.broadcast_to(x_low, (rows, cols)), before(center, 0, rows, row_forward)),
            jnp.where(col == cols - 1, y_high_ref[z], after(center, 1, cols, col_forward)),
            jnp.where(col == 0, y_low_ref[z], before(center, 1, cols, col_forward)),
        ]
        result = storage_term * center
        for face_ref, other in zip(face_refs, others):
            result = result + face_ref[z] * (center - other)
        update = updates[z]
        residual = residual_ref[z] - (result + (1.0 - active_ref[z]) * update)
        residual_out[z] = residual
        if has_scale:
            scaled_out[z] = residual * mass_x_ref[...] * mass_y_ref[...]
        adjoint_out[z] = update if adjoint_ref is None else adjoint_ref[z] + update


def framed_stencil(framed, active, residual, adjoint, x_strips, y_strips, faces, masses=None):
    vmem = pl.BlockSpec(memory_space=pltpu.VMEM)
    shape = jax.ShapeDtypeStruct(active.shape, active.dtype)
    y_low, y_high = (jnp.broadcast_to(strip[:, :, None], active.shape) for strip in y_strips)
    carried = [] if adjoint is None else [adjoint]
    scales = [] if masses is None else list(masses)
    operands = [framed, active, residual, *carried, x_strips[0], x_strips[1], y_low, y_high, *scales, *faces]
    outputs = 2 if masses is None else 3
    return pl.pallas_call(
        functools.partial(framed_kernel, adjoint is not None, masses is not None),
        out_shape=(shape,) * outputs,
        in_specs=[vmem] * len(operands),
        out_specs=(vmem,) * outputs,
    )(*operands)


def solve_kernel(diag_ref, coup_ref, shifts_ref, rhs_ref, out_ref, ratio_ref):
    count = rhs_ref.shape[0]
    shifts = shifts_ref[...]
    denom = diag_ref[0] + shifts
    ratio = -coup_ref[0] / denom
    ratio_ref[0] = ratio
    part = rhs_ref[0] / denom
    out_ref[0] = part
    for position in range(1, count):
        denom = diag_ref[position] + shifts + coup_ref[position - 1] * ratio
        if position < count - 1:
            ratio = -coup_ref[position] / denom
            ratio_ref[position] = ratio
        part = (rhs_ref[position] + coup_ref[position - 1] * part) / denom
        out_ref[position] = part
    solved = part
    for position in range(count - 2, -1, -1):
        solved = out_ref[position] - ratio_ref[position] * solved
        out_ref[position] = solved


def vertical_solve(rhs, diagonal, coupling, shifts):
    smem = pl.BlockSpec(memory_space=pltpu.SMEM)
    vmem = pl.BlockSpec(memory_space=pltpu.VMEM)
    return pl.pallas_call(
        solve_kernel,
        out_shape=jax.ShapeDtypeStruct(rhs.shape, rhs.dtype),
        in_specs=[smem, smem, vmem, vmem],
        out_specs=vmem,
        scratch_shapes=[pltpu.VMEM(rhs.shape, rhs.dtype)],
    )(diagonal, coupling, shifts, rhs)


def split_bf16(values):
    rounded = lax.reduce_precision(values, exponent_bits=8, mantissa_bits=7)
    return rounded.astype(jnp.bfloat16), (values - rounded).astype(jnp.bfloat16)


def transform(spec, data, basis):
    high, low = split_bf16(data)
    basis_high, basis_low = basis

    def product(first, second):
        return jnp.einsum(spec, first, second, preferred_element_type=jnp.float32)

    return product(high, basis_high) + (product(low, basis_high) + product(high, basis_low))


def shards(
    right_side,
    conduct,
    excavated,
    vectors_x,
    mass_x,
    values_x,
    vectors_y,
    mass_y,
    values_y,
    vertical_diag,
    vertical_coupling,
):
    active = excavated.astype(jnp.float32)
    both = edges(jnp.stack([conduct, active]))
    faces = faces_from(conduct, [(low[0], high[0]) for low, high in both])
    active_x, active_y = [(low[1], high[1]) for low, high in both]
    local_modes = vectors_x.shape[1] // (lax.axis_size("gx") * lax.axis_size("gy"))
    mode_start = (lax.axis_index("gx") * lax.axis_size("gy") + lax.axis_index("gy")) * local_modes
    local_values = lax.dynamic_slice_in_dim(values_x, mode_start, local_modes, 0)
    shifts = local_values[:, None] + values_y[None, :]
    adjoint = None
    residual = right_side
    everyone = ("gx", "gy")
    blocks_y = lax.axis_size("gx")
    basis_x = split_bf16(vectors_x)
    rows = right_side.shape[1]
    count_y = lax.axis_size("gx")
    forward_y = [(i, i + 1) for i in range(count_y - 1)]
    backward_y = [(target, source) for source, target in forward_y]
    basis_y = tuple(piece.reshape(blocks_y, -1, vectors_y.shape[1]) for piece in split_bf16(vectors_y))
    rows_of, cols_of = right_side.shape[1], right_side.shape[2]
    masses = (
        jnp.broadcast_to(mass_x[:, None], (rows_of, cols_of)),
        jnp.broadcast_to(mass_y[None, :], (rows_of, cols_of)),
    )
    scaled = residual * mass_x[None, :, None] * mass_y[None, None, :]
    for iteration in range(ITERS):
        modes = transform(
            "zxy,xi->ziy",
            lax.all_to_all(scaled, "gy", split_axis=0, concat_axis=1, tiled=True),
            basis_x,
        )
        chunks = modes.reshape(-1, local_modes, modes.shape[2])
        chunks = lax.all_to_all(chunks, everyone, split_axis=0, concat_axis=0, tiled=True)
        chunks = chunks.reshape(blocks_y, -1, local_modes, chunks.shape[2])
        modes = transform("azil,alj->zij", chunks, basis_y)
        solved = vertical_solve(modes, vertical_diag, vertical_coupling, shifts)
        chunks = transform("zij,alj->azil", solved, basis_y)
        chunks = chunks.reshape(-1, local_modes, chunks.shape[3])
        chunks = lax.all_to_all(chunks, everyone, split_axis=0, concat_axis=0, tiled=True)
        solved = chunks.reshape(-1, chunks.shape[2])
        plane = transform("iy,xi->xy", solved, basis_x)
        blocks = plane.reshape(-1, rows, plane.shape[1])
        from_left = lax.ppermute(blocks[:, :, -1], "gx", forward_y)
        from_right = lax.ppermute(blocks[:, :, 0], "gx", backward_y)
        zero = jnp.zeros_like(blocks[:1, :1])
        below = jnp.concatenate([zero, blocks[:-1, -1:]], axis=0)
        above = jnp.concatenate([blocks[1:, :1], zero], axis=0)
        halo_row = jnp.concatenate([from_left, from_right], axis=1)[:, None, :]
        framed = jnp.concatenate([below, blocks, above, halo_row], axis=1)
        framed = lax.all_to_all(framed, "gy", split_axis=0, concat_axis=0, tiled=True)
        y_strips = (active_y[0] * framed[:, -1, :rows], active_y[1] * framed[:, -1, rows:])
        if iteration + 1 < ITERS:
            residual, adjoint, scaled = framed_stencil(
                framed, active, residual, adjoint, active_x, y_strips, faces, masses
            )
        else:
            residual, adjoint = framed_stencil(framed, active, residual, adjoint, active_x, y_strips, faces)
    return (adjoint, residual)


def solution(mesh):
    in_specs = (
        P(None, "gy", "gx"),
        P(None, "gy", "gx"),
        P(None, "gy", "gx"),
        P(),
        P("gy"),
        P(),
        P(),
        P("gx"),
        P(),
        P(),
        P(),
    )
    out_specs = (P(None, "gy", "gx"), P(None, "gy", "gx"))
    return jax.shard_map(shards, mesh=mesh, in_specs=in_specs, out_specs=out_specs, check_vma=False)
```

```python
import functools

import jax
import jax.numpy as jnp
from jax import lax
from jax.experimental import pallas as pl
from jax.experimental.pallas import tpu as pltpu
from jax.sharding import PartitionSpec as P

ITERS = 2


storage_term = 0.2


def edge_pair(block, axis, dim):
    count = lax.axis_size(axis)
    forward = [(i, i + 1) for i in range(count - 1)]
    backward = [(target, source) for source, target in forward]
    last = lax.index_in_dim(block, block.shape[dim] - 1, axis=dim, keepdims=False)
    first = lax.index_in_dim(block, 0, axis=dim, keepdims=False)
    return lax.ppermute(last, axis, forward), lax.ppermute(first, axis, backward)


def edges(block):
    return [edge_pair(block, "gy", block.ndim - 2), edge_pair(block, "gx", block.ndim - 1)]


def harmonic(first, second):
    return 2.0 * first * second / (first + second)


def neighbours(center, strips):
    (x_low, x_high), (y_low, y_high) = strips
    zeros = jnp.zeros_like(center[:1])
    return [
        jnp.concatenate([center[1:], zeros], axis=0),
        jnp.concatenate([zeros, center[:-1]], axis=0),
        jnp.concatenate([center[:, 1:], x_high[:, None, :]], axis=1),
        jnp.concatenate([x_low[:, None, :], center[:, :-1]], axis=1),
        jnp.concatenate([center[:, :, 1:], y_high[:, :, None]], axis=2),
        jnp.concatenate([y_low[:, :, None], center[:, :, :-1]], axis=2),
    ]


def faces_from(center, strips):
    return [harmonic(center, other) for other in neighbours(center, strips)]


def framed_kernel(has_adjoint, has_scale, framed_ref, active_ref, residual_ref, *refs):
    refs = list(refs)
    adjoint_ref = refs.pop(0) if has_adjoint else None
    x_low_ref, x_high_ref, y_low_ref, y_high_ref = refs[:4]
    refs = refs[4:]
    mass_x_ref, mass_y_ref = (refs.pop(0), refs.pop(0)) if has_scale else (None, None)
    scaled_out = refs.pop() if has_scale else None
    face_refs, residual_out, adjoint_out = refs[:-2], refs[-2], refs[-1]
    planes, rows, cols = active_ref.shape
    row = lax.broadcasted_iota(jnp.int32, (rows, cols), 0)
    col = lax.broadcasted_iota(jnp.int32, (rows, cols), 1)
    row_forward = pltpu.roll(row, 1, 0) == jnp.where(row == 0, rows - 1, row - 1)
    col_forward = pltpu.roll(col, 1, 1) == jnp.where(col == 0, cols - 1, col - 1)

    def before(plane, axis, count, forward):
        return jnp.where(forward, pltpu.roll(plane, 1, axis), pltpu.roll(plane, count - 1, axis))

    def after(plane, axis, count, forward):
        return jnp.where(forward, pltpu.roll(plane, count - 1, axis), pltpu.roll(plane, 1, axis))

    zeros = jnp.zeros((rows, cols), jnp.float32)
    updates = [framed_ref[z, pl.ds(1, rows), :] for z in range(planes)]
    masked = [active_ref[z] * updates[z] for z in range(planes)]
    for z in range(planes):
        center = masked[z]
        x_low = x_low_ref[pl.ds(z, 1), :] * framed_ref[z, pl.ds(0, 1), :]
        x_high = x_high_ref[pl.ds(z, 1), :] * framed_ref[z, pl.ds(rows + 1, 1), :]
        others = [
            masked[z + 1] if z + 1 < planes else zeros,
            masked[z - 1] if z > 0 else zeros,
            jnp.where(row == rows - 1, jnp.broadcast_to(x_high, (rows, cols)), after(center, 0, rows, row_forward)),
            jnp.where(row == 0, jnp.broadcast_to(x_low, (rows, cols)), before(center, 0, rows, row_forward)),
            jnp.where(col == cols - 1, y_high_ref[z], after(center, 1, cols, col_forward)),
            jnp.where(col == 0, y_low_ref[z], before(center, 1, cols, col_forward)),
        ]
        result = storage_term * center
        for face_ref, other in zip(face_refs, others):
            result = result + face_ref[z] * (center - other)
        update = updates[z]
        residual = residual_ref[z] - (result + (1.0 - active_ref[z]) * update)
        residual_out[z] = residual
        if has_scale:
            scaled_out[z] = residual * mass_x_ref[...] * mass_y_ref[...]
        adjoint_out[z] = update if adjoint_ref is None else adjoint_ref[z] + update


def framed_stencil(framed, active, residual, adjoint, x_strips, y_strips, faces, masses=None):
    vmem = pl.BlockSpec(memory_space=pltpu.VMEM)
    shape = jax.ShapeDtypeStruct(active.shape, active.dtype)
    y_low, y_high = (jnp.broadcast_to(strip[:, :, None], active.shape) for strip in y_strips)
    carried = [] if adjoint is None else [adjoint]
    scales = [] if masses is None else list(masses)
    operands = [framed, active, residual, *carried, x_strips[0], x_strips[1], y_low, y_high, *scales, *faces]
    outputs = 2 if masses is None else 3
    return pl.pallas_call(
        functools.partial(framed_kernel, adjoint is not None, masses is not None),
        out_shape=(shape,) * outputs,
        in_specs=[vmem] * len(operands),
        out_specs=(vmem,) * outputs,
    )(*operands)


def solve_kernel(diag_ref, coup_ref, shifts_ref, rhs_ref, out_ref, ratio_ref):
    count = rhs_ref.shape[0]
    shifts = shifts_ref[...]
    denom = diag_ref[0] + shifts
    ratio = -coup_ref[0] / denom
    ratio_ref[0] = ratio
    part = rhs_ref[0] / denom
    out_ref[0] = part
    for position in range(1, count):
        denom = diag_ref[position] + shifts + coup_ref[position - 1] * ratio
        if position < count - 1:
            ratio = -coup_ref[position] / denom
            ratio_ref[position] = ratio
        part = (rhs_ref[position] + coup_ref[position - 1] * part) / denom
        out_ref[position] = part
    solved = part
    for position in range(count - 2, -1, -1):
        solved = out_ref[position] - ratio_ref[position] * solved
        out_ref[position] = solved


def vertical_solve(rhs, diagonal, coupling, shifts):
    smem = pl.BlockSpec(memory_space=pltpu.SMEM)
    vmem = pl.BlockSpec(memory_space=pltpu.VMEM)
    return pl.pallas_call(
        solve_kernel,
        out_shape=jax.ShapeDtypeStruct(rhs.shape, rhs.dtype),
        in_specs=[smem, smem, vmem, vmem],
        out_specs=vmem,
        scratch_shapes=[pltpu.VMEM(rhs.shape, rhs.dtype)],
    )(diagonal, coupling, shifts, rhs)


def split_bf16(values):
    rounded = lax.reduce_precision(values, exponent_bits=8, mantissa_bits=7)
    return rounded.astype(jnp.bfloat16), (values - rounded).astype(jnp.bfloat16)


def transform(spec, data, basis):
    high, low = split_bf16(data)
    basis_high, basis_low = basis

    def product(first, second):
        return jnp.einsum(spec, first, second, preferred_element_type=jnp.float32)

    return product(high, basis_high) + (product(low, basis_high) + product(high, basis_low))


def shards(
    right_side,
    conduct,
    excavated,
    vectors_x,
    mass_x,
    values_x,
    vectors_y,
    mass_y,
    values_y,
    vertical_diag,
    vertical_coupling,
):
    active = excavated.astype(jnp.float32)
    both = edges(jnp.stack([conduct, active]))
    faces = faces_from(conduct, [(low[0], high[0]) for low, high in both])
    active_x, active_y = [(low[1], high[1]) for low, high in both]
    local_modes = vectors_x.shape[1] // (lax.axis_size("gx") * lax.axis_size("gy"))
    mode_start = (lax.axis_index("gx") * lax.axis_size("gy") + lax.axis_index("gy")) * local_modes
    local_values = lax.dynamic_slice_in_dim(values_x, mode_start, local_modes, 0)
    shifts = local_values[:, None] + values_y[None, :]
    adjoint = None
    residual = right_side
    everyone = ("gx", "gy")
    blocks_y = lax.axis_size("gx")
    basis_x = split_bf16(vectors_x)
    rows = right_side.shape[1]
    count_y = lax.axis_size("gx")
    forward_y = [(i, i + 1) for i in range(count_y - 1)]
    backward_y = [(target, source) for source, target in forward_y]
    basis_y = tuple(piece.reshape(blocks_y, -1, vectors_y.shape[1]) for piece in split_bf16(vectors_y))
    rows_of, cols_of = right_side.shape[1], right_side.shape[2]
    masses = (mass_x.reshape(rows_of, 1), mass_y.reshape(1, cols_of))
    scaled = residual * mass_x[None, :, None] * mass_y[None, None, :]
    for iteration in range(ITERS):
        modes = transform(
            "zxy,xi->ziy",
            lax.all_to_all(scaled, "gy", split_axis=0, concat_axis=1, tiled=True),
            basis_x,
        )
        chunks = modes.reshape(-1, local_modes, modes.shape[2])
        chunks = lax.all_to_all(chunks, everyone, split_axis=0, concat_axis=0, tiled=True)
        chunks = chunks.reshape(blocks_y, -1, local_modes, chunks.shape[2])
        modes = transform("azil,alj->zij", chunks, basis_y)
        solved = vertical_solve(modes, vertical_diag, vertical_coupling, shifts)
        chunks = transform("zij,alj->azil", solved, basis_y)
        chunks = chunks.reshape(-1, local_modes, chunks.shape[3])
        chunks = lax.all_to_all(chunks, everyone, split_axis=0, concat_axis=0, tiled=True)
        solved = chunks.reshape(-1, chunks.shape[2])
        plane = transform("iy,xi->xy", solved, basis_x)
        blocks = plane.reshape(-1, rows, plane.shape[1])
        from_left = lax.ppermute(blocks[:, :, -1], "gx", forward_y)
        from_right = lax.ppermute(blocks[:, :, 0], "gx", backward_y)
        zero = jnp.zeros_like(blocks[:1, :1])
        below = jnp.concatenate([zero, blocks[:-1, -1:]], axis=0)
        above = jnp.concatenate([blocks[1:, :1], zero], axis=0)
        halo_row = jnp.concatenate([from_left, from_right], axis=1)[:, None, :]
        framed = jnp.concatenate([below, blocks, above, halo_row], axis=1)
        framed = lax.all_to_all(framed, "gy", split_axis=0, concat_axis=0, tiled=True)
        y_strips = (active_y[0] * framed[:, -1, :rows], active_y[1] * framed[:, -1, rows:])
        if iteration + 1 < ITERS:
            residual, adjoint, scaled = framed_stencil(
                framed, active, residual, adjoint, active_x, y_strips, faces, masses
            )
        else:
            residual, adjoint = framed_stencil(framed, active, residual, adjoint, active_x, y_strips, faces)
    return (adjoint, residual)


def solution(mesh):
    in_specs = (
        P(None, "gy", "gx"),
        P(None, "gy", "gx"),
        P(None, "gy", "gx"),
        P(),
        P("gy"),
        P(),
        P(),
        P("gx"),
        P(),
        P(),
        P(),
    )
    out_specs = (P(None, "gy", "gx"), P(None, "gy", "gx"))
    return jax.shard_map(shards, mesh=mesh, in_specs=in_specs, out_specs=out_specs, check_vma=False)
```

```python
import functools

import jax
import jax.numpy as jnp
from jax import lax
from jax.experimental import pallas as pl
from jax.experimental.pallas import tpu as pltpu
from jax.sharding import PartitionSpec as P

ITERS = 2


storage_term = 0.2


def edge_pair(block, axis, dim):
    count = lax.axis_size(axis)
    forward = [(i, i + 1) for i in range(count - 1)]
    backward = [(target, source) for source, target in forward]
    last = lax.index_in_dim(block, block.shape[dim] - 1, axis=dim, keepdims=False)
    first = lax.index_in_dim(block, 0, axis=dim, keepdims=False)
    return lax.ppermute(last, axis, forward), lax.ppermute(first, axis, backward)


def edges(block):
    return [edge_pair(block, "gy", block.ndim - 2), edge_pair(block, "gx", block.ndim - 1)]


def harmonic(first, second):
    return 2.0 * first * second / (first + second)


def neighbours(center, strips):
    (x_low, x_high), (y_low, y_high) = strips
    zeros = jnp.zeros_like(center[:1])
    return [
        jnp.concatenate([center[1:], zeros], axis=0),
        jnp.concatenate([zeros, center[:-1]], axis=0),
        jnp.concatenate([center[:, 1:], x_high[:, None, :]], axis=1),
        jnp.concatenate([x_low[:, None, :], center[:, :-1]], axis=1),
        jnp.concatenate([center[:, :, 1:], y_high[:, :, None]], axis=2),
        jnp.concatenate([y_low[:, :, None], center[:, :, :-1]], axis=2),
    ]


def faces_from(center, strips):
    return [harmonic(center, other) for other in neighbours(center, strips)]


def framed_kernel(has_adjoint, has_scale, framed_ref, active_ref, residual_ref, *refs):
    refs = list(refs)
    adjoint_ref = refs.pop(0) if has_adjoint else None
    x_low_ref, x_high_ref, y_halo_ref = refs[:3]
    refs = refs[3:]
    mass_x_ref, mass_y_ref = (refs.pop(0), refs.pop(0)) if has_scale else (None, None)
    scaled_out = refs.pop() if has_scale else None
    face_refs, residual_out, adjoint_out = refs[:-2], refs[-2], refs[-1]
    planes, rows, cols = active_ref.shape
    row = lax.broadcasted_iota(jnp.int32, (rows, cols), 0)
    col = lax.broadcasted_iota(jnp.int32, (rows, cols), 1)
    row_forward = pltpu.roll(row, 1, 0) == jnp.where(row == 0, rows - 1, row - 1)
    col_forward = pltpu.roll(col, 1, 1) == jnp.where(col == 0, cols - 1, col - 1)

    def before(plane, axis, count, forward):
        return jnp.where(forward, pltpu.roll(plane, 1, axis), pltpu.roll(plane, count - 1, axis))

    def after(plane, axis, count, forward):
        return jnp.where(forward, pltpu.roll(plane, count - 1, axis), pltpu.roll(plane, 1, axis))

    zeros = jnp.zeros((rows, cols), jnp.float32)
    updates = [framed_ref[z, pl.ds(1, rows), :] for z in range(planes)]
    masked = [active_ref[z] * updates[z] for z in range(planes)]
    for z in range(planes):
        center = masked[z]
        x_low = x_low_ref[pl.ds(z, 1), :] * framed_ref[z, pl.ds(0, 1), :]
        x_high = x_high_ref[pl.ds(z, 1), :] * framed_ref[z, pl.ds(rows + 1, 1), :]
        others = [
            masked[z + 1] if z + 1 < planes else zeros,
            masked[z - 1] if z > 0 else zeros,
            jnp.where(row == rows - 1, jnp.broadcast_to(x_high, (rows, cols)), after(center, 0, rows, row_forward)),
            jnp.where(row == 0, jnp.broadcast_to(x_low, (rows, cols)), before(center, 0, rows, row_forward)),
            jnp.where(col == cols - 1, y_halo_ref[z], after(center, 1, cols, col_forward)),
            jnp.where(col == 0, y_halo_ref[z], before(center, 1, cols, col_forward)),
        ]
        result = storage_term * center
        for face_ref, other in zip(face_refs, others):
            result = result + face_ref[z] * (center - other)
        update = updates[z]
        residual = residual_ref[z] - (result + (1.0 - active_ref[z]) * update)
        residual_out[z] = residual
        if has_scale:
            scaled_out[z] = residual * mass_x_ref[...] * mass_y_ref[...]
        adjoint_out[z] = update if adjoint_ref is None else adjoint_ref[z] + update


def framed_stencil(framed, active, residual, adjoint, x_strips, y_strips, faces, masses=None):
    vmem = pl.BlockSpec(memory_space=pltpu.VMEM)
    shape = jax.ShapeDtypeStruct(active.shape, active.dtype)
    lane = lax.broadcasted_iota(jnp.int32, active.shape, 2)
    y_halo = jnp.where(lane == 0, y_strips[0][:, :, None], y_strips[1][:, :, None])
    carried = [] if adjoint is None else [adjoint]
    scales = [] if masses is None else list(masses)
    operands = [framed, active, residual, *carried, x_strips[0], x_strips[1], y_halo, *scales, *faces]
    outputs = 2 if masses is None else 3
    return pl.pallas_call(
        functools.partial(framed_kernel, adjoint is not None, masses is not None),
        out_shape=(shape,) * outputs,
        in_specs=[vmem] * len(operands),
        out_specs=(vmem,) * outputs,
    )(*operands)


def solve_kernel(diag_ref, coup_ref, shifts_ref, rhs_ref, out_ref, ratio_ref):
    count = rhs_ref.shape[0]
    shifts = shifts_ref[...]
    denom = diag_ref[0] + shifts
    ratio = -coup_ref[0] / denom
    ratio_ref[0] = ratio
    part = rhs_ref[0] / denom
    out_ref[0] = part
    for position in range(1, count):
        denom = diag_ref[position] + shifts + coup_ref[position - 1] * ratio
        if position < count - 1:
            ratio = -coup_ref[position] / denom
            ratio_ref[position] = ratio
        part = (rhs_ref[position] + coup_ref[position - 1] * part) / denom
        out_ref[position] = part
    solved = part
    for position in range(count - 2, -1, -1):
        solved = out_ref[position] - ratio_ref[position] * solved
        out_ref[position] = solved


def vertical_solve(rhs, diagonal, coupling, shifts):
    smem = pl.BlockSpec(memory_space=pltpu.SMEM)
    vmem = pl.BlockSpec(memory_space=pltpu.VMEM)
    return pl.pallas_call(
        solve_kernel,
        out_shape=jax.ShapeDtypeStruct(rhs.shape, rhs.dtype),
        in_specs=[smem, smem, vmem, vmem],
        out_specs=vmem,
        scratch_shapes=[pltpu.VMEM(rhs.shape, rhs.dtype)],
    )(diagonal, coupling, shifts, rhs)


def split_bf16(values):
    rounded = lax.reduce_precision(values, exponent_bits=8, mantissa_bits=7)
    return rounded.astype(jnp.bfloat16), (values - rounded).astype(jnp.bfloat16)


def transform(spec, data, basis):
    high, low = split_bf16(data)
    basis_high, basis_low = basis

    def product(first, second):
        return jnp.einsum(spec, first, second, preferred_element_type=jnp.float32)

    return product(high, basis_high) + (product(low, basis_high) + product(high, basis_low))


def shards(
    right_side,
    conduct,
    excavated,
    vectors_x,
    mass_x,
    values_x,
    vectors_y,
    mass_y,
    values_y,
    vertical_diag,
    vertical_coupling,
):
    active = excavated.astype(jnp.float32)
    both = edges(jnp.stack([conduct, active]))
    faces = faces_from(conduct, [(low[0], high[0]) for low, high in both])
    active_x, active_y = [(low[1], high[1]) for low, high in both]
    local_modes = vectors_x.shape[1] // (lax.axis_size("gx") * lax.axis_size("gy"))
    mode_start = (lax.axis_index("gx") * lax.axis_size("gy") + lax.axis_index("gy")) * local_modes
    local_values = lax.dynamic_slice_in_dim(values_x, mode_start, local_modes, 0)
    shifts = local_values[:, None] + values_y[None, :]
    adjoint = None
    residual = right_side
    everyone = ("gx", "gy")
    blocks_y = lax.axis_size("gx")
    basis_x = split_bf16(vectors_x)
    rows = right_side.shape[1]
    count_y = lax.axis_size("gx")
    forward_y = [(i, i + 1) for i in range(count_y - 1)]
    backward_y = [(target, source) for source, target in forward_y]
    basis_y = tuple(piece.reshape(blocks_y, -1, vectors_y.shape[1]) for piece in split_bf16(vectors_y))
    rows_of, cols_of = right_side.shape[1], right_side.shape[2]
    masses = (mass_x.reshape(rows_of, 1), mass_y.reshape(1, cols_of))
    scaled = residual * mass_x[None, :, None] * mass_y[None, None, :]
    for iteration in range(ITERS):
        modes = transform(
            "zxy,xi->ziy",
            lax.all_to_all(scaled, "gy", split_axis=0, concat_axis=1, tiled=True),
            basis_x,
        )
        chunks = modes.reshape(-1, local_modes, modes.shape[2])
        chunks = lax.all_to_all(chunks, everyone, split_axis=0, concat_axis=0, tiled=True)
        chunks = chunks.reshape(blocks_y, -1, local_modes, chunks.shape[2])
        modes = transform("azil,alj->zij", chunks, basis_y)
        solved = vertical_solve(modes, vertical_diag, vertical_coupling, shifts)
        chunks = transform("zij,alj->azil", solved, basis_y)
        chunks = chunks.reshape(-1, local_modes, chunks.shape[3])
        chunks = lax.all_to_all(chunks, everyone, split_axis=0, concat_axis=0, tiled=True)
        solved = chunks.reshape(-1, chunks.shape[2])
        plane = transform("iy,xi->xy", solved, basis_x)
        blocks = plane.reshape(-1, rows, plane.shape[1])
        from_left = lax.ppermute(blocks[:, :, -1], "gx", forward_y)
        from_right = lax.ppermute(blocks[:, :, 0], "gx", backward_y)
        zero = jnp.zeros_like(blocks[:1, :1])
        below = jnp.concatenate([zero, blocks[:-1, -1:]], axis=0)
        above = jnp.concatenate([blocks[1:, :1], zero], axis=0)
        halo_row = jnp.concatenate([from_left, from_right], axis=1)[:, None, :]
        framed = jnp.concatenate([below, blocks, above, halo_row], axis=1)
        framed = lax.all_to_all(framed, "gy", split_axis=0, concat_axis=0, tiled=True)
        y_strips = (active_y[0] * framed[:, -1, :rows], active_y[1] * framed[:, -1, rows:])
        if iteration + 1 < ITERS:
            residual, adjoint, scaled = framed_stencil(
                framed, active, residual, adjoint, active_x, y_strips, faces, masses
            )
        else:
            residual, adjoint = framed_stencil(framed, active, residual, adjoint, active_x, y_strips, faces)
    return (adjoint, residual)


def solution(mesh):
    in_specs = (
        P(None, "gy", "gx"),
        P(None, "gy", "gx"),
        P(None, "gy", "gx"),
        P(),
        P("gy"),
        P(),
        P(),
        P("gx"),
        P(),
        P(),
        P(),
    )
    out_specs = (P(None, "gy", "gx"), P(None, "gy", "gx"))
    return jax.shard_map(shards, mesh=mesh, in_specs=in_specs, out_specs=out_specs, check_vma=False)
```

```python
import functools

import jax
import jax.numpy as jnp
from jax import lax
from jax.experimental import pallas as pl
from jax.experimental.pallas import tpu as pltpu
from jax.sharding import PartitionSpec as P

ITERS = 2


storage_term = 0.2


def edge_pair(block, axis, dim):
    count = lax.axis_size(axis)
    forward = [(i, i + 1) for i in range(count - 1)]
    backward = [(target, source) for source, target in forward]
    last = lax.index_in_dim(block, block.shape[dim] - 1, axis=dim, keepdims=False)
    first = lax.index_in_dim(block, 0, axis=dim, keepdims=False)
    return lax.ppermute(last, axis, forward), lax.ppermute(first, axis, backward)


def edges(block):
    return [edge_pair(block, "gy", block.ndim - 2), edge_pair(block, "gx", block.ndim - 1)]


def harmonic(first, second):
    return 2.0 * first * second / (first + second)


def neighbours(center, strips):
    (x_low, x_high), (y_low, y_high) = strips
    zeros = jnp.zeros_like(center[:1])
    return [
        jnp.concatenate([center[1:], zeros], axis=0),
        jnp.concatenate([zeros, center[:-1]], axis=0),
        jnp.concatenate([center[:, 1:], x_high[:, None, :]], axis=1),
        jnp.concatenate([x_low[:, None, :], center[:, :-1]], axis=1),
        jnp.concatenate([center[:, :, 1:], y_high[:, :, None]], axis=2),
        jnp.concatenate([y_low[:, :, None], center[:, :, :-1]], axis=2),
    ]


def faces_from(center, strips):
    return [harmonic(center, other) for other in neighbours(center, strips)]


def framed_kernel(has_adjoint, has_scale, framed_ref, active_ref, residual_ref, *refs):
    refs = list(refs)
    adjoint_ref = refs.pop(0) if has_adjoint else None
    x_low_ref, x_high_ref, y_halo_ref = refs[:3]
    refs = refs[3:]
    mass_x_ref, mass_y_ref = (refs.pop(0), refs.pop(0)) if has_scale else (None, None)
    scaled_out = refs.pop() if has_scale else None
    face_refs, residual_out, adjoint_out = refs[:-2], refs[-2], refs[-1]
    planes, rows, cols = active_ref.shape
    row = lax.broadcasted_iota(jnp.int32, (rows, cols), 0)
    col = lax.broadcasted_iota(jnp.int32, (rows, cols), 1)
    row_forward = pltpu.roll(row, 1, 0) == jnp.where(row == 0, rows - 1, row - 1)
    col_forward = pltpu.roll(col, 1, 1) == jnp.where(col == 0, cols - 1, col - 1)

    def before(plane, axis, count, forward):
        return jnp.where(forward, pltpu.roll(plane, 1, axis), pltpu.roll(plane, count - 1, axis))

    def after(plane, axis, count, forward):
        return jnp.where(forward, pltpu.roll(plane, count - 1, axis), pltpu.roll(plane, 1, axis))

    zeros = jnp.zeros((rows, cols), jnp.float32)
    updates = [framed_ref[z, pl.ds(1, rows), :] for z in range(planes)]
    masked = [active_ref[z] * updates[z] for z in range(planes)]
    for z in range(planes):
        center = masked[z]
        x_low = x_low_ref[pl.ds(z, 1), :] * framed_ref[z, pl.ds(0, 1), :]
        x_high = x_high_ref[pl.ds(z, 1), :] * framed_ref[z, pl.ds(rows + 1, 1), :]
        others = [
            masked[z + 1] if z + 1 < planes else zeros,
            masked[z - 1] if z > 0 else zeros,
            jnp.where(row == rows - 1, jnp.broadcast_to(x_high, (rows, cols)), after(center, 0, rows, row_forward)),
            jnp.where(row == 0, jnp.broadcast_to(x_low, (rows, cols)), before(center, 0, rows, row_forward)),
            jnp.where(col == cols - 1, y_halo_ref[z], after(center, 1, cols, col_forward)),
            jnp.where(col == 0, y_halo_ref[z], before(center, 1, cols, col_forward)),
        ]
        result = storage_term * center
        below = face_refs[0][z - 1] if z > 0 else zeros
        plane_faces = [face_refs[0][z], below] + [face_ref[z] for face_ref in face_refs[1:]]
        for face, other in zip(plane_faces, others):
            result = result + face * (center - other)
        update = updates[z]
        residual = residual_ref[z] - (result + (1.0 - active_ref[z]) * update)
        residual_out[z] = residual
        if has_scale:
            scaled_out[z] = residual * mass_x_ref[...] * mass_y_ref[...]
        adjoint_out[z] = update if adjoint_ref is None else adjoint_ref[z] + update


def framed_stencil(framed, active, residual, adjoint, x_strips, y_strips, faces, masses=None):
    vmem = pl.BlockSpec(memory_space=pltpu.VMEM)
    shape = jax.ShapeDtypeStruct(active.shape, active.dtype)
    lane = lax.broadcasted_iota(jnp.int32, active.shape, 2)
    y_halo = jnp.where(lane == 0, y_strips[0][:, :, None], y_strips[1][:, :, None])
    carried = [] if adjoint is None else [adjoint]
    scales = [] if masses is None else list(masses)
    operands = [framed, active, residual, *carried, x_strips[0], x_strips[1], y_halo, *scales, *faces]
    outputs = 2 if masses is None else 3
    return pl.pallas_call(
        functools.partial(framed_kernel, adjoint is not None, masses is not None),
        out_shape=(shape,) * outputs,
        in_specs=[vmem] * len(operands),
        out_specs=(vmem,) * outputs,
    )(*operands)


def solve_kernel(diag_ref, coup_ref, shifts_ref, rhs_ref, out_ref, ratio_ref):
    count = rhs_ref.shape[0]
    shifts = shifts_ref[...]
    denom = diag_ref[0] + shifts
    ratio = -coup_ref[0] / denom
    ratio_ref[0] = ratio
    part = rhs_ref[0] / denom
    out_ref[0] = part
    for position in range(1, count):
        denom = diag_ref[position] + shifts + coup_ref[position - 1] * ratio
        if position < count - 1:
            ratio = -coup_ref[position] / denom
            ratio_ref[position] = ratio
        part = (rhs_ref[position] + coup_ref[position - 1] * part) / denom
        out_ref[position] = part
    solved = part
    for position in range(count - 2, -1, -1):
        solved = out_ref[position] - ratio_ref[position] * solved
        out_ref[position] = solved


def vertical_solve(rhs, diagonal, coupling, shifts):
    smem = pl.BlockSpec(memory_space=pltpu.SMEM)
    vmem = pl.BlockSpec(memory_space=pltpu.VMEM)
    return pl.pallas_call(
        solve_kernel,
        out_shape=jax.ShapeDtypeStruct(rhs.shape, rhs.dtype),
        in_specs=[smem, smem, vmem, vmem],
        out_specs=vmem,
        scratch_shapes=[pltpu.VMEM(rhs.shape, rhs.dtype)],
    )(diagonal, coupling, shifts, rhs)


def split_bf16(values):
    rounded = lax.reduce_precision(values, exponent_bits=8, mantissa_bits=7)
    return rounded.astype(jnp.bfloat16), (values - rounded).astype(jnp.bfloat16)


def transform(spec, data, basis):
    high, low = split_bf16(data)
    basis_high, basis_low = basis

    def product(first, second):
        return jnp.einsum(spec, first, second, preferred_element_type=jnp.float32)

    return product(high, basis_high) + (product(low, basis_high) + product(high, basis_low))


def shards(
    right_side,
    conduct,
    excavated,
    vectors_x,
    mass_x,
    values_x,
    vectors_y,
    mass_y,
    values_y,
    vertical_diag,
    vertical_coupling,
):
    active = excavated.astype(jnp.float32)
    both = edges(jnp.stack([conduct, active]))
    faces = faces_from(conduct, [(low[0], high[0]) for low, high in both])
    active_x, active_y = [(low[1], high[1]) for low, high in both]
    local_modes = vectors_x.shape[1] // (lax.axis_size("gx") * lax.axis_size("gy"))
    mode_start = (lax.axis_index("gx") * lax.axis_size("gy") + lax.axis_index("gy")) * local_modes
    local_values = lax.dynamic_slice_in_dim(values_x, mode_start, local_modes, 0)
    shifts = local_values[:, None] + values_y[None, :]
    adjoint = None
    residual = right_side
    everyone = ("gx", "gy")
    blocks_y = lax.axis_size("gx")
    basis_x = split_bf16(vectors_x)
    rows = right_side.shape[1]
    count_y = lax.axis_size("gx")
    forward_y = [(i, i + 1) for i in range(count_y - 1)]
    backward_y = [(target, source) for source, target in forward_y]
    basis_y = tuple(piece.reshape(blocks_y, -1, vectors_y.shape[1]) for piece in split_bf16(vectors_y))
    rows_of, cols_of = right_side.shape[1], right_side.shape[2]
    masses = (mass_x.reshape(rows_of, 1), mass_y.reshape(1, cols_of))
    scaled = residual * mass_x[None, :, None] * mass_y[None, None, :]
    for iteration in range(ITERS):
        modes = transform(
            "zxy,xi->ziy",
            lax.all_to_all(scaled, "gy", split_axis=0, concat_axis=1, tiled=True),
            basis_x,
        )
        chunks = modes.reshape(-1, local_modes, modes.shape[2])
        chunks = lax.all_to_all(chunks, everyone, split_axis=0, concat_axis=0, tiled=True)
        chunks = chunks.reshape(blocks_y, -1, local_modes, chunks.shape[2])
        modes = transform("azil,alj->zij", chunks, basis_y)
        solved = vertical_solve(modes, vertical_diag, vertical_coupling, shifts)
        chunks = transform("zij,alj->azil", solved, basis_y)
        chunks = chunks.reshape(-1, local_modes, chunks.shape[3])
        chunks = lax.all_to_all(chunks, everyone, split_axis=0, concat_axis=0, tiled=True)
        solved = chunks.reshape(-1, chunks.shape[2])
        plane = transform("iy,xi->xy", solved, basis_x)
        blocks = plane.reshape(-1, rows, plane.shape[1])
        from_left = lax.ppermute(blocks[:, :, -1], "gx", forward_y)
        from_right = lax.ppermute(blocks[:, :, 0], "gx", backward_y)
        zero = jnp.zeros_like(blocks[:1, :1])
        below = jnp.concatenate([zero, blocks[:-1, -1:]], axis=0)
        above = jnp.concatenate([blocks[1:, :1], zero], axis=0)
        halo_row = jnp.concatenate([from_left, from_right], axis=1)[:, None, :]
        framed = jnp.concatenate([below, blocks, above, halo_row], axis=1)
        framed = lax.all_to_all(framed, "gy", split_axis=0, concat_axis=0, tiled=True)
        y_strips = (active_y[0] * framed[:, -1, :rows], active_y[1] * framed[:, -1, rows:])
        if iteration + 1 < ITERS:
            residual, adjoint, scaled = framed_stencil(
                framed, active, residual, adjoint, active_x, y_strips, [faces[0], *faces[2:]], masses
            )
        else:
            residual, adjoint = framed_stencil(framed, active, residual, adjoint, active_x, y_strips, [faces[0], *faces[2:]])
    return (adjoint, residual)


def solution(mesh):
    in_specs = (
        P(None, "gy", "gx"),
        P(None, "gy", "gx"),
        P(None, "gy", "gx"),
        P(),
        P("gy"),
        P(),
        P(),
        P("gx"),
        P(),
        P(),
        P(),
    )
    out_specs = (P(None, "gy", "gx"), P(None, "gy", "gx"))
    return jax.shard_map(shards, mesh=mesh, in_specs=in_specs, out_specs=out_specs, check_vma=False)
```

```python
import functools

import jax
import jax.numpy as jnp
from jax import lax
from jax.experimental import pallas as pl
from jax.experimental.pallas import tpu as pltpu
from jax.sharding import PartitionSpec as P

ITERS = 2


storage_term = 0.2


def edge_pair(block, axis, dim):
    count = lax.axis_size(axis)
    forward = [(i, i + 1) for i in range(count - 1)]
    backward = [(target, source) for source, target in forward]
    last = lax.index_in_dim(block, block.shape[dim] - 1, axis=dim, keepdims=False)
    first = lax.index_in_dim(block, 0, axis=dim, keepdims=False)
    return lax.ppermute(last, axis, forward), lax.ppermute(first, axis, backward)


def edges(block):
    return [edge_pair(block, "gy", block.ndim - 2), edge_pair(block, "gx", block.ndim - 1)]


def harmonic(first, second):
    return 2.0 * first * second / (first + second)


def neighbours(center, strips):
    (x_low, x_high), (y_low, y_high) = strips
    zeros = jnp.zeros_like(center[:1])
    return [
        jnp.concatenate([center[1:], zeros], axis=0),
        jnp.concatenate([zeros, center[:-1]], axis=0),
        jnp.concatenate([center[:, 1:], x_high[:, None, :]], axis=1),
        jnp.concatenate([x_low[:, None, :], center[:, :-1]], axis=1),
        jnp.concatenate([center[:, :, 1:], y_high[:, :, None]], axis=2),
        jnp.concatenate([y_low[:, :, None], center[:, :, :-1]], axis=2),
    ]


def faces_from(center, strips):
    return [harmonic(center, other) for other in neighbours(center, strips)]


def framed_kernel(has_adjoint, has_scale, framed_ref, active_ref, residual_ref, *refs):
    refs = list(refs)
    adjoint_ref = refs.pop(0) if has_adjoint else None
    x_low_ref, x_high_ref, y_halo_ref, x_face_ref = refs[:4]
    refs = refs[4:]
    mass_x_ref, mass_y_ref = (refs.pop(0), refs.pop(0)) if has_scale else (None, None)
    scaled_out = refs.pop() if has_scale else None
    face_refs, residual_out, adjoint_out = refs[:-2], refs[-2], refs[-1]
    planes, rows, cols = active_ref.shape
    row = lax.broadcasted_iota(jnp.int32, (rows, cols), 0)
    col = lax.broadcasted_iota(jnp.int32, (rows, cols), 1)
    row_forward = pltpu.roll(row, 1, 0) == jnp.where(row == 0, rows - 1, row - 1)
    col_forward = pltpu.roll(col, 1, 1) == jnp.where(col == 0, cols - 1, col - 1)

    def before(plane, axis, count, forward):
        return jnp.where(forward, pltpu.roll(plane, 1, axis), pltpu.roll(plane, count - 1, axis))

    def after(plane, axis, count, forward):
        return jnp.where(forward, pltpu.roll(plane, count - 1, axis), pltpu.roll(plane, 1, axis))

    zeros = jnp.zeros((rows, cols), jnp.float32)
    updates = [framed_ref[z, pl.ds(1, rows), :] for z in range(planes)]
    masked = [active_ref[z] * updates[z] for z in range(planes)]
    for z in range(planes):
        center = masked[z]
        x_low = x_low_ref[pl.ds(z, 1), :] * framed_ref[z, pl.ds(0, 1), :]
        x_high = x_high_ref[pl.ds(z, 1), :] * framed_ref[z, pl.ds(rows + 1, 1), :]
        others = [
            masked[z + 1] if z + 1 < planes else zeros,
            masked[z - 1] if z > 0 else zeros,
            jnp.where(row == rows - 1, jnp.broadcast_to(x_high, (rows, cols)), after(center, 0, rows, row_forward)),
            jnp.where(row == 0, jnp.broadcast_to(x_low, (rows, cols)), before(center, 0, rows, row_forward)),
            jnp.where(col == cols - 1, y_halo_ref[z], after(center, 1, cols, col_forward)),
            jnp.where(col == 0, y_halo_ref[z], before(center, 1, cols, col_forward)),
        ]
        result = storage_term * center
        below = face_refs[0][z - 1] if z > 0 else zeros
        x_plus = face_refs[1][z]
        x_edge = jnp.broadcast_to(x_face_ref[pl.ds(z, 1), :], (rows, cols))
        x_minus = jnp.where(row == 0, x_edge, before(x_plus, 0, rows, row_forward))
        plane_faces = [face_refs[0][z], below, x_plus, x_minus] + [face_ref[z] for face_ref in face_refs[2:]]
        for face, other in zip(plane_faces, others):
            result = result + face * (center - other)
        update = updates[z]
        residual = residual_ref[z] - (result + (1.0 - active_ref[z]) * update)
        residual_out[z] = residual
        if has_scale:
            scaled_out[z] = residual * mass_x_ref[...] * mass_y_ref[...]
        adjoint_out[z] = update if adjoint_ref is None else adjoint_ref[z] + update


def framed_stencil(framed, active, residual, adjoint, x_strips, y_strips, faces, masses=None):
    vmem = pl.BlockSpec(memory_space=pltpu.VMEM)
    shape = jax.ShapeDtypeStruct(active.shape, active.dtype)
    lane = lax.broadcasted_iota(jnp.int32, active.shape, 2)
    y_halo = jnp.where(lane == 0, y_strips[0][:, :, None], y_strips[1][:, :, None])
    carried = [] if adjoint is None else [adjoint]
    scales = [] if masses is None else list(masses)
    operands = [framed, active, residual, *carried, x_strips[0], x_strips[1], y_halo, faces[3][:, 0, :], *scales, faces[0], faces[2], *faces[4:]]
    outputs = 2 if masses is None else 3
    return pl.pallas_call(
        functools.partial(framed_kernel, adjoint is not None, masses is not None),
        out_shape=(shape,) * outputs,
        in_specs=[vmem] * len(operands),
        out_specs=(vmem,) * outputs,
    )(*operands)


def solve_kernel(diag_ref, coup_ref, shifts_ref, rhs_ref, out_ref, ratio_ref):
    count = rhs_ref.shape[0]
    shifts = shifts_ref[...]
    denom = diag_ref[0] + shifts
    ratio = -coup_ref[0] / denom
    ratio_ref[0] = ratio
    part = rhs_ref[0] / denom
    out_ref[0] = part
    for position in range(1, count):
        denom = diag_ref[position] + shifts + coup_ref[position - 1] * ratio
        if position < count - 1:
            ratio = -coup_ref[position] / denom
            ratio_ref[position] = ratio
        part = (rhs_ref[position] + coup_ref[position - 1] * part) / denom
        out_ref[position] = part
    solved = part
    for position in range(count - 2, -1, -1):
        solved = out_ref[position] - ratio_ref[position] * solved
        out_ref[position] = solved


def vertical_solve(rhs, diagonal, coupling, shifts):
    smem = pl.BlockSpec(memory_space=pltpu.SMEM)
    vmem = pl.BlockSpec(memory_space=pltpu.VMEM)
    return pl.pallas_call(
        solve_kernel,
        out_shape=jax.ShapeDtypeStruct(rhs.shape, rhs.dtype),
        in_specs=[smem, smem, vmem, vmem],
        out_specs=vmem,
        scratch_shapes=[pltpu.VMEM(rhs.shape, rhs.dtype)],
    )(diagonal, coupling, shifts, rhs)


def split_bf16(values):
    rounded = lax.reduce_precision(values, exponent_bits=8, mantissa_bits=7)
    return rounded.astype(jnp.bfloat16), (values - rounded).astype(jnp.bfloat16)


def transform(spec, data, basis):
    high, low = split_bf16(data)
    basis_high, basis_low = basis

    def product(first, second):
        return jnp.einsum(spec, first, second, preferred_element_type=jnp.float32)

    return product(high, basis_high) + (product(low, basis_high) + product(high, basis_low))


def shards(
    right_side,
    conduct,
    excavated,
    vectors_x,
    mass_x,
    values_x,
    vectors_y,
    mass_y,
    values_y,
    vertical_diag,
    vertical_coupling,
):
    active = excavated.astype(jnp.float32)
    both = edges(jnp.stack([conduct, active]))
    faces = faces_from(conduct, [(low[0], high[0]) for low, high in both])
    active_x, active_y = [(low[1], high[1]) for low, high in both]
    local_modes = vectors_x.shape[1] // (lax.axis_size("gx") * lax.axis_size("gy"))
    mode_start = (lax.axis_index("gx") * lax.axis_size("gy") + lax.axis_index("gy")) * local_modes
    local_values = lax.dynamic_slice_in_dim(values_x, mode_start, local_modes, 0)
    shifts = local_values[:, None] + values_y[None, :]
    adjoint = None
    residual = right_side
    everyone = ("gx", "gy")
    blocks_y = lax.axis_size("gx")
    basis_x = split_bf16(vectors_x)
    rows = right_side.shape[1]
    count_y = lax.axis_size("gx")
    forward_y = [(i, i + 1) for i in range(count_y - 1)]
    backward_y = [(target, source) for source, target in forward_y]
    basis_y = tuple(piece.reshape(blocks_y, -1, vectors_y.shape[1]) for piece in split_bf16(vectors_y))
    rows_of, cols_of = right_side.shape[1], right_side.shape[2]
    masses = (mass_x.reshape(rows_of, 1), mass_y.reshape(1, cols_of))
    scaled = residual * mass_x[None, :, None] * mass_y[None, None, :]
    for iteration in range(ITERS):
        modes = transform(
            "zxy,xi->ziy",
            lax.all_to_all(scaled, "gy", split_axis=0, concat_axis=1, tiled=True),
            basis_x,
        )
        chunks = modes.reshape(-1, local_modes, modes.shape[2])
        chunks = lax.all_to_all(chunks, everyone, split_axis=0, concat_axis=0, tiled=True)
        chunks = chunks.reshape(blocks_y, -1, local_modes, chunks.shape[2])
        modes = transform("azil,alj->zij", chunks, basis_y)
        solved = vertical_solve(modes, vertical_diag, vertical_coupling, shifts)
        chunks = transform("zij,alj->azil", solved, basis_y)
        chunks = chunks.reshape(-1, local_modes, chunks.shape[3])
        chunks = lax.all_to_all(chunks, everyone, split_axis=0, concat_axis=0, tiled=True)
        solved = chunks.reshape(-1, chunks.shape[2])
        plane = transform("iy,xi->xy", solved, basis_x)
        blocks = plane.reshape(-1, rows, plane.shape[1])
        from_left = lax.ppermute(blocks[:, :, -1], "gx", forward_y)
        from_right = lax.ppermute(blocks[:, :, 0], "gx", backward_y)
        zero = jnp.zeros_like(blocks[:1, :1])
        below = jnp.concatenate([zero, blocks[:-1, -1:]], axis=0)
        above = jnp.concatenate([blocks[1:, :1], zero], axis=0)
        halo_row = jnp.concatenate([from_left, from_right], axis=1)[:, None, :]
        framed = jnp.concatenate([below, blocks, above, halo_row], axis=1)
        framed = lax.all_to_all(framed, "gy", split_axis=0, concat_axis=0, tiled=True)
        y_strips = (active_y[0] * framed[:, -1, :rows], active_y[1] * framed[:, -1, rows:])
        if iteration + 1 < ITERS:
            residual, adjoint, scaled = framed_stencil(
                framed, active, residual, adjoint, active_x, y_strips, faces, masses
            )
        else:
            residual, adjoint = framed_stencil(framed, active, residual, adjoint, active_x, y_strips, faces)
    return (adjoint, residual)


def solution(mesh):
    in_specs = (
        P(None, "gy", "gx"),
        P(None, "gy", "gx"),
        P(None, "gy", "gx"),
        P(),
        P("gy"),
        P(),
        P(),
        P("gx"),
        P(),
        P(),
        P(),
    )
    out_specs = (P(None, "gy", "gx"), P(None, "gy", "gx"))
    return jax.shard_map(shards, mesh=mesh, in_specs=in_specs, out_specs=out_specs, check_vma=False)
```
